32 devices in a mesh: groups: 2 (over y), space: 4 (over z), tm: 2 (over x), heads: 2 (over core).
Axes of the slice: x: 2, y: 2, z: 4, core: 2. Of those that a mesh axis runs over, the one named last changes fastest.
Arguments:
- latent: bfloat16 [12, 16, 52, 1536], P(('groups', 'tm'), 'space', None, 'heads'), parts along dimension 0, may hold values from -6 to 6
- query_weight: bfloat16 [1536, 1536], P(None, 'heads'), may hold values from -0.15625 to 0.15625
- key_weight: bfloat16 [1536, 1536], P(None, 'heads'), may hold values from -0.15625 to 0.15625
- value_weight: bfloat16 [1536, 1536], P(None, 'heads'), may hold values from -0.15625 to 0.15625
- output_weight: bfloat16 [1536, 1536], P('heads'), may hold values from -0.15625 to 0.15625
- query_gain: float32 [1536], P('heads'), may hold values from 0.6 to 7
- key_gain: float32 [1536], P('heads'), may hold values from 0.6 to 7
- modulation: float32 [16, 3, 1536], replicated, may hold values from -4 to 4
- noise_level: int32 [4], P(('groups', 'tm')), parts along dimension 0, may hold values from 0 to 15
- tile_pattern: int32 [4, 3, 6, 3], P('space'), may hold values from 0 to 1, as said below
Outputs:
- updated: bfloat16 [12, 16, 52, 1536], P(('groups', 'tm'), 'space', None, 'heads'), parts along dimension 0
The draws below stay inside these ranges and needn't reach their ends.
There are 2 independent parts, one for each index of `groups`. The reference program is written for one: setup_inputs(seed, part) draws one part's arguments, and reference() takes and returns one part's arrays. A program takes and returns all parts, laid end to end along the dimension named above; an argument that names none is the same for every part. Nothing has to cross between parts.
Inputs may be any that keep to these rules, and one draw needn't show every extreme that they name: tile_pattern[s, f, 3 + f, 1] is 1 for every strip s and frame f; entries that name a strip outside the grid are 0.
All inputs are finite; a program needn't handle non-finite values.
Results may differ from the reference program's by a relative error of at most 0.0045.
The reference program's roundings to bfloat16 on the way (of `hidden`, `values`, `weights` and `attended`) count: a program that leaves them out, or rounds other values in their place, can miss the bound.
Values may be sent and summed in bfloat16 or wider, within the bound.
No kernel may reach another device: no remote copies, remote signals or barrier semaphores. Data moves between devices by JAX's collectives and lax.ppermute only.
A program may use at most 128 MiB of HBM per device.

```python
import jax
import jax.numpy as jnp
from jax import lax

D = 1536
HEADS = 12
HD = 128
FRAMES = 3
COLS = 52
STRIP = 4
LEVELS = 16
ROWS = 16
NF = 6
N_SPACE = 4
N_TM = 2


def draw_query_gain(key, part):
    subkey = jax.random.fold_in(key, 11)
    return jax.random.uniform(subkey, (D,), jnp.float32, 0.6, 1.6)


def draw_key_gain(key, part):
    subkey = jax.random.fold_in(key, 12)
    return jax.random.uniform(subkey, (D,), jnp.float32, 0.6, 1.6)


def draw_tile_pattern(key, part):
    tiles = ROWS // STRIP
    subkey = jax.random.fold_in(key, 5)
    random_bits = jax.random.randint(subkey, (tiles, FRAMES, 2 * FRAMES, 3), 0, 2, dtype=jnp.int32)
    strip_ids = jnp.arange(tiles, dtype=jnp.int32)[:, None, None, None]
    frame_ids = jnp.arange(FRAMES, dtype=jnp.int32)[None, :, None, None]
    other_ids = jnp.arange(2 * FRAMES, dtype=jnp.int32)[None, None, :, None]
    offset_ids = jnp.arange(3, dtype=jnp.int32)[None, None, None, :]
    own_tile = (other_ids == frame_ids + FRAMES) & (offset_ids == 1)
    outside = (strip_ids == 0) & (offset_ids == 0) | (strip_ids == tiles - 1) & (offset_ids == 2)
    return jnp.where(own_tile, 1, jnp.where(outside, 0, random_bits)).astype(jnp.int32)


def block_scale(key, dims, cuts, smallest, top_value):
    def one(axis_at, shards_of):
        draws = jax.random.uniform(jax.random.fold_in(jax.random.fold_in(key, 6), axis_at), (shards_of,), jnp.float32, smallest / len(cuts), top_value / len(cuts))
        return jnp.repeat(jnp.exp(draws), dims[axis_at] // shards_of).reshape((-1,) + (1,) * (len(dims) - axis_at - 1))

    factor_of = one(*cuts[0])
    for cut in cuts[1:]:
        factor_of = factor_of * one(*cut)
    return factor_of


def normal_values(rng, extent, spread, reach, cuts=(), kind=jnp.bfloat16):
    level = block_scale(rng, extent, cuts, -0.22, 0.18) if cuts else 1.0
    entries = jax.random.normal(rng, extent, jnp.float32) * spread * level
    return jnp.minimum(jnp.maximum(entries, -reach), reach).astype(kind)


def setup_inputs(seed: int = 0, part: int = 0) -> dict:
    arg_keys = jax.random.split(jax.random.key(seed), 11)
    part_keys = jax.random.split(jax.random.fold_in(arg_keys[10], part), 11)
    latent = normal_values(part_keys[0], (NF, ROWS, COLS, D), 1.0, 6.0, ((0, 2), (1, 4), (3, 2)))
    query_weight = normal_values(arg_keys[1], (D, D), D ** -0.5, 0.15625, ((1, 2),))
    key_weight = normal_values(arg_keys[2], (D, D), D ** -0.5, 0.15625, ((1, 2),))
    value_weight = normal_values(arg_keys[3], (D, D), D ** -0.5, 0.15625, ((1, 2),))
    output_weight = normal_values(arg_keys[4], (D, D), D ** -0.5, 0.15625, ((0, 2),))
    query_gain = draw_query_gain(jax.random.fold_in(arg_keys[10], 71), part)
    key_gain = draw_key_gain(jax.random.fold_in(arg_keys[10], 71), part)
    modulation = normal_values(arg_keys[7], (LEVELS, 3, D), 0.7, 4.0, (), jnp.float32)
    noise_level = jax.random.randint(part_keys[8], (N_TM,), 0, LEVELS).astype(jnp.int32)
    tile_pattern = draw_tile_pattern(jax.random.fold_in(arg_keys[10], 71), part)
    return dict(latent=latent, query_weight=query_weight, key_weight=key_weight, value_weight=value_weight, output_weight=output_weight, query_gain=query_gain, key_gain=key_gain, modulation=modulation, noise_level=noise_level, tile_pattern=tile_pattern)


def arrange_tiles(values):
    shaped = values.reshape(N_TM, FRAMES, N_SPACE, STRIP * COLS, D)
    return jnp.transpose(shaped, (0, 2, 1, 3, 4))

def unit_norm(raw, gain):
    return (raw * lax.rsqrt(lax.optimization_barrier(jnp.mean(raw * raw, axis=1, keepdims=True)) + 1e-06) * gain).astype(jnp.bfloat16)

def reference(latent, query_weight, key_weight, value_weight, output_weight, query_gain, key_gain, modulation, noise_level, tile_pattern):
    tile_size = STRIP * COLS
    onehot = (noise_level[:, None] == jnp.arange(LEVELS, dtype=jnp.int32)[None, :]).astype(jnp.float32)
    mod_table = jnp.dot(onehot, modulation.reshape(LEVELS, 3 * D), precision=lax.Precision.HIGHEST).reshape(N_TM, 3, D)
    token_rows = latent.astype(jnp.float32).reshape(N_TM, FRAMES * ROWS * COLS, D)
    center = token_rows - lax.optimization_barrier(jnp.mean(token_rows, axis=2, keepdims=True))
    normed = center * lax.rsqrt(lax.optimization_barrier(jnp.mean(center * center, axis=2, keepdims=True)) + 1e-06)
    hidden = (normed * (1.0 + mod_table[:, 1][:, None, :]) + mod_table[:, 0][:, None, :]).astype(jnp.bfloat16).reshape(-1, D)
    queries = unit_norm(jnp.dot(hidden, query_weight, preferred_element_type=jnp.float32), query_gain)
    key_rows = unit_norm(jnp.dot(hidden, key_weight, preferred_element_type=jnp.float32), key_gain)
    value_rows = jnp.dot(hidden, value_weight, preferred_element_type=jnp.float32).astype(jnp.bfloat16)
    query_tiles = arrange_tiles(queries)
    key_padded = jnp.pad(arrange_tiles(key_rows), ((1, 0), (1, 1), (0, 0), (0, 0), (0, 0)))
    value_padded = jnp.pad(arrange_tiles(value_rows), ((1, 0), (1, 1), (0, 0), (0, 0), (0, 0)))
    score_scale = 1.0 / HD ** 0.5

    def attend(block_index):
        span_index = (block_index // N_SPACE).astype(jnp.int32)
        strip_index = (block_index % N_SPACE).astype(jnp.int32)
        anchor = jnp.zeros((), jnp.int32)
        block_keys = lax.dynamic_slice(key_padded, (span_index, strip_index, anchor, anchor, anchor), (2, 3, FRAMES, tile_size, D))
        block_values = lax.dynamic_slice(value_padded, (span_index, strip_index, anchor, anchor, anchor), (2, 3, FRAMES, tile_size, D))
        query_block = lax.dynamic_slice(query_tiles, (span_index, strip_index, anchor, anchor, anchor), (1, 1, FRAMES, tile_size, D))
        pattern = lax.dynamic_index_in_dim(tile_pattern, strip_index, 0, keepdims=False)
        pattern = jnp.transpose(pattern.reshape(FRAMES, 2, FRAMES, 3), (0, 1, 3, 2))
        source_valid = jnp.stack([span_index > 0, jnp.array(True)])
        offset_valid = jnp.stack([strip_index > 0, jnp.array(True), strip_index < N_SPACE - 1])
        visible = (pattern > 0) & source_valid[None, :, None, None] & offset_valid[None, None, :, None]
        visible = visible.reshape(FRAMES, 6 * FRAMES)
        query_float = query_block.astype(jnp.float32).reshape(FRAMES * tile_size, HEADS, HD)
        key_float = block_keys.astype(jnp.float32).reshape(6 * FRAMES * tile_size, HEADS, HD)
        value_float = block_values.astype(jnp.float32).reshape(6 * FRAMES * tile_size, HEADS, HD)
        scores = jnp.einsum('qhd,khd->hqk', query_float, key_float, precision=lax.Precision.HIGHEST) * score_scale
        scores = scores.reshape(HEADS, FRAMES, tile_size, 6 * FRAMES, tile_size)
        scores = jnp.where(visible[None, :, None, :, None], scores, -1e+30)
        maximum = lax.optimization_barrier(jnp.max(scores, axis=(3, 4), keepdims=True))
        exponent = jnp.exp(scores - maximum)
        totals = lax.optimization_barrier(jnp.sum(exponent, axis=(3, 4), keepdims=True))
        weights = (exponent / totals).astype(jnp.bfloat16).reshape(HEADS, FRAMES * tile_size, 6 * FRAMES * tile_size)
        result = jnp.einsum('hqk,khd->qhd', weights.astype(jnp.float32), value_float, precision=lax.Precision.HIGHEST)
        return result.reshape(FRAMES * tile_size, D).astype(jnp.bfloat16)
    results = lax.map(attend, jnp.arange(N_TM * N_SPACE, dtype=jnp.int32))
    attended = jnp.transpose(results.reshape(N_TM, N_SPACE, FRAMES, tile_size, D), (0, 2, 1, 3, 4)).reshape(-1, D)
    projected = jnp.dot(attended, output_weight, preferred_element_type=jnp.float32).reshape(N_TM, FRAMES * ROWS * COLS, D)
    updated = (token_rows + mod_table[:, 2][:, None, :] * projected).astype(jnp.bfloat16)
    return updated.reshape(NF, ROWS, COLS, D)
```

```python
import functools
import math

import jax
import jax.numpy as jnp
from jax import lax
from jax.experimental import pallas as pl
from jax.experimental.pallas import tpu as pltpu
from jax.sharding import PartitionSpec as P

HD = 128


EPSILON = 1e-06


def from_behind(value, axis, steps):
    count = lax.axis_size(axis)
    first, last = (max(0, -steps), min(count, count - steps))
    return lax.ppermute(value, axis, [(source, source + steps) for source in range(first, last)])


def from_diagonal(value, steps):
    n_tm = lax.axis_size("tm")
    n_space = lax.axis_size("space")
    pairs = []
    for t in range(n_tm - 1):
        for s in range(n_space):
            if 0 <= s + steps < n_space:
                pairs.append((s * n_tm + t, (s + steps) * n_tm + t + 1))
    return lax.ppermute(value, ("space", "tm"), pairs)


def attention_kernel(score_scale, n_tiles, vis_ref, q_ref, *refs):
    kv_refs = refs[:-5]
    o_ref = refs[-5]
    s_scr, m_scr, l_scr, acc_scr = refs[-4:]
    frame = pl.program_id(1)
    frames = kv_refs[0].shape[1]
    q = q_ref[...]
    tiles = [(source, g) for source in range(len(kv_refs)) for g in range(frames)]
    m_scr[...] = jnp.full(m_scr.shape, -jnp.inf, jnp.float32)
    for t, (source, g) in enumerate(tiles):

        @pl.when(vis_ref[frame, t] > 0)
        def _():
            k = kv_refs[source][0, g]
            s = (
                lax.dot_general(
                    q, k, (((1,), (1,)), ((), ())), preferred_element_type=jnp.float32
                )
                * score_scale
            )
            s_scr[t] = s
            m_scr[...] = jnp.maximum(m_scr[...], s)

    m = jnp.max(m_scr[...], axis=1, keepdims=True)
    l_scr[...] = jnp.zeros(l_scr.shape, jnp.float32)
    for t, (source, g) in enumerate(tiles):

        @pl.when(vis_ref[frame, t] > 0)
        def _():
            e = jnp.exp(s_scr[t] - m)
            s_scr[t] = e
            l_scr[...] += e

    total = jnp.sum(l_scr[...], axis=1, keepdims=True)
    acc_scr[...] = jnp.zeros(acc_scr.shape, jnp.float32)
    for t, (source, g) in enumerate(tiles):

        @pl.when(vis_ref[frame, t] > 0)
        def _():
            w = (s_scr[t] / total).astype(jnp.bfloat16)
            acc_scr[...] += jnp.dot(w, kv_refs[source][1, g], preferred_element_type=jnp.float32)

    o_ref[...] = acc_scr[...].astype(o_ref.dtype)


def attention(visible, queries, kv_list, frames, tile_size):
    local_width = queries.shape[1]
    heads = local_width // HD
    n_tiles = len(kv_list) * frames
    kernel = functools.partial(attention_kernel, 1.0 / math.sqrt(HD), n_tiles)
    kv_spec = pl.BlockSpec((2, frames, tile_size, HD), lambda h, f, vis: (0, 0, 0, h))
    grid_spec = pltpu.PrefetchScalarGridSpec(
        num_scalar_prefetch=1,
        grid=(heads, frames),
        in_specs=[pl.BlockSpec((tile_size, HD), lambda h, f, vis: (f, h))]
        + [kv_spec] * len(kv_list),
        out_specs=pl.BlockSpec((tile_size, HD), lambda h, f, vis: (f, h)),
        scratch_shapes=[
            pltpu.VMEM((n_tiles, tile_size, tile_size), jnp.float32),
            pltpu.VMEM((tile_size, tile_size), jnp.float32),
            pltpu.VMEM((tile_size, tile_size), jnp.float32),
            pltpu.VMEM((tile_size, HD), jnp.float32),
        ],
    )
    return pl.pallas_call(
        kernel,
        grid_spec=grid_spec,
        out_shape=jax.ShapeDtypeStruct(queries.shape, jnp.bfloat16),
    )(visible, queries, *kv_list)


def shards(
    latent,
    query_weight,
    key_weight,
    value_weight,
    output_weight,
    query_gain,
    key_gain,
    modulation,
    noise_level,
    tile_pattern,
):
    frames, strip_rows, columns, local_width = latent.shape
    width = local_width * lax.axis_size("heads")
    token_count = frames * strip_rows * columns
    tile_size = strip_rows * columns
    levels = modulation.shape[0]
    whole = lax.all_gather(latent, "heads", axis=3, tiled=True)
    onehot = (noise_level[0] == jnp.arange(levels, dtype=jnp.int32)).astype(jnp.float32)
    mod_table = jnp.dot(
        onehot[None, :], modulation.reshape(levels, 3 * width), precision=lax.Precision.HIGHEST
    ).reshape(3, width)
    token_rows = whole.reshape(token_count, width).astype(jnp.float32)
    center = token_rows - jnp.mean(token_rows, axis=1, keepdims=True)
    normed = center * lax.rsqrt(jnp.mean(center * center, axis=1, keepdims=True) + EPSILON)
    hidden = (normed * (1.0 + mod_table[1]) + mod_table[0]).astype(jnp.bfloat16)
    query_raw = jnp.dot(hidden, query_weight, preferred_element_type=jnp.float32)
    key_raw = jnp.dot(hidden, key_weight, preferred_element_type=jnp.float32)
    value_rows = jnp.dot(hidden, value_weight, preferred_element_type=jnp.float32).astype(
        jnp.bfloat16
    )
    squares = lax.psum(
        (jnp.sum(query_raw * query_raw, axis=1), jnp.sum(key_raw * key_raw, axis=1)), "heads"
    )
    queries = (query_raw * lax.rsqrt(squares[0] / width + EPSILON)[:, None] * query_gain).astype(
        jnp.bfloat16
    )
    key_rows = (key_raw * lax.rsqrt(squares[1] / width + EPSILON)[:, None] * key_gain).astype(
        jnp.bfloat16
    )
    kv = jnp.stack(
        [
            key_rows.reshape(frames, tile_size, local_width),
            value_rows.reshape(frames, tile_size, local_width),
        ]
    )
    own_low = from_behind(kv, "space", 1)
    own_high = from_behind(kv, "space", -1)
    prior_mid = from_behind(kv, "tm", 1)
    prior_low = from_diagonal(kv, 1)
    prior_high = from_diagonal(kv, -1)
    kv_list = [prior_low, prior_mid, prior_high, own_low, kv, own_high]
    pattern = jnp.transpose(tile_pattern[0].reshape(frames, 2, frames, 3), (0, 1, 3, 2))
    span_index = lax.axis_index("tm")
    strip_index = lax.axis_index("space")
    source_valid = jnp.stack([span_index > 0, jnp.array(True)])
    offset_valid = jnp.stack(
        [strip_index > 0, jnp.array(True), strip_index < lax.axis_size("space") - 1]
    )
    visible = (pattern > 0) & source_valid[None, :, None, None] & offset_valid[None, None, :, None]
    visible = visible.reshape(frames, 6 * frames).astype(jnp.int32)
    attended = attention(visible, queries, kv_list, frames, tile_size)
    column_start = lax.axis_index("heads") * local_width
    projected = jnp.transpose(
        lax.psum_scatter(
            lax.dot_general(
                output_weight,
                attended,
                (((0,), (1,)), ((), ())),
                preferred_element_type=jnp.float32,
            ),
            "heads",
            scatter_dimension=0,
            tiled=True,
        )
    )
    gate_half = lax.dynamic_slice_in_dim(mod_table[2], column_start, local_width)
    own_rows = latent.reshape(token_count, local_width).astype(jnp.float32)
    updated = (own_rows + gate_half * projected).astype(jnp.bfloat16)
    return updated.reshape(latent.shape)


def solution(mesh):
    placed = (
        P(("groups", "tm"), "space", None, "heads"),
        P(None, "heads"),
        P(None, "heads"),
        P(None, "heads"),
        P("heads", None),
        P("heads"),
        P("heads"),
        P(),
        P(("groups", "tm")),
        P("space", None, None, None),
    )
    return jax.shard_map(
        shards,
        mesh=mesh,
        in_specs=placed,
        out_specs=P(("groups", "tm"), "space", None, "heads"),
        check_vma=False,
    )
```

```python
import functools
import math

import jax
import jax.numpy as jnp
from jax import lax
from jax.experimental import pallas as pl
from jax.experimental.pallas import tpu as pltpu
from jax.sharding import PartitionSpec as P

HD = 128


EPSILON = 1e-06


def from_behind(value, axis, steps):
    count = lax.axis_size(axis)
    first, last = (max(0, -steps), min(count, count - steps))
    return lax.ppermute(value, axis, [(source, source + steps) for source in range(first, last)])


def from_diagonal(value, steps):
    n_tm = lax.axis_size("tm")
    n_space = lax.axis_size("space")
    pairs = []
    for t in range(n_tm - 1):
        for s in range(n_space):
            if 0 <= s + steps < n_space:
                pairs.append((s * n_tm + t, (s + steps) * n_tm + t + 1))
    return lax.ppermute(value, ("space", "tm"), pairs)


def gather_heads(latent):
    if lax.axis_size("heads") != 2:
        return lax.all_gather(latent, "heads", axis=3, tiled=True)
    me = lax.axis_index("heads")
    other = lax.ppermute(latent, "heads", [(0, 1), (1, 0)])
    first = jnp.where(me == 0, latent, other)
    second = jnp.where(me == 0, other, latent)
    return jnp.concatenate([first, second], axis=3)


def sum_heads(partial, local_width):
    if lax.axis_size("heads") != 2:
        return lax.psum_scatter(partial, "heads", scatter_dimension=1, tiled=True)
    me = lax.axis_index("heads")
    mine = lax.dynamic_slice_in_dim(partial, me * local_width, local_width, 1)
    theirs = lax.dynamic_slice_in_dim(partial, (1 - me) * local_width, local_width, 1)
    return mine + lax.ppermute(theirs, "heads", [(0, 1), (1, 0)])


def attention_kernel(score_scale, n_tiles, vis_ref, q_ref, *refs):
    kv_refs = refs[:-5]
    o_ref = refs[-5]
    s_scr, m_scr, l_scr, acc_scr = refs[-4:]
    frame = pl.program_id(1)
    frames = kv_refs[0].shape[1]
    q = q_ref[...]
    tiles = [(source, g) for source in range(len(kv_refs)) for g in range(frames)]
    m_scr[...] = jnp.full(m_scr.shape, -jnp.inf, jnp.float32)
    for t, (source, g) in enumerate(tiles):

        @pl.when(vis_ref[frame, t] > 0)
        def _():
            k = kv_refs[source][0, g]
            s = (
                lax.dot_general(
                    q, k, (((1,), (1,)), ((), ())), preferred_element_type=jnp.float32
                )
                * score_scale
            )
            s_scr[t] = s
            m_scr[...] = jnp.maximum(m_scr[...], s)

    m = jnp.max(m_scr[...], axis=1, keepdims=True)
    l_scr[...] = jnp.zeros(l_scr.shape, jnp.float32)
    for t, (source, g) in enumerate(tiles):

        @pl.when(vis_ref[frame, t] > 0)
        def _():
            e = jnp.exp(s_scr[t] - m)
            s_scr[t] = e
            l_scr[...] += e

    total = jnp.sum(l_scr[...], axis=1, keepdims=True)
    acc_scr[...] = jnp.zeros(acc_scr.shape, jnp.float32)
    for t, (source, g) in enumerate(tiles):

        @pl.when(vis_ref[frame, t] > 0)
        def _():
            w = (s_scr[t] / total).astype(jnp.bfloat16)
            acc_scr[...] += jnp.dot(w, kv_refs[source][1, g], preferred_element_type=jnp.float32)

    o_ref[...] = acc_scr[...].astype(o_ref.dtype)


def attention(visible, queries, kv_list, frames, tile_size):
    local_width = queries.shape[1]
    heads = local_width // HD
    n_tiles = len(kv_list) * frames
    kernel = functools.partial(attention_kernel, 1.0 / math.sqrt(HD), n_tiles)
    kv_spec = pl.BlockSpec((2, frames, tile_size, HD), lambda h, f, vis: (0, 0, 0, h))
    grid_spec = pltpu.PrefetchScalarGridSpec(
        num_scalar_prefetch=1,
        grid=(heads, frames),
        in_specs=[pl.BlockSpec((tile_size, HD), lambda h, f, vis: (f, h))]
        + [kv_spec] * len(kv_list),
        out_specs=pl.BlockSpec((tile_size, HD), lambda h, f, vis: (f, h)),
        scratch_shapes=[
            pltpu.VMEM((n_tiles, tile_size, tile_size), jnp.float32),
            pltpu.VMEM((tile_size, tile_size), jnp.float32),
            pltpu.VMEM((tile_size, tile_size), jnp.float32),
            pltpu.VMEM((tile_size, HD), jnp.float32),
        ],
    )
    return pl.pallas_call(
        kernel,
        grid_spec=grid_spec,
        out_shape=jax.ShapeDtypeStruct(queries.shape, jnp.bfloat16),
    )(visible, queries, *kv_list)


def shards(
    latent,
    query_weight,
    key_weight,
    value_weight,
    output_weight,
    query_gain,
    key_gain,
    modulation,
    noise_level,
    tile_pattern,
):
    frames, strip_rows, columns, local_width = latent.shape
    width = local_width * lax.axis_size("heads")
    token_count = frames * strip_rows * columns
    tile_size = strip_rows * columns
    levels = modulation.shape[0]
    whole = gather_heads(latent)
    onehot = (noise_level[0] == jnp.arange(levels, dtype=jnp.int32)).astype(jnp.float32)
    mod_table = jnp.dot(
        onehot[None, :], modulation.reshape(levels, 3 * width), precision=lax.Precision.HIGHEST
    ).reshape(3, width)
    token_rows = whole.reshape(token_count, width).astype(jnp.float32)
    center = token_rows - jnp.mean(token_rows, axis=1, keepdims=True)
    normed = center * lax.rsqrt(jnp.mean(center * center, axis=1, keepdims=True) + EPSILON)
    hidden = (normed * (1.0 + mod_table[1]) + mod_table[0]).astype(jnp.bfloat16)
    query_raw = jnp.dot(hidden, query_weight, preferred_element_type=jnp.float32)
    key_raw = jnp.dot(hidden, key_weight, preferred_element_type=jnp.float32)
    value_rows = jnp.dot(hidden, value_weight, preferred_element_type=jnp.float32).astype(
        jnp.bfloat16
    )
    squares = lax.psum(
        (jnp.sum(query_raw * query_raw, axis=1), jnp.sum(key_raw * key_raw, axis=1)), "heads"
    )
    queries = (query_raw * lax.rsqrt(squares[0] / width + EPSILON)[:, None] * query_gain).astype(
        jnp.bfloat16
    )
    key_rows = (key_raw * lax.rsqrt(squares[1] / width + EPSILON)[:, None] * key_gain).astype(
        jnp.bfloat16
    )
    kv = jnp.stack(
        [
            key_rows.reshape(frames, tile_size, local_width),
            value_rows.reshape(frames, tile_size, local_width),
        ]
    )
    own_low = from_behind(kv, "space", 1)
    own_high = from_behind(kv, "space", -1)
    prior_mid = from_behind(kv, "tm", 1)
    prior_low = from_behind(prior_mid, "space", 1)
    prior_high = from_behind(prior_mid, "space", -1)
    kv_list = [prior_low, prior_mid, prior_high, own_low, kv, own_high]
    pattern = jnp.transpose(tile_pattern[0].reshape(frames, 2, frames, 3), (0, 1, 3, 2))
    span_index = lax.axis_index("tm")
    strip_index = lax.axis_index("space")
    source_valid = jnp.stack([span_index > 0, jnp.array(True)])
    offset_valid = jnp.stack(
        [strip_index > 0, jnp.array(True), strip_index < lax.axis_size("space") - 1]
    )
    visible = (pattern > 0) & source_valid[None, :, None, None] & offset_valid[None, None, :, None]
    visible = visible.reshape(frames, 6 * frames).astype(jnp.int32)
    attended = attention(visible, queries, kv_list, frames, tile_size)
    column_start = lax.axis_index("heads") * local_width
    partial = jnp.dot(attended, output_weight, preferred_element_type=jnp.float32)
    projected = sum_heads(partial, local_width)
    gate_half = lax.dynamic_slice_in_dim(mod_table[2], column_start, local_width)
    own_rows = latent.reshape(token_count, local_width).astype(jnp.float32)
    updated = (own_rows + gate_half * projected).astype(jnp.bfloat16)
    return updated.reshape(latent.shape)


def solution(mesh):
    placed = (
        P(("groups", "tm"), "space", None, "heads"),
        P(None, "heads"),
        P(None, "heads"),
        P(None, "heads"),
        P("heads", None),
        P("heads"),
        P("heads"),
        P(),
        P(("groups", "tm")),
        P("space", None, None, None),
    )
    return jax.shard_map(
        shards,
        mesh=mesh,
        in_specs=placed,
        out_specs=P(("groups", "tm"), "space", None, "heads"),
        check_vma=False,
    )
```

```python
import functools
import math

import jax
import jax.numpy as jnp
from jax import lax
from jax.experimental import pallas as pl
from jax.experimental.pallas import tpu as pltpu
from jax.sharding import PartitionSpec as P

HD = 128


EPSILON = 1e-06


def from_behind(value, axis, steps):
    count = lax.axis_size(axis)
    first, last = (max(0, -steps), min(count, count - steps))
    return lax.ppermute(value, axis, [(source, source + steps) for source in range(first, last)])


def gather_heads(half):
    if lax.axis_size("heads") != 2:
        return lax.all_gather(half, "heads", axis=half.ndim - 1, tiled=True)
    me = lax.axis_index("heads")
    other = lax.ppermute(half, "heads", [(0, 1), (1, 0)])
    first = jnp.where(me == 0, half, other)
    second = jnp.where(me == 0, other, half)
    return jnp.concatenate([first, second], axis=-1)


def sum_heads(partial, local_width):
    if lax.axis_size("heads") != 2:
        return lax.psum_scatter(partial, "heads", scatter_dimension=1, tiled=True)
    me = lax.axis_index("heads")
    mine = lax.dynamic_slice_in_dim(partial, me * local_width, local_width, 1)
    theirs = lax.dynamic_slice_in_dim(partial, (1 - me) * local_width, local_width, 1)
    return mine + lax.ppermute(theirs, "heads", [(0, 1), (1, 0)])


def norm_kernel(x_ref, mod_ref, o_ref):
    x = x_ref[0].astype(jnp.float32)
    center = x - jnp.mean(x, axis=1, keepdims=True)
    normed = center * lax.rsqrt(jnp.mean(center * center, axis=1, keepdims=True) + EPSILON)
    o_ref[0] = (normed * (1.0 + mod_ref[0, 1:2, :]) + mod_ref[0, 0:1, :]).astype(o_ref.dtype)


def modulated_norm(tokens, mods, block_rows):
    sets, count, width = tokens.shape
    return pl.pallas_call(
        norm_kernel,
        grid=(sets, count // block_rows),
        in_specs=[
            pl.BlockSpec((1, block_rows, width), lambda i, j: (i, j, 0)),
            pl.BlockSpec((1, 3, width), lambda i, j: (i, 0, 0)),
        ],
        out_specs=pl.BlockSpec((1, block_rows, width), lambda i, j: (i, j, 0)),
        out_shape=jax.ShapeDtypeStruct(tokens.shape, jnp.bfloat16),
    )(tokens, mods)


def attention_kernel(score_scale, slots, vis_ref, q_ref, *refs):
    groups = len(slots)
    k_refs = refs[:groups]
    v_refs = refs[groups : 2 * groups]
    o_ref = refs[2 * groups]
    s_scr, m_scr, l_scr, acc_scr = refs[2 * groups + 1 :]
    frame = pl.program_id(1)
    frames = k_refs[0].shape[1]
    q = q_ref[...]
    tiles = []
    for g, group_slots in enumerate(slots):
        for j, slot in enumerate(group_slots):
            for fr in range(frames):
                tiles.append((g, j, fr, slot * frames + fr))
    m_scr[...] = jnp.full(m_scr.shape, -jnp.inf, jnp.float32)
    for n, (g, j, fr, t) in enumerate(tiles):

        @pl.when(vis_ref[frame, t] > 0)
        def _():
            s = (
                lax.dot_general(
                    q, k_refs[g][j, fr], (((1,), (1,)), ((), ())), preferred_element_type=jnp.float32
                )
                * score_scale
            )
            s_scr[n] = s
            m_scr[...] = jnp.maximum(m_scr[...], s)

    m = jnp.max(m_scr[...], axis=1, keepdims=True)
    l_scr[...] = jnp.zeros(l_scr.shape, jnp.float32)
    for n, (g, j, fr, t) in enumerate(tiles):

        @pl.when(vis_ref[frame, t] > 0)
        def _():
            e = jnp.exp(s_scr[n] - m)
            s_scr[n] = e
            l_scr[...] += e

    total = jnp.sum(l_scr[...], axis=1, keepdims=True)
    acc_scr[...] = jnp.zeros(acc_scr.shape, jnp.float32)
    for n, (g, j, fr, t) in enumerate(tiles):

        @pl.when(vis_ref[frame, t] > 0)
        def _():
            w = (s_scr[n] / total).astype(jnp.bfloat16)
            acc_scr[...] += jnp.dot(w, v_refs[g][j, fr], preferred_element_type=jnp.float32)

    o_ref[...] = acc_scr[...].astype(o_ref.dtype)


def attention(visible, queries, keys, values, slots, tile_size):
    local_width = queries.shape[1]
    heads = local_width // HD
    frames = keys[0].shape[1]
    n_tiles = sum(len(s) for s in slots) * frames
    kernel = functools.partial(attention_kernel, 1.0 / math.sqrt(HD), slots)
    kv_specs = [
        pl.BlockSpec((k.shape[0], frames, tile_size, HD), lambda h, f, vis: (0, 0, 0, h))
        for k in keys
    ]
    grid_spec = pltpu.PrefetchScalarGridSpec(
        num_scalar_prefetch=1,
        grid=(heads, frames),
        in_specs=[pl.BlockSpec((tile_size, HD), lambda h, f, vis: (f, h))] + kv_specs + kv_specs,
        out_specs=pl.BlockSpec((tile_size, HD), lambda h, f, vis: (f, h)),
        scratch_shapes=[
            pltpu.VMEM((n_tiles, tile_size, tile_size), jnp.float32),
            pltpu.VMEM((tile_size, tile_size), jnp.float32),
            pltpu.VMEM((tile_size, tile_size), jnp.float32),
            pltpu.VMEM((tile_size, HD), jnp.float32),
        ],
    )
    return pl.pallas_call(
        kernel,
        grid_spec=grid_spec,
        out_shape=jax.ShapeDtypeStruct(queries.shape, jnp.bfloat16),
    )(visible, queries, *keys, *values)


def unit_rows(raw, gain, width):
    squares = lax.psum(jnp.sum(raw * raw, axis=-1), "heads")
    return (raw * lax.rsqrt(squares / width + EPSILON)[..., None] * gain).astype(jnp.bfloat16)


def shards(
    latent,
    query_weight,
    key_weight,
    value_weight,
    output_weight,
    query_gain,
    key_gain,
    modulation,
    noise_level,
    tile_pattern,
):
    frames, strip_rows, columns, local_width = latent.shape
    width = local_width * lax.axis_size("heads")
    token_count = frames * strip_rows * columns
    tile_size = strip_rows * columns
    levels = modulation.shape[0]
    rows = latent.reshape(token_count, local_width)
    own_low = from_behind(rows, "space", 1)
    own_high = from_behind(rows, "space", -1)
    prior_mid = from_behind(rows, "tm", 1)
    prior_level = from_behind(noise_level, "tm", 1)
    prior_low = from_behind(prior_mid, "space", 1)
    prior_high = from_behind(prior_mid, "space", -1)

    def table(level):
        onehot = (level[0] == jnp.arange(levels, dtype=jnp.int32)).astype(jnp.float32)
        return jnp.dot(
            onehot[None, :], modulation.reshape(levels, 3 * width), precision=lax.Precision.HIGHEST
        ).reshape(3, width)

    mod_table = table(noise_level)
    prior_table = table(prior_level)

    def project(halves, mods):
        sets = len(halves)
        tokens = gather_heads(jnp.stack(halves))
        hidden = modulated_norm(tokens, jnp.stack(mods), tile_size)
        flat = hidden.reshape(sets * token_count, width)
        key_rows = unit_rows(
            jnp.dot(flat, key_weight, preferred_element_type=jnp.float32), key_gain, width
        )
        value_rows = jnp.dot(flat, value_weight, preferred_element_type=jnp.float32).astype(
            jnp.bfloat16
        )
        shape = (sets, frames, tile_size, local_width)
        return flat, key_rows.reshape(shape), value_rows.reshape(shape)

    own_flat, own_keys, own_values = project([rows], [mod_table])
    queries = unit_rows(
        jnp.dot(own_flat, query_weight, preferred_element_type=jnp.float32), query_gain, width
    )
    _, near_keys, near_values = project(
        [own_low, own_high, prior_mid], [mod_table, mod_table, prior_table]
    )
    _, far_keys, far_values = project([prior_low, prior_high], [prior_table, prior_table])
    slots = ((4,), (3, 5, 1), (0, 2))

    pattern = jnp.transpose(tile_pattern[0].reshape(frames, 2, frames, 3), (0, 1, 3, 2))
    span_index = lax.axis_index("tm")
    strip_index = lax.axis_index("space")
    source_valid = jnp.stack([span_index > 0, jnp.array(True)])
    offset_valid = jnp.stack(
        [strip_index > 0, jnp.array(True), strip_index < lax.axis_size("space") - 1]
    )
    visible = (pattern > 0) & source_valid[None, :, None, None] & offset_valid[None, None, :, None]
    visible = visible.reshape(frames, 6 * frames).astype(jnp.int32)
    attended = attention(
        visible,
        queries,
        [own_keys, near_keys, far_keys],
        [own_values, near_values, far_values],
        slots,
        tile_size,
    )
    column_start = lax.axis_index("heads") * local_width
    partial = jnp.dot(attended, output_weight, preferred_element_type=jnp.float32)
    projected = sum_heads(partial, local_width)
    gate_half = lax.dynamic_slice_in_dim(mod_table[2], column_start, local_width)
    updated = (rows.astype(jnp.float32) + gate_half * projected).astype(jnp.bfloat16)
    return updated.reshape(latent.shape)


def solution(mesh):
    placed = (
        P(("groups", "tm"), "space", None, "heads"),
        P(None, "heads"),
        P(None, "heads"),
        P(None, "heads"),
        P("heads", None),
        P("heads"),
        P("heads"),
        P(),
        P(("groups", "tm")),
        P("space", None, None, None),
    )
    return jax.shard_map(
        shards,
        mesh=mesh,
        in_specs=placed,
        out_specs=P(("groups", "tm"), "space", None, "heads"),
        check_vma=False,
    )
```

```python
import functools
import math

import jax
import jax.numpy as jnp
from jax import lax
from jax.experimental import pallas as pl
from jax.experimental.pallas import tpu as pltpu
from jax.sharding import PartitionSpec as P

HD = 128


EPSILON = 1e-06


def from_behind(value, axis, steps):
    count = lax.axis_size(axis)
    first, last = (max(0, -steps), min(count, count - steps))
    return lax.ppermute(value, axis, [(source, source + steps) for source in range(first, last)])


def gather_heads(half):
    if lax.axis_size("heads") != 2:
        return lax.all_gather(half, "heads", axis=half.ndim - 1, tiled=True)
    me = lax.axis_index("heads")
    other = lax.ppermute(half, "heads", [(0, 1), (1, 0)])
    first = jnp.where(me == 0, half, other)
    second = jnp.where(me == 0, other, half)
    return jnp.concatenate([first, second], axis=-1)


def sum_heads(partial, local_width):
    if lax.axis_size("heads") != 2:
        return lax.psum_scatter(partial, "heads", scatter_dimension=1, tiled=True)
    me = lax.axis_index("heads")
    mine = lax.dynamic_slice_in_dim(partial, me * local_width, local_width, 1)
    theirs = lax.dynamic_slice_in_dim(partial, (1 - me) * local_width, local_width, 1)
    return mine + lax.ppermute(theirs, "heads", [(0, 1), (1, 0)])


def attention_kernel(score_scale, tile_ids, vis_ref, q_ref, *refs):
    kv_refs = refs[:-5]
    o_ref = refs[-5]
    s_scr, m_scr, l_scr, acc_scr = refs[-4:]
    frame = pl.program_id(1)
    q = q_ref[...]
    tiles = [(source, g) for source, ids in enumerate(tile_ids) for g in range(len(ids))]
    slot_of = [ids[g] for ids in tile_ids for g in range(len(ids))]
    m_scr[...] = jnp.full(m_scr.shape, -jnp.inf, jnp.float32)
    for t, (source, g) in enumerate(tiles):

        @pl.when(vis_ref[frame, slot_of[t]] > 0)
        def _():
            k = kv_refs[source][0, g]
            s = (
                lax.dot_general(
                    q, k, (((1,), (1,)), ((), ())), preferred_element_type=jnp.float32
                )
                * score_scale
            )
            s_scr[t] = s
            m_scr[...] = jnp.maximum(m_scr[...], s)

    m = jnp.max(m_scr[...], axis=1, keepdims=True)
    l_scr[...] = jnp.zeros(l_scr.shape, jnp.float32)
    for t, (source, g) in enumerate(tiles):

        @pl.when(vis_ref[frame, slot_of[t]] > 0)
        def _():
            e = jnp.exp(s_scr[t] - m)
            s_scr[t] = e
            l_scr[...] += e

    total = jnp.sum(l_scr[...], axis=1, keepdims=True)
    acc_scr[...] = jnp.zeros(acc_scr.shape, jnp.float32)
    for t, (source, g) in enumerate(tiles):

        @pl.when(vis_ref[frame, slot_of[t]] > 0)
        def _():
            w = (s_scr[t] / total).astype(jnp.bfloat16)
            acc_scr[...] += jnp.dot(w, kv_refs[source][1, g], preferred_element_type=jnp.float32)

    o_ref[...] = acc_scr[...].astype(o_ref.dtype)


def attention(visible, queries, kv_list, frames, tile_size):
    local_width = queries.shape[1]
    heads = local_width // HD
    tile_ids = tuple(tuple(ids) for _, ids in kv_list)
    n_tiles = sum(len(ids) for ids in tile_ids)
    kernel = functools.partial(attention_kernel, 1.0 / math.sqrt(HD), tile_ids)
    kv_specs = [
        pl.BlockSpec((2, len(ids), tile_size, HD), lambda h, f, vis: (0, 0, 0, h))
        for _, ids in kv_list
    ]
    grid_spec = pltpu.PrefetchScalarGridSpec(
        num_scalar_prefetch=1,
        grid=(heads, frames),
        in_specs=[pl.BlockSpec((tile_size, HD), lambda h, f, vis: (f, h))]
        + kv_specs,
        out_specs=pl.BlockSpec((tile_size, HD), lambda h, f, vis: (f, h)),
        scratch_shapes=[
            pltpu.VMEM((n_tiles, tile_size, tile_size), jnp.float32),
            pltpu.VMEM((tile_size, tile_size), jnp.float32),
            pltpu.VMEM((tile_size, tile_size), jnp.float32),
            pltpu.VMEM((tile_size, HD), jnp.float32),
        ],
    )
    return pl.pallas_call(
        kernel,
        grid_spec=grid_spec,
        out_shape=jax.ShapeDtypeStruct(queries.shape, jnp.bfloat16),
    )(visible, queries, *[kv for kv, _ in kv_list])


def shards(
    latent,
    query_weight,
    key_weight,
    value_weight,
    output_weight,
    query_gain,
    key_gain,
    modulation,
    noise_level,
    tile_pattern,
):
    frames, strip_rows, columns, local_width = latent.shape
    width = local_width * lax.axis_size("heads")
    token_count = frames * strip_rows * columns
    tile_size = strip_rows * columns
    levels = modulation.shape[0]
    rows = latent.reshape(token_count, local_width)
    whole = gather_heads(rows)
    onehot = (noise_level[0] == jnp.arange(levels, dtype=jnp.int32)).astype(jnp.float32)
    mod_table = jnp.dot(
        onehot[None, :], modulation.reshape(levels, 3 * width), precision=lax.Precision.HIGHEST
    ).reshape(3, width)
    token_rows = whole.astype(jnp.float32)
    center = token_rows - jnp.mean(token_rows, axis=1, keepdims=True)
    normed = center * lax.rsqrt(jnp.mean(center * center, axis=1, keepdims=True) + EPSILON)
    hidden = (normed * (1.0 + mod_table[1]) + mod_table[0]).astype(jnp.bfloat16)
    query_raw = jnp.dot(hidden, query_weight, preferred_element_type=jnp.float32)
    key_raw = jnp.dot(hidden, key_weight, preferred_element_type=jnp.float32)
    value_rows = jnp.dot(hidden, value_weight, preferred_element_type=jnp.float32).astype(
        jnp.bfloat16
    )
    squares = lax.psum(
        (jnp.sum(query_raw * query_raw, axis=1), jnp.sum(key_raw * key_raw, axis=1)), "heads"
    )
    queries = (query_raw * lax.rsqrt(squares[0] / width + EPSILON)[:, None] * query_gain).astype(
        jnp.bfloat16
    )
    key_rows = (key_raw * lax.rsqrt(squares[1] / width + EPSILON)[:, None] * key_gain).astype(
        jnp.bfloat16
    )
    kv = jnp.stack(
        [
            key_rows.reshape(frames, tile_size, local_width),
            value_rows.reshape(frames, tile_size, local_width),
        ]
    )
    own_low = from_behind(kv, "space", 1)
    own_high = from_behind(kv, "space", -1)
    prior_mid = from_behind(kv, "tm", 1)
    split = frames - frames // 3
    low_far = from_behind(prior_mid[:, :split], "space", 1)
    high_far = from_behind(prior_mid[:, :split], "space", -1)
    low_near = from_behind(own_low[:, split:], "tm", 1)
    high_near = from_behind(own_high[:, split:], "tm", 1)
    fr = list(range(frames))
    kv_list = [
        (low_far, [0 * frames + f for f in fr[:split]]),
        (low_near, [0 * frames + f for f in fr[split:]]),
        (prior_mid, [1 * frames + f for f in fr]),
        (high_far, [2 * frames + f for f in fr[:split]]),
        (high_near, [2 * frames + f for f in fr[split:]]),
        (own_low, [3 * frames + f for f in fr]),
        (kv, [4 * frames + f for f in fr]),
        (own_high, [5 * frames + f for f in fr]),
    ]
    pattern = jnp.transpose(tile_pattern[0].reshape(frames, 2, frames, 3), (0, 1, 3, 2))
    span_index = lax.axis_index("tm")
    strip_index = lax.axis_index("space")
    source_valid = jnp.stack([span_index > 0, jnp.array(True)])
    offset_valid = jnp.stack(
        [strip_index > 0, jnp.array(True), strip_index < lax.axis_size("space") - 1]
    )
    visible = (pattern > 0) & source_valid[None, :, None, None] & offset_valid[None, None, :, None]
    visible = visible.reshape(frames, 6 * frames).astype(jnp.int32)
    attended = attention(visible, queries, kv_list, frames, tile_size)
    column_start = lax.axis_index("heads") * local_width
    partial = jnp.dot(attended, output_weight, preferred_element_type=jnp.float32)
    projected = sum_heads(partial, local_width)
    gate_half = lax.dynamic_slice_in_dim(mod_table[2], column_start, local_width)
    own_rows = rows.astype(jnp.float32)
    updated = (own_rows + gate_half * projected).astype(jnp.bfloat16)
    return updated.reshape(latent.shape)


def solution(mesh):
    placed = (
        P(("groups", "tm"), "space", None, "heads"),
        P(None, "heads"),
        P(None, "heads"),
        P(None, "heads"),
        P("heads", None),
        P("heads"),
        P("heads"),
        P(),
        P(("groups", "tm")),
        P("space", None, None, None),
    )
    return jax.shard_map(
        shards,
        mesh=mesh,
        in_specs=placed,
        out_specs=P(("groups", "tm"), "space", None, "heads"),
        check_vma=False,
    )
```

```python
import functools
import math

import jax
import jax.numpy as jnp
from jax import lax
from jax.experimental import pallas as pl
from jax.experimental.pallas import tpu as pltpu
from jax.sharding import PartitionSpec as P

HD = 128


EPSILON = 1e-06


def from_behind(value, axis, steps):
    count = lax.axis_size(axis)
    first, last = (max(0, -steps), min(count, count - steps))
    return lax.ppermute(value, axis, [(source, source + steps) for source in range(first, last)])


def gather_heads(half):
    if lax.axis_size("heads") != 2:
        return lax.all_gather(half, "heads", axis=half.ndim - 1, tiled=True)
    me = lax.axis_index("heads")
    other = lax.ppermute(half, "heads", [(0, 1), (1, 0)])
    first = jnp.where(me == 0, half, other)
    second = jnp.where(me == 0, other, half)
    return jnp.concatenate([first, second], axis=-1)


def sum_heads(partial, local_width):
    if lax.axis_size("heads") != 2:
        return lax.psum_scatter(partial, "heads", scatter_dimension=1, tiled=True)
    me = lax.axis_index("heads")
    mine = lax.dynamic_slice_in_dim(partial, me * local_width, local_width, 1)
    theirs = lax.dynamic_slice_in_dim(partial, (1 - me) * local_width, local_width, 1)
    return mine + lax.ppermute(theirs, "heads", [(0, 1), (1, 0)])


def attention_kernel(score_scale, tile_ids, first, vis_ref, q_ref, *refs):
    if first:
        kv_refs = refs[:-7]
        acc_out, m_out, l_out = refs[-7:-4]
    else:
        kv_refs = refs[:-8]
        acc_in, m_in, l_in, o_ref = refs[-8:-4]
    s_scr, m_scr, l_scr, acc_scr = refs[-4:]
    frame = pl.program_id(1)
    q = q_ref[...]
    tiles = [(source, g) for source, ids in enumerate(tile_ids) for g in range(len(ids))]
    slot_of = [ids[g] for ids in tile_ids for g in range(len(ids))]
    m_scr[...] = jnp.full(m_scr.shape, -jnp.inf, jnp.float32)
    for t, (source, g) in enumerate(tiles):

        @pl.when(vis_ref[frame, slot_of[t]] > 0)
        def _():
            k = kv_refs[source][0, g]
            s = (
                lax.dot_general(
                    q, k, (((1,), (1,)), ((), ())), preferred_element_type=jnp.float32
                )
                * score_scale
            )
            s_scr[t] = s
            m_scr[...] = jnp.maximum(m_scr[...], s)

    m = jnp.max(m_scr[...], axis=1, keepdims=True)
    if not first:
        m_prev = m_in[:, 0:1]
        m = jnp.maximum(m_prev, m)
    l_scr[...] = jnp.zeros(l_scr.shape, jnp.float32)
    for t, (source, g) in enumerate(tiles):

        @pl.when(vis_ref[frame, slot_of[t]] > 0)
        def _():
            e = jnp.exp(s_scr[t] - m)
            s_scr[t] = e
            l_scr[...] += e

    total = jnp.sum(l_scr[...], axis=1, keepdims=True)
    if not first:
        carried = l_in[:, 0:1] * jnp.exp(m_prev - m)
        total = carried + total
    acc_scr[...] = jnp.zeros(acc_scr.shape, jnp.float32)
    for t, (source, g) in enumerate(tiles):

        @pl.when(vis_ref[frame, slot_of[t]] > 0)
        def _():
            w = (s_scr[t] / total).astype(jnp.bfloat16)
            acc_scr[...] += jnp.dot(w, kv_refs[source][1, g], preferred_element_type=jnp.float32)

    if first:
        acc_out[...] = acc_scr[...]
        m_out[...] = jnp.broadcast_to(m, m_out.shape)
        l_out[...] = jnp.broadcast_to(total, l_out.shape)
    else:
        o_ref[...] = (acc_in[...] * (carried / total) + acc_scr[...]).astype(o_ref.dtype)


def attention(visible, queries, kv_list, frames, tile_size, carry=None):
    local_width = queries.shape[1]
    heads = local_width // HD
    tile_ids = tuple(tuple(ids) for _, ids in kv_list)
    n_tiles = sum(len(ids) for ids in tile_ids)
    first = carry is None
    kernel = functools.partial(attention_kernel, 1.0 / math.sqrt(HD), tile_ids, first)
    kv_specs = [
        pl.BlockSpec((2, len(ids), tile_size, HD), lambda h, f, vis: (0, 0, 0, h))
        for _, ids in kv_list
    ]
    row_spec = pl.BlockSpec((tile_size, HD), lambda h, f, vis: (f, h))
    row_f32 = jax.ShapeDtypeStruct(queries.shape, jnp.float32)
    if first:
        out_specs = [row_spec] * 3
        out_shape = [row_f32] * 3
        carried = []
    else:
        out_specs = row_spec
        out_shape = jax.ShapeDtypeStruct(queries.shape, jnp.bfloat16)
        carried = list(carry)
    grid_spec = pltpu.PrefetchScalarGridSpec(
        num_scalar_prefetch=1,
        grid=(heads, frames),
        in_specs=[row_spec] + kv_specs + [row_spec] * len(carried),
        out_specs=out_specs,
        scratch_shapes=[
            pltpu.VMEM((n_tiles, tile_size, tile_size), jnp.float32),
            pltpu.VMEM((tile_size, tile_size), jnp.float32),
            pltpu.VMEM((tile_size, tile_size), jnp.float32),
            pltpu.VMEM((tile_size, HD), jnp.float32),
        ],
    )
    tokens = queries.shape[0]
    cost = pl.CostEstimate(
        flops=4 * tokens * n_tiles * tile_size * local_width // 2,
        transcendentals=tokens * n_tiles * tile_size * heads // 2,
        bytes_accessed=(2 * n_tiles * tile_size + 4 * tokens) * local_width * 2,
    )
    return pl.pallas_call(
        kernel,
        grid_spec=grid_spec,
        out_shape=out_shape,
        cost_estimate=cost,
    )(visible, queries, *[kv for kv, _ in kv_list], *carried)


def shards(
    latent,
    query_weight,
    key_weight,
    value_weight,
    output_weight,
    query_gain,
    key_gain,
    modulation,
    noise_level,
    tile_pattern,
):
    frames, strip_rows, columns, local_width = latent.shape
    width = local_width * lax.axis_size("heads")
    token_count = frames * strip_rows * columns
    tile_size = strip_rows * columns
    levels = modulation.shape[0]
    rows = latent.reshape(token_count, local_width)
    whole = gather_heads(rows)
    onehot = (noise_level[0] == jnp.arange(levels, dtype=jnp.int32)).astype(jnp.float32)
    mod_table = jnp.dot(
        onehot[None, :], modulation.reshape(levels, 3 * width), precision=lax.Precision.HIGHEST
    ).reshape(3, width)
    token_rows = whole.astype(jnp.float32)
    center = token_rows - jnp.mean(token_rows, axis=1, keepdims=True)
    normed = center * lax.rsqrt(jnp.mean(center * center, axis=1, keepdims=True) + EPSILON)
    hidden = (normed * (1.0 + mod_table[1]) + mod_table[0]).astype(jnp.bfloat16)
    query_raw = jnp.dot(hidden, query_weight, preferred_element_type=jnp.float32)
    key_raw = jnp.dot(hidden, key_weight, preferred_element_type=jnp.float32)
    value_rows = jnp.dot(hidden, value_weight, preferred_element_type=jnp.float32).astype(
        jnp.bfloat16
    )
    squares = lax.psum(
        (jnp.sum(query_raw * query_raw, axis=1), jnp.sum(key_raw * key_raw, axis=1)), "heads"
    )
    queries = (query_raw * lax.rsqrt(squares[0] / width + EPSILON)[:, None] * query_gain).astype(
        jnp.bfloat16
    )
    key_rows = (key_raw * lax.rsqrt(squares[1] / width + EPSILON)[:, None] * key_gain).astype(
        jnp.bfloat16
    )
    kv = jnp.stack(
        [
            key_rows.reshape(frames, tile_size, local_width),
            value_rows.reshape(frames, tile_size, local_width),
        ]
    )
    own_low = from_behind(kv, "space", 1)
    own_high = from_behind(kv, "space", -1)
    prior_mid = from_behind(kv, "tm", 1)
    split = frames - frames // 3
    low_far = from_behind(prior_mid[:, :split], "space", 1)
    high_far = from_behind(prior_mid[:, :split], "space", -1)
    low_near = from_behind(own_low[:, split:], "tm", 1)
    high_near = from_behind(own_high[:, split:], "tm", 1)
    fr = list(range(frames))
    kv_list = [
        (low_far, [0 * frames + f for f in fr[:split]]),
        (low_near, [0 * frames + f for f in fr[split:]]),
        (prior_mid, [1 * frames + f for f in fr]),
        (high_far, [2 * frames + f for f in fr[:split]]),
        (high_near, [2 * frames + f for f in fr[split:]]),
        (own_low, [3 * frames + f for f in fr]),
        (kv, [4 * frames + f for f in fr]),
        (own_high, [5 * frames + f for f in fr]),
    ]
    pattern = jnp.transpose(tile_pattern[0].reshape(frames, 2, frames, 3), (0, 1, 3, 2))
    span_index = lax.axis_index("tm")
    strip_index = lax.axis_index("space")
    source_valid = jnp.stack([span_index > 0, jnp.array(True)])
    offset_valid = jnp.stack(
        [strip_index > 0, jnp.array(True), strip_index < lax.axis_size("space") - 1]
    )
    visible = (pattern > 0) & source_valid[None, :, None, None] & offset_valid[None, None, :, None]
    visible = visible.reshape(frames, 6 * frames).astype(jnp.int32)
    near = [kv_list[i] for i in (2, 5, 6, 7)]
    far = [kv_list[i] for i in (0, 1, 3, 4)]
    carry = attention(visible, queries, near, frames, tile_size)
    attended = attention(visible, queries, far, frames, tile_size, carry)
    column_start = lax.axis_index("heads") * local_width
    partial = jnp.dot(attended, output_weight, preferred_element_type=jnp.float32)
    projected = sum_heads(partial, local_width)
    gate_half = lax.dynamic_slice_in_dim(mod_table[2], column_start, local_width)
    own_rows = rows.astype(jnp.float32)
    updated = (own_rows + gate_half * projected).astype(jnp.bfloat16)
    return updated.reshape(latent.shape)


def solution(mesh):
    placed = (
        P(("groups", "tm"), "space", None, "heads"),
        P(None, "heads"),
        P(None, "heads"),
        P(None, "heads"),
        P("heads", None),
        P("heads"),
        P("heads"),
        P(),
        P(("groups", "tm")),
        P("space", None, None, None),
    )
    return jax.shard_map(
        shards,
        mesh=mesh,
        in_specs=placed,
        out_specs=P(("groups", "tm"), "space", None, "heads"),
        check_vma=False,
    )
```

```python
import functools
import math

import jax
import jax.numpy as jnp
from jax import lax
from jax.experimental import pallas as pl
from jax.experimental.pallas import tpu as pltpu
from jax.sharding import PartitionSpec as P

HD = 128


EPSILON = 1e-06


def from_behind(value, axis, steps):
    count = lax.axis_size(axis)
    first, last = (max(0, -steps), min(count, count - steps))
    return lax.ppermute(value, axis, [(source, source + steps) for source in range(first, last)])


def gather_heads(half):
    if lax.axis_size("heads") != 2:
        return lax.all_gather(half, "heads", axis=half.ndim - 1, tiled=True)
    me = lax.axis_index("heads")
    other = lax.ppermute(half, "heads", [(0, 1), (1, 0)])
    first = jnp.where(me == 0, half, other)
    second = jnp.where(me == 0, other, half)
    return jnp.concatenate([first, second], axis=-1)


def sum_heads(partial, local_width):
    if lax.axis_size("heads") != 2:
        return lax.psum_scatter(partial, "heads", scatter_dimension=1, tiled=True)
    me = lax.axis_index("heads")
    mine = lax.dynamic_slice_in_dim(partial, me * local_width, local_width, 1)
    theirs = lax.dynamic_slice_in_dim(partial, (1 - me) * local_width, local_width, 1)
    return mine + lax.ppermute(theirs, "heads", [(0, 1), (1, 0)])


def attention_kernel(score_scale, tile_ids, has_in, has_out, vis_ref, q_ref, *refs):
    n_in = len(tile_ids) + (3 if has_in else 0)
    kv_refs = refs[: len(tile_ids)]
    carry_in = refs[len(tile_ids) : n_in]
    outs = refs[n_in:-4]
    s_scr, m_scr, l_scr, acc_scr = refs[-4:]
    frame = pl.program_id(1)
    q = q_ref[...]
    tiles = [(source, g) for source, ids in enumerate(tile_ids) for g in range(len(ids))]
    slot_of = [ids[g] for ids in tile_ids for g in range(len(ids))]
    m_scr[...] = jnp.full(m_scr.shape, -jnp.inf, jnp.float32)
    for t, (source, g) in enumerate(tiles):

        @pl.when(vis_ref[frame, slot_of[t]] > 0)
        def _():
            k = kv_refs[source][0, g]
            s = (
                lax.dot_general(
                    q, k, (((1,), (1,)), ((), ())), preferred_element_type=jnp.float32
                )
                * score_scale
            )
            s_scr[t] = s
            m_scr[...] = jnp.maximum(m_scr[...], s)

    m = jnp.max(m_scr[...], axis=1, keepdims=True)
    if has_in:
        acc_in, m_in, l_in = carry_in
        m_prev = m_in[:, 0:1]
        m = jnp.maximum(m_prev, m)
    l_scr[...] = jnp.zeros(l_scr.shape, jnp.float32)
    for t, (source, g) in enumerate(tiles):

        @pl.when(vis_ref[frame, slot_of[t]] > 0)
        def _():
            e = jnp.exp(s_scr[t] - m)
            s_scr[t] = e
            l_scr[...] += e

    total = jnp.sum(l_scr[...], axis=1, keepdims=True)
    if has_in:
        carried = l_in[:, 0:1] * jnp.exp(m_prev - m)
        total = carried + total
    inverse = 1.0 / total
    if has_in:
        acc_scr[...] = acc_in[...] * (carried * inverse)
    else:
        acc_scr[...] = jnp.zeros(acc_scr.shape, jnp.float32)
    for t, (source, g) in enumerate(tiles):

        @pl.when(vis_ref[frame, slot_of[t]] > 0)
        def _():
            w = (s_scr[t] * inverse).astype(jnp.bfloat16)
            acc_scr[...] += jnp.dot(w, kv_refs[source][1, g], preferred_element_type=jnp.float32)

    if has_out:
        acc_out, m_out, l_out = outs
        acc_out[...] = acc_scr[...]
        m_out[...] = jnp.broadcast_to(m, m_out.shape)
        l_out[...] = jnp.broadcast_to(total, l_out.shape)
    else:
        outs[0][...] = acc_scr[...].astype(outs[0].dtype)


def attention(visible, queries, kv_list, frames, tile_size, carry=None, last=True):
    local_width = queries.shape[1]
    heads = local_width // HD
    tile_ids = tuple(tuple(ids) for _, ids in kv_list)
    n_tiles = sum(len(ids) for ids in tile_ids)
    has_in = carry is not None
    kernel = functools.partial(attention_kernel, 1.0 / math.sqrt(HD), tile_ids, has_in, not last)
    kv_specs = [
        pl.BlockSpec((2, len(ids), tile_size, HD), lambda h, f, vis: (0, 0, 0, h))
        for _, ids in kv_list
    ]
    row_spec = pl.BlockSpec((tile_size, HD), lambda h, f, vis: (f, h))
    row_f32 = jax.ShapeDtypeStruct(queries.shape, jnp.float32)
    if last:
        out_specs = row_spec
        out_shape = jax.ShapeDtypeStruct(queries.shape, jnp.bfloat16)
    else:
        out_specs = [row_spec] * 3
        out_shape = [row_f32] * 3
    carried = list(carry) if has_in else []
    grid_spec = pltpu.PrefetchScalarGridSpec(
        num_scalar_prefetch=1,
        grid=(heads, frames),
        in_specs=[row_spec] + kv_specs + [row_spec] * len(carried),
        out_specs=out_specs,
        scratch_shapes=[
            pltpu.VMEM((n_tiles, tile_size, tile_size), jnp.float32),
            pltpu.VMEM((tile_size, tile_size), jnp.float32),
            pltpu.VMEM((tile_size, tile_size), jnp.float32),
            pltpu.VMEM((tile_size, HD), jnp.float32),
        ],
    )
    tokens = queries.shape[0]
    cost = pl.CostEstimate(
        flops=4 * tokens * n_tiles * tile_size * local_width // 2,
        transcendentals=tokens * n_tiles * tile_size * heads // 2,
        bytes_accessed=(2 * n_tiles * tile_size + 4 * tokens) * local_width * 2,
    )
    return pl.pallas_call(
        kernel,
        grid_spec=grid_spec,
        out_shape=out_shape,
        cost_estimate=cost,
    )(visible, queries, *[kv for kv, _ in kv_list], *carried)


def shards(
    latent,
    query_weight,
    key_weight,
    value_weight,
    output_weight,
    query_gain,
    key_gain,
    modulation,
    noise_level,
    tile_pattern,
):
    frames, strip_rows, columns, local_width = latent.shape
    width = local_width * lax.axis_size("heads")
    token_count = frames * strip_rows * columns
    tile_size = strip_rows * columns
    levels = modulation.shape[0]
    rows = latent.reshape(token_count, local_width)
    whole = gather_heads(rows)
    onehot = (noise_level[0] == jnp.arange(levels, dtype=jnp.int32)).astype(jnp.float32)
    mod_table = jnp.dot(
        onehot[None, :], modulation.reshape(levels, 3 * width), precision=lax.Precision.HIGHEST
    ).reshape(3, width)
    token_rows = whole.astype(jnp.float32)
    center = token_rows - jnp.mean(token_rows, axis=1, keepdims=True)
    normed = center * lax.rsqrt(jnp.mean(center * center, axis=1, keepdims=True) + EPSILON)
    hidden = (normed * (1.0 + mod_table[1]) + mod_table[0]).astype(jnp.bfloat16)
    query_raw = jnp.dot(hidden, query_weight, preferred_element_type=jnp.float32)
    key_raw = jnp.dot(hidden, key_weight, preferred_element_type=jnp.float32)
    value_rows = jnp.dot(hidden, value_weight, preferred_element_type=jnp.float32).astype(
        jnp.bfloat16
    )
    squares = lax.psum(
        (jnp.sum(query_raw * query_raw, axis=1), jnp.sum(key_raw * key_raw, axis=1)), "heads"
    )
    queries = (query_raw * lax.rsqrt(squares[0] / width + EPSILON)[:, None] * query_gain).astype(
        jnp.bfloat16
    )
    key_rows = (key_raw * lax.rsqrt(squares[1] / width + EPSILON)[:, None] * key_gain).astype(
        jnp.bfloat16
    )
    kv = jnp.stack(
        [
            key_rows.reshape(frames, tile_size, local_width),
            value_rows.reshape(frames, tile_size, local_width),
        ]
    )
    own_low = from_behind(kv, "space", 1)
    own_high = from_behind(kv, "space", -1)
    prior_mid = from_behind(kv, "tm", 1)
    split = frames - frames // 3
    low_far = from_behind(prior_mid[:, :split], "space", 1)
    high_far = from_behind(prior_mid[:, :split], "space", -1)
    low_near = from_behind(own_low[:, split:], "tm", 1)
    high_near = from_behind(own_high[:, split:], "tm", 1)
    fr = list(range(frames))
    kv_list = [
        (low_far, [0 * frames + f for f in fr[:split]]),
        (low_near, [0 * frames + f for f in fr[split:]]),
        (prior_mid, [1 * frames + f for f in fr]),
        (high_far, [2 * frames + f for f in fr[:split]]),
        (high_near, [2 * frames + f for f in fr[split:]]),
        (own_low, [3 * frames + f for f in fr]),
        (kv, [4 * frames + f for f in fr]),
        (own_high, [5 * frames + f for f in fr]),
    ]
    pattern = jnp.transpose(tile_pattern[0].reshape(frames, 2, frames, 3), (0, 1, 3, 2))
    span_index = lax.axis_index("tm")
    strip_index = lax.axis_index("space")
    source_valid = jnp.stack([span_index > 0, jnp.array(True)])
    offset_valid = jnp.stack(
        [strip_index > 0, jnp.array(True), strip_index < lax.axis_size("space") - 1]
    )
    visible = (pattern > 0) & source_valid[None, :, None, None] & offset_valid[None, None, :, None]
    visible = visible.reshape(frames, 6 * frames).astype(jnp.int32)
    own = [kv_list[6]]
    near = [kv_list[i] for i in (2, 5, 7)]
    far = [kv_list[i] for i in (0, 1, 3, 4)]
    carry = attention(visible, queries, own, frames, tile_size, last=False)
    carry = attention(visible, queries, near, frames, tile_size, carry, last=False)
    attended = attention(visible, queries, far, frames, tile_size, carry)
    column_start = lax.axis_index("heads") * local_width
    partial = jnp.dot(attended, output_weight, preferred_element_type=jnp.float32)
    projected = sum_heads(partial, local_width)
    gate_half = lax.dynamic_slice_in_dim(mod_table[2], column_start, local_width)
    own_rows = rows.astype(jnp.float32)
    updated = (own_rows + gate_half * projected).astype(jnp.bfloat16)
    return updated.reshape(latent.shape)


def solution(mesh):
    placed = (
        P(("groups", "tm"), "space", None, "heads"),
        P(None, "heads"),
        P(None, "heads"),
        P(None, "heads"),
        P("heads", None),
        P("heads"),
        P("heads"),
        P(),
        P(("groups", "tm")),
        P("space", None, None, None),
    )
    return jax.shard_map(
        shards,
        mesh=mesh,
        in_specs=placed,
        out_specs=P(("groups", "tm"), "space", None, "heads"),
        check_vma=False,
    )
```

```python
import functools
import math

import jax
import jax.numpy as jnp
from jax import lax
from jax.experimental import pallas as pl
from jax.experimental.pallas import tpu as pltpu
from jax.sharding import PartitionSpec as P

HD = 128


EPSILON = 1e-06


def from_behind(value, axis, steps):
    count = lax.axis_size(axis)
    first, last = (max(0, -steps), min(count, count - steps))
    return lax.ppermute(value, axis, [(source, source + steps) for source in range(first, last)])


def gather_heads(half):
    if lax.axis_size("heads") != 2:
        return lax.all_gather(half, "heads", axis=half.ndim - 1, tiled=True)
    me = lax.axis_index("heads")
    other = lax.ppermute(half, "heads", [(0, 1), (1, 0)])
    first = jnp.where(me == 0, half, other)
    second = jnp.where(me == 0, other, half)
    return jnp.concatenate([first, second], axis=-1)


def sum_heads(partial, local_width):
    if lax.axis_size("heads") != 2:
        return lax.psum_scatter(partial, "heads", scatter_dimension=1, tiled=True)
    me = lax.axis_index("heads")
    mine = lax.dynamic_slice_in_dim(partial, me * local_width, local_width, 1)
    theirs = lax.dynamic_slice_in_dim(partial, (1 - me) * local_width, local_width, 1)
    return mine + lax.ppermute(theirs, "heads", [(0, 1), (1, 0)])


def attention_kernel(score_scale, tile_ids, has_in, has_out, vis_ref, q_ref, *refs):
    n_in = len(tile_ids) + (3 if has_in else 0)
    kv_refs = refs[: len(tile_ids)]
    carry_in = refs[len(tile_ids) : n_in]
    outs = refs[n_in:-4]
    s_scr, m_scr, l_scr, acc_scr = refs[-4:]
    frame = pl.program_id(1)
    q = q_ref[...]
    tiles = [(source, g) for source, ids in enumerate(tile_ids) for g in range(len(ids))]
    slot_of = [ids[g] for ids in tile_ids for g in range(len(ids))]
    m_scr[...] = jnp.full(m_scr.shape, -jnp.inf, jnp.float32)
    for t, (source, g) in enumerate(tiles):

        @pl.when(vis_ref[frame, slot_of[t]] > 0)
        def _():
            k = kv_refs[source][0, g]
            s = (
                lax.dot_general(
                    q, k, (((1,), (1,)), ((), ())), preferred_element_type=jnp.float32
                )
                * score_scale
            )
            s_scr[t] = s
            m_scr[...] = jnp.maximum(m_scr[...], s)

    m = jnp.max(m_scr[...], axis=1, keepdims=True)
    if has_in:
        acc_in, m_in, l_in = carry_in
        m_prev = m_in[:, 0:1]
        m = jnp.maximum(m_prev, m)
        rescale = jnp.exp(m_prev - m)
        acc_scr[...] = acc_in[...] * rescale
    else:
        acc_scr[...] = jnp.zeros(acc_scr.shape, jnp.float32)
    l_scr[...] = jnp.zeros(l_scr.shape, jnp.float32)
    for t, (source, g) in enumerate(tiles):

        @pl.when(vis_ref[frame, slot_of[t]] > 0)
        def _():
            e = jnp.exp(s_scr[t] - m)
            l_scr[...] += e
            acc_scr[...] += jnp.dot(
                e.astype(jnp.bfloat16), kv_refs[source][1, g], preferred_element_type=jnp.float32
            )

    total = jnp.sum(l_scr[...], axis=1, keepdims=True)
    if has_in:
        total = l_in[:, 0:1] * rescale + total
    if has_out:
        acc_out, m_out, l_out = outs
        acc_out[...] = acc_scr[...]
        m_out[...] = jnp.broadcast_to(m, m_out.shape)
        l_out[...] = jnp.broadcast_to(total, l_out.shape)
    else:
        outs[0][...] = (acc_scr[...] / total).astype(outs[0].dtype)


def attention(visible, queries, kv_list, frames, tile_size, carry=None, last=True):
    local_width = queries.shape[1]
    heads = local_width // HD
    tile_ids = tuple(tuple(ids) for _, ids in kv_list)
    n_tiles = sum(len(ids) for ids in tile_ids)
    has_in = carry is not None
    kernel = functools.partial(attention_kernel, 1.0 / math.sqrt(HD), tile_ids, has_in, not last)
    kv_specs = [
        pl.BlockSpec((2, len(ids), tile_size, HD), lambda h, f, vis: (0, 0, 0, h))
        for _, ids in kv_list
    ]
    row_spec = pl.BlockSpec((tile_size, HD), lambda h, f, vis: (f, h))
    row_f32 = jax.ShapeDtypeStruct(queries.shape, jnp.float32)
    if last:
        out_specs = row_spec
        out_shape = jax.ShapeDtypeStruct(queries.shape, jnp.bfloat16)
    else:
        out_specs = [row_spec] * 3
        out_shape = [row_f32] * 3
    carried = list(carry) if has_in else []
    grid_spec = pltpu.PrefetchScalarGridSpec(
        num_scalar_prefetch=1,
        grid=(heads, frames),
        in_specs=[row_spec] + kv_specs + [row_spec] * len(carried),
        out_specs=out_specs,
        scratch_shapes=[
            pltpu.VMEM((n_tiles, tile_size, tile_size), jnp.float32),
            pltpu.VMEM((tile_size, tile_size), jnp.float32),
            pltpu.VMEM((tile_size, tile_size), jnp.float32),
            pltpu.VMEM((tile_size, HD), jnp.float32),
        ],
    )
    tokens = queries.shape[0]
    cost = pl.CostEstimate(
        flops=4 * tokens * n_tiles * tile_size * local_width // 2,
        transcendentals=tokens * n_tiles * tile_size * heads // 2,
        bytes_accessed=(2 * n_tiles * tile_size + 4 * tokens) * local_width * 2,
    )
    return pl.pallas_call(
        kernel,
        grid_spec=grid_spec,
        out_shape=out_shape,
        cost_estimate=cost,
    )(visible, queries, *[kv for kv, _ in kv_list], *carried)


def shards(
    latent,
    query_weight,
    key_weight,
    value_weight,
    output_weight,
    query_gain,
    key_gain,
    modulation,
    noise_level,
    tile_pattern,
):
    frames, strip_rows, columns, local_width = latent.shape
    width = local_width * lax.axis_size("heads")
    token_count = frames * strip_rows * columns
    tile_size = strip_rows * columns
    levels = modulation.shape[0]
    rows = latent.reshape(token_count, local_width)
    whole = gather_heads(rows)
    onehot = (noise_level[0] == jnp.arange(levels, dtype=jnp.int32)).astype(jnp.float32)
    mod_table = jnp.dot(
        onehot[None, :], modulation.reshape(levels, 3 * width), precision=lax.Precision.HIGHEST
    ).reshape(3, width)
    token_rows = whole.astype(jnp.float32)
    center = token_rows - jnp.mean(token_rows, axis=1, keepdims=True)
    normed = center * lax.rsqrt(jnp.mean(center * center, axis=1, keepdims=True) + EPSILON)
    hidden = (normed * (1.0 + mod_table[1]) + mod_table[0]).astype(jnp.bfloat16)
    query_raw = jnp.dot(hidden, query_weight, preferred_element_type=jnp.float32)
    key_raw = jnp.dot(hidden, key_weight, preferred_element_type=jnp.float32)
    value_rows = jnp.dot(hidden, value_weight, preferred_element_type=jnp.float32).astype(
        jnp.bfloat16
    )
    squares = lax.psum(
        (jnp.sum(query_raw * query_raw, axis=1), jnp.sum(key_raw * key_raw, axis=1)), "heads"
    )
    queries = (query_raw * lax.rsqrt(squares[0] / width + EPSILON)[:, None] * query_gain).astype(
        jnp.bfloat16
    )
    key_rows = (key_raw * lax.rsqrt(squares[1] / width + EPSILON)[:, None] * key_gain).astype(
        jnp.bfloat16
    )
    kv = jnp.stack(
        [
            key_rows.reshape(frames, tile_size, local_width),
            value_rows.reshape(frames, tile_size, local_width),
        ]
    )
    own_low = from_behind(kv, "space", 1)
    own_high = from_behind(kv, "space", -1)
    prior_mid = from_behind(kv, "tm", 1)
    split = frames - frames // 3
    low_far = from_behind(prior_mid[:, :split], "space", 1)
    high_far = from_behind(prior_mid[:, :split], "space", -1)
    low_near = from_behind(own_low[:, split:], "tm", 1)
    high_near = from_behind(own_high[:, split:], "tm", 1)
    fr = list(range(frames))
    kv_list = [
        (low_far, [0 * frames + f for f in fr[:split]]),
        (low_near, [0 * frames + f for f in fr[split:]]),
        (prior_mid, [1 * frames + f for f in fr]),
        (high_far, [2 * frames + f for f in fr[:split]]),
        (high_near, [2 * frames + f for f in fr[split:]]),
        (own_low, [3 * frames + f for f in fr]),
        (kv, [4 * frames + f for f in fr]),
        (own_high, [5 * frames + f for f in fr]),
    ]
    pattern = jnp.transpose(tile_pattern[0].reshape(frames, 2, frames, 3), (0, 1, 3, 2))
    span_index = lax.axis_index("tm")
    strip_index = lax.axis_index("space")
    source_valid = jnp.stack([span_index > 0, jnp.array(True)])
    offset_valid = jnp.stack(
        [strip_index > 0, jnp.array(True), strip_index < lax.axis_size("space") - 1]
    )
    visible = (pattern > 0) & source_valid[None, :, None, None] & offset_valid[None, None, :, None]
    visible = visible.reshape(frames, 6 * frames).astype(jnp.int32)
    near = [kv_list[i] for i in (2, 5, 6, 7)]
    far = [kv_list[i] for i in (0, 1, 3, 4)]
    carry = attention(visible, queries, near, frames, tile_size, last=False)
    attended = attention(visible, queries, far, frames, tile_size, carry)
    column_start = lax.axis_index("heads") * local_width
    partial = jnp.dot(attended, output_weight, preferred_element_type=jnp.float32)
    projected = sum_heads(partial, local_width)
    gate_half = lax.dynamic_slice_in_dim(mod_table[2], column_start, local_width)
    own_rows = rows.astype(jnp.float32)
    updated = (own_rows + gate_half * projected).astype(jnp.bfloat16)
    return updated.reshape(latent.shape)


def solution(mesh):
    placed = (
        P(("groups", "tm"), "space", None, "heads"),
        P(None, "heads"),
        P(None, "heads"),
        P(None, "heads"),
        P("heads", None),
        P("heads"),
        P("heads"),
        P(),
        P(("groups", "tm")),
        P("space", None, None, None),
    )
    return jax.shard_map(
        shards,
        mesh=mesh,
        in_specs=placed,
        out_specs=P(("groups", "tm"), "space", None, "heads"),
        check_vma=False,
    )
```

```python
import functools
import math

import jax
import jax.numpy as jnp
from jax import lax
from jax.experimental import pallas as pl
from jax.experimental.pallas import tpu as pltpu
from jax.sharding import PartitionSpec as P

HD = 128


EPSILON = 1e-06


def from_behind(value, axis, steps):
    count = lax.axis_size(axis)
    first, last = (max(0, -steps), min(count, count - steps))
    return lax.ppermute(value, axis, [(source, source + steps) for source in range(first, last)])


def gather_heads(half):
    if lax.axis_size("heads") != 2:
        return lax.all_gather(half, "heads", axis=half.ndim - 1, tiled=True)
    me = lax.axis_index("heads")
    other = lax.ppermute(half, "heads", [(0, 1), (1, 0)])
    first = jnp.where(me == 0, half, other)
    second = jnp.where(me == 0, other, half)
    return jnp.concatenate([first, second], axis=-1)


def sum_heads(partial, local_width):
    if lax.axis_size("heads") != 2:
        return lax.psum_scatter(partial, "heads", scatter_dimension=1, tiled=True)
    me = lax.axis_index("heads")
    mine = lax.dynamic_slice_in_dim(partial, me * local_width, local_width, 1)
    theirs = lax.dynamic_slice_in_dim(partial, (1 - me) * local_width, local_width, 1)
    return mine + lax.ppermute(theirs, "heads", [(0, 1), (1, 0)])


def attention_kernel(score_scale, tile_ids, has_in, has_out, vis_ref, q_ref, *refs):
    n_in = len(tile_ids) + (3 if has_in else 0)
    kv_refs = refs[: len(tile_ids)]
    carry_in = refs[len(tile_ids) : n_in]
    outs = refs[n_in:-4]
    s_scr, m_scr, l_scr, acc_scr = refs[-4:]
    frame = pl.program_id(1)
    q = q_ref[...]
    tiles = [(source, g) for source, ids in enumerate(tile_ids) for g in range(len(ids))]
    slot_of = [ids[g] for ids in tile_ids for g in range(len(ids))]
    m_scr[...] = jnp.full(m_scr.shape, -jnp.inf, jnp.float32)
    for t, (source, g) in enumerate(tiles):

        @pl.when(vis_ref[frame, slot_of[t]] > 0)
        def _():
            k = kv_refs[source][0, g]
            s = (
                lax.dot_general(
                    q, k, (((1,), (1,)), ((), ())), preferred_element_type=jnp.float32
                )
                * score_scale
            )
            s_scr[t] = s
            m_scr[...] = jnp.maximum(m_scr[...], s)

    m = jnp.max(m_scr[...], axis=1, keepdims=True)
    if has_in:
        acc_in, m_in, l_in = carry_in
        m_prev = m_in[:, 0:1]
        m = jnp.maximum(m_prev, m)
        rescale = jnp.exp(m_prev - m)
        acc_scr[...] = acc_in[...] * rescale
    else:
        acc_scr[...] = jnp.zeros(acc_scr.shape, jnp.float32)
    l_scr[...] = jnp.zeros(l_scr.shape, jnp.float32)
    for t, (source, g) in enumerate(tiles):

        @pl.when(vis_ref[frame, slot_of[t]] > 0)
        def _():
            e = jnp.exp(s_scr[t] - m)
            l_scr[...] += e
            acc_scr[...] += jnp.dot(
                e.astype(jnp.bfloat16), kv_refs[source][1, g], preferred_element_type=jnp.float32
            )

    total = jnp.sum(l_scr[...], axis=1, keepdims=True)
    if has_in:
        total = l_in[:, 0:1] * rescale + total
    if has_out:
        acc_out, m_out, l_out = outs
        acc_out[...] = acc_scr[...]
        m_out[...] = jnp.broadcast_to(m, m_out.shape)
        l_out[...] = jnp.broadcast_to(total, l_out.shape)
    else:
        outs[0][...] = (acc_scr[...] / total).astype(outs[0].dtype)


def attention(visible, queries, kv_list, frames, tile_size, carry=None, last=True):
    local_width = queries.shape[1]
    heads = local_width // HD
    tile_ids = tuple(tuple(ids) for _, ids in kv_list)
    n_tiles = sum(len(ids) for ids in tile_ids)
    has_in = carry is not None
    kernel = functools.partial(attention_kernel, 1.0 / math.sqrt(HD), tile_ids, has_in, not last)
    kv_specs = [
        pl.BlockSpec((2, len(ids), tile_size, HD), lambda h, f, vis: (0, 0, 0, h))
        for _, ids in kv_list
    ]
    row_spec = pl.BlockSpec((tile_size, HD), lambda h, f, vis: (f, h))
    row_f32 = jax.ShapeDtypeStruct(queries.shape, jnp.float32)
    if last:
        out_specs = row_spec
        out_shape = jax.ShapeDtypeStruct(queries.shape, jnp.bfloat16)
    else:
        out_specs = [row_spec] * 3
        out_shape = [row_f32] * 3
    carried = list(carry) if has_in else []
    grid_spec = pltpu.PrefetchScalarGridSpec(
        num_scalar_prefetch=1,
        grid=(heads, frames),
        in_specs=[row_spec] + kv_specs + [row_spec] * len(carried),
        out_specs=out_specs,
        scratch_shapes=[
            pltpu.VMEM((n_tiles, tile_size, tile_size), jnp.float32),
            pltpu.VMEM((tile_size, tile_size), jnp.float32),
            pltpu.VMEM((tile_size, tile_size), jnp.float32),
            pltpu.VMEM((tile_size, HD), jnp.float32),
        ],
    )
    tokens = queries.shape[0]
    cost = pl.CostEstimate(
        flops=4 * tokens * n_tiles * tile_size * local_width // 2,
        transcendentals=tokens * n_tiles * tile_size * heads // 2,
        bytes_accessed=(2 * n_tiles * tile_size + 4 * tokens) * local_width * 2,
    )
    return pl.pallas_call(
        kernel,
        grid_spec=grid_spec,
        out_shape=out_shape,
        cost_estimate=cost,
    )(visible, queries, *[kv for kv, _ in kv_list], *carried)


def shards(
    latent,
    query_weight,
    key_weight,
    value_weight,
    output_weight,
    query_gain,
    key_gain,
    modulation,
    noise_level,
    tile_pattern,
):
    frames, strip_rows, columns, local_width = latent.shape
    width = local_width * lax.axis_size("heads")
    token_count = frames * strip_rows * columns
    tile_size = strip_rows * columns
    levels = modulation.shape[0]
    rows = latent.reshape(token_count, local_width)
    whole = gather_heads(rows)
    onehot = (noise_level[0] == jnp.arange(levels, dtype=jnp.int32)).astype(jnp.float32)
    mod_table = jnp.dot(
        onehot[None, :], modulation.reshape(levels, 3 * width), precision=lax.Precision.HIGHEST
    ).reshape(3, width)
    token_rows = whole.astype(jnp.float32)
    center = token_rows - jnp.mean(token_rows, axis=1, keepdims=True)
    normed = center * lax.rsqrt(jnp.mean(center * center, axis=1, keepdims=True) + EPSILON)
    hidden = (normed * (1.0 + mod_table[1]) + mod_table[0]).astype(jnp.bfloat16)
    query_raw = jnp.dot(hidden, query_weight, preferred_element_type=jnp.float32)
    key_raw = jnp.dot(hidden, key_weight, preferred_element_type=jnp.float32)
    value_rows = jnp.dot(hidden, value_weight, preferred_element_type=jnp.float32).astype(
        jnp.bfloat16
    )
    squares = lax.psum(
        (jnp.sum(query_raw * query_raw, axis=1), jnp.sum(key_raw * key_raw, axis=1)), "heads"
    )
    queries = (query_raw * lax.rsqrt(squares[0] / width + EPSILON)[:, None] * query_gain).astype(
        jnp.bfloat16
    )
    key_rows = (key_raw * lax.rsqrt(squares[1] / width + EPSILON)[:, None] * key_gain).astype(
        jnp.bfloat16
    )
    kv = jnp.stack(
        [
            key_rows.reshape(frames, tile_size, local_width),
            value_rows.reshape(frames, tile_size, local_width),
        ]
    )
    pattern = jnp.transpose(tile_pattern[0].reshape(frames, 2, frames, 3), (0, 1, 3, 2))
    span_index = lax.axis_index("tm")
    strip_index = lax.axis_index("space")
    source_valid = jnp.stack([span_index > 0, jnp.array(True)])
    offset_valid = jnp.stack(
        [strip_index > 0, jnp.array(True), strip_index < lax.axis_size("space") - 1]
    )
    visible = (pattern > 0) & source_valid[None, :, None, None] & offset_valid[None, None, :, None]
    visible = visible.reshape(frames, 6 * frames).astype(jnp.int32)
    fr = list(range(frames))

    def ids(slot, part):
        return [slot * frames + f for f in part]

    own_low = from_behind(kv, "space", 1)
    own_high = from_behind(kv, "space", -1)
    prior_mid = from_behind(kv, "tm", 1)
    carry = attention(visible, queries, [(kv, ids(4, fr))], frames, tile_size, last=False)
    carry, own_low, own_high, prior_mid = lax.optimization_barrier(
        (carry, own_low, own_high, prior_mid)
    )
    split = frames - frames // 3
    low_far = from_behind(prior_mid[:, :split], "space", 1)
    high_far = from_behind(prior_mid[:, :split], "space", -1)
    low_near = from_behind(own_low[:, split:], "tm", 1)
    high_near = from_behind(own_high[:, split:], "tm", 1)
    near = [(prior_mid, ids(1, fr)), (own_low, ids(3, fr)), (own_high, ids(5, fr))]
    far = [
        (low_far, ids(0, fr[:split])),
        (low_near, ids(0, fr[split:])),
        (high_far, ids(2, fr[:split])),
        (high_near, ids(2, fr[split:])),
    ]
    carry = attention(visible, queries, near, frames, tile_size, carry, last=False)
    attended = attention(visible, queries, far, frames, tile_size, carry)
    column_start = lax.axis_index("heads") * local_width
    partial = jnp.dot(attended, output_weight, preferred_element_type=jnp.float32)
    projected = sum_heads(partial, local_width)
    gate_half = lax.dynamic_slice_in_dim(mod_table[2], column_start, local_width)
    own_rows = rows.astype(jnp.float32)
    updated = (own_rows + gate_half * projected).astype(jnp.bfloat16)
    return updated.reshape(latent.shape)


def solution(mesh):
    placed = (
        P(("groups", "tm"), "space", None, "heads"),
        P(None, "heads"),
        P(None, "heads"),
        P(None, "heads"),
        P("heads", None),
        P("heads"),
        P("heads"),
        P(),
        P(("groups", "tm")),
        P("space", None, None, None),
    )
    return jax.shard_map(
        shards,
        mesh=mesh,
        in_specs=placed,
        out_specs=P(("groups", "tm"), "space", None, "heads"),
        check_vma=False,
    )
```

```python
import functools
import math

import jax
import jax.numpy as jnp
from jax import lax
from jax.experimental import pallas as pl
from jax.experimental.pallas import tpu as pltpu
from jax.sharding import PartitionSpec as P

HD = 128


EPSILON = 1e-06


def from_behind(value, axis, steps):
    count = lax.axis_size(axis)
    first, last = (max(0, -steps), min(count, count - steps))
    return lax.ppermute(value, axis, [(source, source + steps) for source in range(first, last)])


def gather_heads(half):
    if lax.axis_size("heads") != 2:
        return lax.all_gather(half, "heads", axis=half.ndim - 1, tiled=True)
    me = lax.axis_index("heads")
    other = lax.ppermute(half, "heads", [(0, 1), (1, 0)])
    first = jnp.where(me == 0, half, other)
    second = jnp.where(me == 0, other, half)
    return jnp.concatenate([first, second], axis=-1)


def sum_heads(partial, local_width):
    if lax.axis_size("heads") != 2:
        return lax.psum_scatter(partial, "heads", scatter_dimension=1, tiled=True)
    me = lax.axis_index("heads")
    mine = lax.dynamic_slice_in_dim(partial, me * local_width, local_width, 1)
    theirs = lax.dynamic_slice_in_dim(partial, (1 - me) * local_width, local_width, 1)
    return mine + lax.ppermute(theirs, "heads", [(0, 1), (1, 0)])


def output_columns(attended, output_weight, local_width):
    if lax.axis_size("heads") != 2:
        partial = jnp.dot(attended, output_weight, preferred_element_type=jnp.float32)
        return sum_heads(partial, local_width)
    me = lax.axis_index("heads")
    swap = [(0, 1), (1, 0)]
    mine = lax.dynamic_slice_in_dim(output_weight, me * local_width, local_width, 1)
    theirs = lax.dynamic_slice_in_dim(output_weight, (1 - me) * local_width, local_width, 1)
    received = lax.ppermute(theirs, "heads", swap)
    other = lax.ppermute(attended, "heads", swap)
    return jnp.dot(attended, mine, preferred_element_type=jnp.float32) + jnp.dot(
        other, received, preferred_element_type=jnp.float32
    )


def attention_kernel(score_scale, tile_ids, has_in, has_out, vis_ref, q_ref, *refs):
    n_in = len(tile_ids) + (3 if has_in else 0)
    kv_refs = refs[: len(tile_ids)]
    carry_in = refs[len(tile_ids) : n_in]
    outs = refs[n_in:-4]
    s_scr, m_scr, l_scr, acc_scr = refs[-4:]
    frame = pl.program_id(1)
    q = q_ref[...]
    tiles = [(source, g) for source, ids in enumerate(tile_ids) for g in range(len(ids))]
    slot_of = [ids[g] for ids in tile_ids for g in range(len(ids))]
    m_scr[...] = jnp.full(m_scr.shape, -jnp.inf, jnp.float32)
    for t, (source, g) in enumerate(tiles):

        @pl.when(vis_ref[frame, slot_of[t]] > 0)
        def _():
            k = kv_refs[source][0, g]
            s = (
                lax.dot_general(
                    q, k, (((1,), (1,)), ((), ())), preferred_element_type=jnp.float32
                )
                * score_scale
            )
            s_scr[t] = s
            m_scr[...] = jnp.maximum(m_scr[...], s)

    m = jnp.max(m_scr[...], axis=1, keepdims=True)
    if has_in:
        acc_in, m_in, l_in = carry_in
        m_prev = m_in[:, 0:1]
        m = jnp.maximum(m_prev, m)
        rescale = jnp.exp(m_prev - m)
        acc_scr[...] = acc_in[...] * rescale
    else:
        acc_scr[...] = jnp.zeros(acc_scr.shape, jnp.float32)
    l_scr[...] = jnp.zeros(l_scr.shape, jnp.float32)
    for t, (source, g) in enumerate(tiles):

        @pl.when(vis_ref[frame, slot_of[t]] > 0)
        def _():
            e = jnp.exp(s_scr[t] - m)
            l_scr[...] += e
            acc_scr[...] += jnp.dot(
                e.astype(jnp.bfloat16), kv_refs[source][1, g], preferred_element_type=jnp.float32
            )

    total = jnp.sum(l_scr[...], axis=1, keepdims=True)
    if has_in:
        total = l_in[:, 0:1] * rescale + total
    if has_out:
        acc_out, m_out, l_out = outs
        acc_out[...] = acc_scr[...]
        m_out[...] = jnp.broadcast_to(m, m_out.shape)
        l_out[...] = jnp.broadcast_to(total, l_out.shape)
    else:
        outs[0][...] = (acc_scr[...] / total).astype(outs[0].dtype)


def attention(visible, queries, kv_list, frames, tile_size, carry=None, last=True):
    local_width = queries.shape[1]
    heads = local_width // HD
    tile_ids = tuple(tuple(ids) for _, ids in kv_list)
    n_tiles = sum(len(ids) for ids in tile_ids)
    has_in = carry is not None
    kernel = functools.partial(attention_kernel, 1.0 / math.sqrt(HD), tile_ids, has_in, not last)
    kv_specs = [
        pl.BlockSpec((2, len(ids), tile_size, HD), lambda h, f, vis: (0, 0, 0, h))
        for _, ids in kv_list
    ]
    row_spec = pl.BlockSpec((tile_size, HD), lambda h, f, vis: (f, h))
    row_f32 = jax.ShapeDtypeStruct(queries.shape, jnp.float32)
    if last:
        out_specs = row_spec
        out_shape = jax.ShapeDtypeStruct(queries.shape, jnp.bfloat16)
    else:
        out_specs = [row_spec] * 3
        out_shape = [row_f32] * 3
    carried = list(carry) if has_in else []
    grid_spec = pltpu.PrefetchScalarGridSpec(
        num_scalar_prefetch=1,
        grid=(heads, frames),
        in_specs=[row_spec] + kv_specs + [row_spec] * len(carried),
        out_specs=out_specs,
        scratch_shapes=[
            pltpu.VMEM((n_tiles, tile_size, tile_size), jnp.float32),
            pltpu.VMEM((tile_size, tile_size), jnp.float32),
            pltpu.VMEM((tile_size, tile_size), jnp.float32),
            pltpu.VMEM((tile_size, HD), jnp.float32),
        ],
    )
    tokens = queries.shape[0]
    cost = pl.CostEstimate(
        flops=4 * tokens * n_tiles * tile_size * local_width // 2,
        transcendentals=tokens * n_tiles * tile_size * heads // 2,
        bytes_accessed=(2 * n_tiles * tile_size + 4 * tokens) * local_width * 2,
    )
    return pl.pallas_call(
        kernel,
        grid_spec=grid_spec,
        out_shape=out_shape,
        cost_estimate=cost,
    )(visible, queries, *[kv for kv, _ in kv_list], *carried)


def shards(
    latent,
    query_weight,
    key_weight,
    value_weight,
    output_weight,
    query_gain,
    key_gain,
    modulation,
    noise_level,
    tile_pattern,
):
    frames, strip_rows, columns, local_width = latent.shape
    width = local_width * lax.axis_size("heads")
    token_count = frames * strip_rows * columns
    tile_size = strip_rows * columns
    levels = modulation.shape[0]
    rows = latent.reshape(token_count, local_width)
    whole = gather_heads(rows)
    onehot = (noise_level[0] == jnp.arange(levels, dtype=jnp.int32)).astype(jnp.float32)
    mod_table = jnp.dot(
        onehot[None, :], modulation.reshape(levels, 3 * width), precision=lax.Precision.HIGHEST
    ).reshape(3, width)
    token_rows = whole.astype(jnp.float32)
    center = token_rows - jnp.mean(token_rows, axis=1, keepdims=True)
    normed = center * lax.rsqrt(jnp.mean(center * center, axis=1, keepdims=True) + EPSILON)
    hidden = (normed * (1.0 + mod_table[1]) + mod_table[0]).astype(jnp.bfloat16)
    query_raw = jnp.dot(hidden, query_weight, preferred_element_type=jnp.float32)
    key_raw = jnp.dot(hidden, key_weight, preferred_element_type=jnp.float32)
    value_rows = jnp.dot(hidden, value_weight, preferred_element_type=jnp.float32).astype(
        jnp.bfloat16
    )
    squares = lax.psum(
        (jnp.sum(query_raw * query_raw, axis=1), jnp.sum(key_raw * key_raw, axis=1)), "heads"
    )
    queries = (query_raw * lax.rsqrt(squares[0] / width + EPSILON)[:, None] * query_gain).astype(
        jnp.bfloat16
    )
    key_rows = (key_raw * lax.rsqrt(squares[1] / width + EPSILON)[:, None] * key_gain).astype(
        jnp.bfloat16
    )
    kv = jnp.stack(
        [
            key_rows.reshape(frames, tile_size, local_width),
            value_rows.reshape(frames, tile_size, local_width),
        ]
    )
    own_low = from_behind(kv, "space", 1)
    own_high = from_behind(kv, "space", -1)
    prior_mid = from_behind(kv, "tm", 1)
    split = frames - frames // 3
    low_far = from_behind(prior_mid[:, :split], "space", 1)
    high_far = from_behind(prior_mid[:, :split], "space", -1)
    low_near = from_behind(own_low[:, split:], "tm", 1)
    high_near = from_behind(own_high[:, split:], "tm", 1)
    fr = list(range(frames))
    kv_list = [
        (low_far, [0 * frames + f for f in fr[:split]]),
        (low_near, [0 * frames + f for f in fr[split:]]),
        (prior_mid, [1 * frames + f for f in fr]),
        (high_far, [2 * frames + f for f in fr[:split]]),
        (high_near, [2 * frames + f for f in fr[split:]]),
        (own_low, [3 * frames + f for f in fr]),
        (kv, [4 * frames + f for f in fr]),
        (own_high, [5 * frames + f for f in fr]),
    ]
    pattern = jnp.transpose(tile_pattern[0].reshape(frames, 2, frames, 3), (0, 1, 3, 2))
    span_index = lax.axis_index("tm")
    strip_index = lax.axis_index("space")
    source_valid = jnp.stack([span_index > 0, jnp.array(True)])
    offset_valid = jnp.stack(
        [strip_index > 0, jnp.array(True), strip_index < lax.axis_size("space") - 1]
    )
    visible = (pattern > 0) & source_valid[None, :, None, None] & offset_valid[None, None, :, None]
    visible = visible.reshape(frames, 6 * frames).astype(jnp.int32)
    near = [kv_list[i] for i in (2, 5, 6, 7)]
    far = [kv_list[i] for i in (0, 1, 3, 4)]
    carry = attention(visible, queries, near, frames, tile_size, last=False)
    attended = attention(visible, queries, far, frames, tile_size, carry)
    column_start = lax.axis_index("heads") * local_width
    projected = output_columns(attended, output_weight, local_width)
    gate_half = lax.dynamic_slice_in_dim(mod_table[2], column_start, local_width)
    own_rows = rows.astype(jnp.float32)
    updated = (own_rows + gate_half * projected).astype(jnp.bfloat16)
    return updated.reshape(latent.shape)


def solution(mesh):
    placed = (
        P(("groups", "tm"), "space", None, "heads"),
        P(None, "heads"),
        P(None, "heads"),
        P(None, "heads"),
        P("heads", None),
        P("heads"),
        P("heads"),
        P(),
        P(("groups", "tm")),
        P("space", None, None, None),
    )
    return jax.shard_map(
        shards,
        mesh=mesh,
        in_specs=placed,
        out_specs=P(("groups", "tm"), "space", None, "heads"),
        check_vma=False,
    )
```

```python
import functools
import math

import jax
import jax.numpy as jnp
from jax import lax
from jax.experimental import pallas as pl
from jax.experimental.pallas import tpu as pltpu
from jax.sharding import PartitionSpec as P

HD = 128


EPSILON = 1e-06


def from_behind(value, axis, steps):
    count = lax.axis_size(axis)
    first, last = (max(0, -steps), min(count, count - steps))
    return lax.ppermute(value, axis, [(source, source + steps) for source in range(first, last)])


def gather_heads(half):
    if lax.axis_size("heads") != 2:
        return lax.all_gather(half, "heads", axis=half.ndim - 1, tiled=True)
    me = lax.axis_index("heads")
    other = lax.ppermute(half, "heads", [(0, 1), (1, 0)])
    first = jnp.where(me == 0, half, other)
    second = jnp.where(me == 0, other, half)
    return jnp.concatenate([first, second], axis=-1)


def sum_heads(partial, local_width):
    if lax.axis_size("heads") != 2:
        return lax.psum_scatter(partial, "heads", scatter_dimension=1, tiled=True)
    me = lax.axis_index("heads")
    mine = lax.dynamic_slice_in_dim(partial, me * local_width, local_width, 1)
    theirs = lax.dynamic_slice_in_dim(partial, (1 - me) * local_width, local_width, 1)
    return mine + lax.ppermute(theirs, "heads", [(0, 1), (1, 0)])


def output_columns(attended, output_weight, local_width):
    if lax.axis_size("heads") != 2:
        partial = jnp.dot(attended, output_weight, preferred_element_type=jnp.float32)
        return sum_heads(partial, local_width)
    me = lax.axis_index("heads")
    swap = [(0, 1), (1, 0)]
    mine = lax.dynamic_slice_in_dim(output_weight, me * local_width, local_width, 1)
    theirs = lax.dynamic_slice_in_dim(output_weight, (1 - me) * local_width, local_width, 1)
    received = lax.ppermute(theirs, "heads", swap)
    other = lax.ppermute(attended, "heads", swap)
    return jnp.dot(attended, mine, preferred_element_type=jnp.float32) + jnp.dot(
        other, received, preferred_element_type=jnp.float32
    )


GROUP = 3


def attention_kernel(score_scale, n_tiles, has_in, has_out, order_ref, count_ref, q_ref, *refs):
    kv_ref = refs[0]
    carry_in = refs[1:4] if has_in else ()
    outs = refs[1 + len(carry_in) : -4]
    s_scr, m_scr, l_scr, acc_scr = refs[-4:]
    frame = pl.program_id(1)
    count = count_ref[frame]
    q = q_ref[...]
    groups = [list(range(i, min(i + GROUP, n_tiles))) for i in range(0, n_tiles, GROUP)]
    m_scr[...] = jnp.full(m_scr.shape, -jnp.inf, jnp.float32)
    for group in groups:

        @pl.when(count > group[0])
        def _():
            for n in group:
                s = (
                    lax.dot_general(
                        q, kv_ref[0, order_ref[frame, n]], (((1,), (1,)), ((), ())),
                        preferred_element_type=jnp.float32,
                    )
                    * score_scale
                )
                s = jnp.where(n < count, s, -jnp.inf)
                s_scr[n] = s
                m_scr[...] = jnp.maximum(m_scr[...], s)

    m = jnp.max(m_scr[...], axis=1, keepdims=True)
    if has_in:
        acc_in, m_in, l_in = carry_in
        m_prev = m_in[:, 0:1]
        m = jnp.maximum(m_prev, m)
        rescale = jnp.exp(m_prev - m)
        acc_scr[...] = acc_in[...] * rescale
    else:
        acc_scr[...] = jnp.zeros(acc_scr.shape, jnp.float32)
    l_scr[...] = jnp.zeros(l_scr.shape, jnp.float32)
    for group in groups:

        @pl.when(count > group[0])
        def _():
            for n in group:
                e = jnp.exp(s_scr[n] - m)
                l_scr[...] += e
                acc_scr[...] += jnp.dot(
                    e.astype(jnp.bfloat16), kv_ref[1, order_ref[frame, n]],
                    preferred_element_type=jnp.float32,
                )

    total = jnp.sum(l_scr[...], axis=1, keepdims=True)
    if has_in:
        total = l_in[:, 0:1] * rescale + total
    if has_out:
        acc_out, m_out, l_out = outs
        acc_out[...] = acc_scr[...]
        m_out[...] = jnp.broadcast_to(m, m_out.shape)
        l_out[...] = jnp.broadcast_to(total, l_out.shape)
    else:
        outs[0][...] = (acc_scr[...] / total).astype(outs[0].dtype)


def attention(visible, queries, kv_list, frames, tile_size, carry=None, last=True):
    local_width = queries.shape[1]
    heads = local_width // HD
    slots = [t for _, ids in kv_list for t in ids]
    n_tiles = len(slots)
    kv_all = jnp.concatenate([kv for kv, _ in kv_list], axis=1)
    seen = visible[:, jnp.array(slots, jnp.int32)]
    order = jnp.argsort(1 - seen, axis=1, stable=True).astype(jnp.int32)
    count = jnp.sum(seen, axis=1).astype(jnp.int32)
    has_in = carry is not None
    kernel = functools.partial(attention_kernel, 1.0 / math.sqrt(HD), n_tiles, has_in, not last)
    kv_spec = pl.BlockSpec((2, n_tiles, tile_size, HD), lambda h, f, o, c: (0, 0, 0, h))
    row_spec = pl.BlockSpec((tile_size, HD), lambda h, f, o, c: (f, h))
    row_f32 = jax.ShapeDtypeStruct(queries.shape, jnp.float32)
    if last:
        out_specs = row_spec
        out_shape = jax.ShapeDtypeStruct(queries.shape, jnp.bfloat16)
    else:
        out_specs = [row_spec] * 3
        out_shape = [row_f32] * 3
    carried = list(carry) if has_in else []
    grid_spec = pltpu.PrefetchScalarGridSpec(
        num_scalar_prefetch=2,
        grid=(heads, frames),
        in_specs=[row_spec, kv_spec] + [row_spec] * len(carried),
        out_specs=out_specs,
        scratch_shapes=[
            pltpu.VMEM((n_tiles, tile_size, tile_size), jnp.float32),
            pltpu.VMEM((tile_size, tile_size), jnp.float32),
            pltpu.VMEM((tile_size, tile_size), jnp.float32),
            pltpu.VMEM((tile_size, HD), jnp.float32),
        ],
    )
    tokens = queries.shape[0]
    cost = pl.CostEstimate(
        flops=4 * tokens * n_tiles * tile_size * local_width // 2,
        transcendentals=tokens * n_tiles * tile_size * heads // 2,
        bytes_accessed=(2 * n_tiles * tile_size + 4 * tokens) * local_width * 2,
    )
    return pl.pallas_call(
        kernel,
        grid_spec=grid_spec,
        out_shape=out_shape,
        cost_estimate=cost,
    )(order, count, queries, kv_all, *carried)


def shards(
    latent,
    query_weight,
    key_weight,
    value_weight,
    output_weight,
    query_gain,
    key_gain,
    modulation,
    noise_level,
    tile_pattern,
):
    frames, strip_rows, columns, local_width = latent.shape
    width = local_width * lax.axis_size("heads")
    token_count = frames * strip_rows * columns
    tile_size = strip_rows * columns
    levels = modulation.shape[0]
    rows = latent.reshape(token_count, local_width)
    whole = gather_heads(rows)
    onehot = (noise_level[0] == jnp.arange(levels, dtype=jnp.int32)).astype(jnp.float32)
    mod_table = jnp.dot(
        onehot[None, :], modulation.reshape(levels, 3 * width), precision=lax.Precision.HIGHEST
    ).reshape(3, width)
    token_rows = whole.astype(jnp.float32)
    center = token_rows - jnp.mean(token_rows, axis=1, keepdims=True)
    normed = center * lax.rsqrt(jnp.mean(center * center, axis=1, keepdims=True) + EPSILON)
    hidden = (normed * (1.0 + mod_table[1]) + mod_table[0]).astype(jnp.bfloat16)
    query_raw = jnp.dot(hidden, query_weight, preferred_element_type=jnp.float32)
    key_raw = jnp.dot(hidden, key_weight, preferred_element_type=jnp.float32)
    value_rows = jnp.dot(hidden, value_weight, preferred_element_type=jnp.float32).astype(
        jnp.bfloat16
    )
    squares = lax.psum(
        (jnp.sum(query_raw * query_raw, axis=1), jnp.sum(key_raw * key_raw, axis=1)), "heads"
    )
    queries = (query_raw * lax.rsqrt(squares[0] / width + EPSILON)[:, None] * query_gain).astype(
        jnp.bfloat16
    )
    key_rows = (key_raw * lax.rsqrt(squares[1] / width + EPSILON)[:, None] * key_gain).astype(
        jnp.bfloat16
    )
    kv = jnp.stack(
        [
            key_rows.reshape(frames, tile_size, local_width),
            value_rows.reshape(frames, tile_size, local_width),
        ]
    )
    own_low = from_behind(kv, "space", 1)
    own_high = from_behind(kv, "space", -1)
    prior_mid = from_behind(kv, "tm", 1)
    split = frames - frames // 3
    low_far = from_behind(prior_mid[:, :split], "space", 1)
    high_far = from_behind(prior_mid[:, :split], "space", -1)
    low_near = from_behind(own_low[:, split:], "tm", 1)
    high_near = from_behind(own_high[:, split:], "tm", 1)
    fr = list(range(frames))
    kv_list = [
        (low_far, [0 * frames + f for f in fr[:split]]),
        (low_near, [0 * frames + f for f in fr[split:]]),
        (prior_mid, [1 * frames + f for f in fr]),
        (high_far, [2 * frames + f for f in fr[:split]]),
        (high_near, [2 * frames + f for f in fr[split:]]),
        (own_low, [3 * frames + f for f in fr]),
        (kv, [4 * frames + f for f in fr]),
        (own_high, [5 * frames + f for f in fr]),
    ]
    pattern = jnp.transpose(tile_pattern[0].reshape(frames, 2, frames, 3), (0, 1, 3, 2))
    span_index = lax.axis_index("tm")
    strip_index = lax.axis_index("space")
    source_valid = jnp.stack([span_index > 0, jnp.array(True)])
    offset_valid = jnp.stack(
        [strip_index > 0, jnp.array(True), strip_index < lax.axis_size("space") - 1]
    )
    visible = (pattern > 0) & source_valid[None, :, None, None] & offset_valid[None, None, :, None]
    visible = visible.reshape(frames, 6 * frames).astype(jnp.int32)
    near = [kv_list[i] for i in (2, 5, 6, 7)]
    far = [kv_list[i] for i in (0, 1, 3, 4)]
    carry = attention(visible, queries, near, frames, tile_size, last=False)
    attended = attention(visible, queries, far, frames, tile_size, carry)
    column_start = lax.axis_index("heads") * local_width
    projected = output_columns(attended, output_weight, local_width)
    gate_half = lax.dynamic_slice_in_dim(mod_table[2], column_start, local_width)
    own_rows = rows.astype(jnp.float32)
    updated = (own_rows + gate_half * projected).astype(jnp.bfloat16)
    return updated.reshape(latent.shape)


def solution(mesh):
    placed = (
        P(("groups", "tm"), "space", None, "heads"),
        P(None, "heads"),
        P(None, "heads"),
        P(None, "heads"),
        P("heads", None),
        P("heads"),
        P("heads"),
        P(),
        P(("groups", "tm")),
        P("space", None, None, None),
    )
    return jax.shard_map(
        shards,
        mesh=mesh,
        in_specs=placed,
        out_specs=P(("groups", "tm"), "space", None, "heads"),
        check_vma=False,
    )
```

```python
import functools
import math

import jax
import jax.numpy as jnp
from jax import lax
from jax.experimental import pallas as pl
from jax.experimental.pallas import tpu as pltpu
from jax.sharding import PartitionSpec as P

HD = 128


EPSILON = 1e-06


def from_behind(value, axis, steps):
    count = lax.axis_size(axis)
    first, last = (max(0, -steps), min(count, count - steps))
    return lax.ppermute(value, axis, [(source, source + steps) for source in range(first, last)])


def gather_heads(half):
    if lax.axis_size("heads") != 2:
        return lax.all_gather(half, "heads", axis=half.ndim - 1, tiled=True)
    me = lax.axis_index("heads")
    other = lax.ppermute(half, "heads", [(0, 1), (1, 0)])
    first = jnp.where(me == 0, half, other)
    second = jnp.where(me == 0, other, half)
    return jnp.concatenate([first, second], axis=-1)


def sum_heads(partial, local_width):
    if lax.axis_size("heads") != 2:
        return lax.psum_scatter(partial, "heads", scatter_dimension=1, tiled=True)
    me = lax.axis_index("heads")
    mine = lax.dynamic_slice_in_dim(partial, me * local_width, local_width, 1)
    theirs = lax.dynamic_slice_in_dim(partial, (1 - me) * local_width, local_width, 1)
    return mine + lax.ppermute(theirs, "heads", [(0, 1), (1, 0)])


def output_columns(attended, output_weight, local_width):
    if lax.axis_size("heads") != 2:
        partial = jnp.dot(attended, output_weight, preferred_element_type=jnp.float32)
        return sum_heads(partial, local_width)
    me = lax.axis_index("heads")
    swap = [(0, 1), (1, 0)]
    mine = lax.dynamic_slice_in_dim(output_weight, me * local_width, local_width, 1)
    theirs = lax.dynamic_slice_in_dim(output_weight, (1 - me) * local_width, local_width, 1)
    received = lax.ppermute(theirs, "heads", swap)
    other = lax.ppermute(attended, "heads", swap)
    return jnp.dot(attended, mine, preferred_element_type=jnp.float32) + jnp.dot(
        other, received, preferred_element_type=jnp.float32
    )


GROUP = 3


def attention_kernel(score_scale, n_tiles, has_in, has_out, order_ref, count_ref, q_ref, *refs):
    kv_ref = refs[0]
    carry_in = refs[1:4] if has_in else ()
    outs = refs[1 + len(carry_in) : -4]
    s_scr, m_scr, l_scr, acc_scr = refs[-4:]
    frame = pl.program_id(1)
    count = count_ref[frame]
    q = q_ref[...]
    groups = [list(range(i, min(i + GROUP, n_tiles))) for i in range(0, n_tiles, GROUP)]
    m_scr[...] = jnp.full(m_scr.shape, -jnp.inf, jnp.float32)
    for group in groups:

        @pl.when(count > group[0])
        def _():
            for n in group:
                s = (
                    lax.dot_general(
                        q, kv_ref[0, order_ref[frame, n]], (((1,), (1,)), ((), ())),
                        preferred_element_type=jnp.float32,
                    )
                    * score_scale
                )
                s = jnp.where(n < count, s, -jnp.inf)
                s_scr[n] = s
                m_scr[...] = jnp.maximum(m_scr[...], s)

    m = jnp.max(m_scr[...], axis=1, keepdims=True)
    if has_in:
        acc_in, m_in, l_in = carry_in
        m_prev = m_in[:, 0:1]
        m = jnp.maximum(m_prev, m)
        rescale = jnp.exp(m_prev - m)
        acc_scr[...] = acc_in[...] * rescale
    else:
        acc_scr[...] = jnp.zeros(acc_scr.shape, jnp.float32)
    l_scr[...] = jnp.zeros(l_scr.shape, jnp.float32)
    for group in groups:

        @pl.when(count > group[0])
        def _():
            for n in group:
                e = jnp.exp(s_scr[n] - m)
                l_scr[...] += e
                acc_scr[...] += jnp.dot(
                    e.astype(jnp.bfloat16), kv_ref[1, order_ref[frame, n]],
                    preferred_element_type=jnp.float32,
                )

    total = jnp.sum(l_scr[...], axis=1, keepdims=True)
    if has_in:
        total = l_in[:, 0:1] * rescale + total
    if has_out:
        acc_out, m_out, l_out = outs
        acc_out[...] = acc_scr[...]
        m_out[...] = jnp.broadcast_to(m, m_out.shape)
        l_out[...] = jnp.broadcast_to(total, l_out.shape)
    else:
        outs[0][...] = (acc_scr[...] / total).astype(outs[0].dtype)


def attention(visible, queries, kv_list, frames, tile_size, carry=None, last=True):
    local_width = queries.shape[1]
    heads = local_width // HD
    slots = [t for _, ids in kv_list for t in ids]
    n_tiles = len(slots)
    kv_all = jnp.concatenate([kv for kv, _ in kv_list], axis=1)
    seen = visible[:, jnp.array(slots, jnp.int32)]
    order = jnp.argsort(1 - seen, axis=1, stable=True).astype(jnp.int32)
    count = jnp.sum(seen, axis=1).astype(jnp.int32)
    has_in = carry is not None
    kernel = functools.partial(attention_kernel, 1.0 / math.sqrt(HD), n_tiles, has_in, not last)
    kv_spec = pl.BlockSpec((2, n_tiles, tile_size, HD), lambda h, f, o, c: (0, 0, 0, h))
    row_spec = pl.BlockSpec((tile_size, HD), lambda h, f, o, c: (f, h))
    row_f32 = jax.ShapeDtypeStruct(queries.shape, jnp.float32)
    if last:
        out_specs = row_spec
        out_shape = jax.ShapeDtypeStruct(queries.shape, jnp.bfloat16)
    else:
        out_specs = [row_spec] * 3
        out_shape = [row_f32] * 3
    carried = list(carry) if has_in else []
    grid_spec = pltpu.PrefetchScalarGridSpec(
        num_scalar_prefetch=2,
        grid=(heads, frames),
        in_specs=[row_spec, kv_spec] + [row_spec] * len(carried),
        out_specs=out_specs,
        scratch_shapes=[
            pltpu.VMEM((n_tiles, tile_size, tile_size), jnp.float32),
            pltpu.VMEM((tile_size, tile_size), jnp.float32),
            pltpu.VMEM((tile_size, tile_size), jnp.float32),
            pltpu.VMEM((tile_size, HD), jnp.float32),
        ],
    )
    tokens = queries.shape[0]
    cost = pl.CostEstimate(
        flops=4 * tokens * n_tiles * tile_size * local_width // 2,
        transcendentals=tokens * n_tiles * tile_size * heads // 2,
        bytes_accessed=(2 * n_tiles * tile_size + 4 * tokens) * local_width * 2,
    )
    return pl.pallas_call(
        kernel,
        grid_spec=grid_spec,
        out_shape=out_shape,
        cost_estimate=cost,
    )(order, count, queries, kv_all, *carried)


def shards(
    latent,
    query_weight,
    key_weight,
    value_weight,
    output_weight,
    query_gain,
    key_gain,
    modulation,
    noise_level,
    tile_pattern,
):
    frames, strip_rows, columns, local_width = latent.shape
    width = local_width * lax.axis_size("heads")
    token_count = frames * strip_rows * columns
    tile_size = strip_rows * columns
    levels = modulation.shape[0]
    rows = latent.reshape(token_count, local_width)
    whole = gather_heads(rows)
    onehot = (noise_level[0] == jnp.arange(levels, dtype=jnp.int32)).astype(jnp.float32)
    mod_table = jnp.dot(
        onehot[None, :], modulation.reshape(levels, 3 * width), precision=lax.Precision.HIGHEST
    ).reshape(3, width)
    token_rows = whole.astype(jnp.float32)
    center = token_rows - jnp.mean(token_rows, axis=1, keepdims=True)
    normed = center * lax.rsqrt(jnp.mean(center * center, axis=1, keepdims=True) + EPSILON)
    hidden = (normed * (1.0 + mod_table[1]) + mod_table[0]).astype(jnp.bfloat16)
    query_raw = jnp.dot(hidden, query_weight, preferred_element_type=jnp.float32)
    key_raw = jnp.dot(hidden, key_weight, preferred_element_type=jnp.float32)
    value_rows = jnp.dot(hidden, value_weight, preferred_element_type=jnp.float32).astype(
        jnp.bfloat16
    )
    key_squares = lax.psum(jnp.sum(key_raw * key_raw, axis=1), "heads")
    query_squares = jnp.sum(query_raw * query_raw, axis=1)
    if lax.axis_size("heads") == 2:
        query_squares = query_squares + lax.ppermute(query_squares, "heads", [(0, 1), (1, 0)])
    else:
        query_squares = lax.psum(query_squares, "heads")
    queries = (query_raw * lax.rsqrt(query_squares / width + EPSILON)[:, None] * query_gain).astype(
        jnp.bfloat16
    )
    key_rows = (key_raw * lax.rsqrt(key_squares / width + EPSILON)[:, None] * key_gain).astype(
        jnp.bfloat16
    )
    kv = jnp.stack(
        [
            key_rows.reshape(frames, tile_size, local_width),
            value_rows.reshape(frames, tile_size, local_width),
        ]
    )
    own_low = from_behind(kv, "space", 1)
    own_high = from_behind(kv, "space", -1)
    prior_mid = from_behind(kv, "tm", 1)
    split = frames - frames // 3
    low_far = from_behind(prior_mid[:, :split], "space", 1)
    high_far = from_behind(prior_mid[:, :split], "space", -1)
    low_near = from_behind(own_low[:, split:], "tm", 1)
    high_near = from_behind(own_high[:, split:], "tm", 1)
    fr = list(range(frames))
    kv_list = [
        (low_far, [0 * frames + f for f in fr[:split]]),
        (low_near, [0 * frames + f for f in fr[split:]]),
        (prior_mid, [1 * frames + f for f in fr]),
        (high_far, [2 * frames + f for f in fr[:split]]),
        (high_near, [2 * frames + f for f in fr[split:]]),
        (own_low, [3 * frames + f for f in fr]),
        (kv, [4 * frames + f for f in fr]),
        (own_high, [5 * frames + f for f in fr]),
    ]
    pattern = jnp.transpose(tile_pattern[0].reshape(frames, 2, frames, 3), (0, 1, 3, 2))
    span_index = lax.axis_index("tm")
    strip_index = lax.axis_index("space")
    source_valid = jnp.stack([span_index > 0, jnp.array(True)])
    offset_valid = jnp.stack(
        [strip_index > 0, jnp.array(True), strip_index < lax.axis_size("space") - 1]
    )
    visible = (pattern > 0) & source_valid[None, :, None, None] & offset_valid[None, None, :, None]
    visible = visible.reshape(frames, 6 * frames).astype(jnp.int32)
    near = [kv_list[i] for i in (2, 5, 6, 7)]
    far = [kv_list[i] for i in (0, 1, 3, 4)]
    carry = attention(visible, queries, near, frames, tile_size, last=False)
    attended = attention(visible, queries, far, frames, tile_size, carry)
    column_start = lax.axis_index("heads") * local_width
    projected = output_columns(attended, output_weight, local_width)
    gate_half = lax.dynamic_slice_in_dim(mod_table[2], column_start, local_width)
    own_rows = rows.astype(jnp.float32)
    updated = (own_rows + gate_half * projected).astype(jnp.bfloat16)
    return updated.reshape(latent.shape)


def solution(mesh):
    placed = (
        P(("groups", "tm"), "space", None, "heads"),
        P(None, "heads"),
        P(None, "heads"),
        P(None, "heads"),
        P("heads", None),
        P("heads"),
        P("heads"),
        P(),
        P(("groups", "tm")),
        P("space", None, None, None),
    )
    return jax.shard_map(
        shards,
        mesh=mesh,
        in_specs=placed,
        out_specs=P(("groups", "tm"), "space", None, "heads"),
        check_vma=False,
    )
```

```python
import functools
import math

import jax
import jax.numpy as jnp
from jax import lax
from jax.experimental import pallas as pl
from jax.experimental.pallas import tpu as pltpu
from jax.sharding import PartitionSpec as P

HD = 128


EPSILON = 1e-06


def from_behind(value, axis, steps):
    count = lax.axis_size(axis)
    first, last = (max(0, -steps), min(count, count - steps))
    return lax.ppermute(value, axis, [(source, source + steps) for source in range(first, last)])


def gather_heads(half):
    if lax.axis_size("heads") != 2:
        return lax.all_gather(half, "heads", axis=half.ndim - 1, tiled=True)
    me = lax.axis_index("heads")
    other = lax.ppermute(half, "heads", [(0, 1), (1, 0)])
    first = jnp.where(me == 0, half, other)
    second = jnp.where(me == 0, other, half)
    return jnp.concatenate([first, second], axis=-1)


def sum_heads(partial, local_width):
    if lax.axis_size("heads") != 2:
        return lax.psum_scatter(partial, "heads", scatter_dimension=1, tiled=True)
    me = lax.axis_index("heads")
    mine = lax.dynamic_slice_in_dim(partial, me * local_width, local_width, 1)
    theirs = lax.dynamic_slice_in_dim(partial, (1 - me) * local_width, local_width, 1)
    return mine + lax.ppermute(theirs, "heads", [(0, 1), (1, 0)])


def output_columns(attended, output_weight, local_width):
    if lax.axis_size("heads") != 2:
        partial = jnp.dot(attended, output_weight, preferred_element_type=jnp.float32)
        return sum_heads(partial, local_width)
    me = lax.axis_index("heads")
    swap = [(0, 1), (1, 0)]
    mine = lax.dynamic_slice_in_dim(output_weight, me * local_width, local_width, 1)
    theirs = lax.dynamic_slice_in_dim(output_weight, (1 - me) * local_width, local_width, 1)
    received = lax.ppermute(theirs, "heads", swap)
    other = lax.ppermute(attended, "heads", swap)
    return jnp.dot(attended, mine, preferred_element_type=jnp.float32) + jnp.dot(
        other, received, preferred_element_type=jnp.float32
    )


GROUP = 3


def attention_kernel(score_scale, n_tiles, has_in, has_out, order_ref, count_ref, q_ref, *refs):
    kv_ref = refs[0]
    carry_in = refs[1:4] if has_in else ()
    outs = refs[1 + len(carry_in) : -4]
    s_scr, m_scr, l_scr, acc_scr = refs[-4:]
    frame = pl.program_id(1)
    count = count_ref[frame]
    q = q_ref[...]
    groups = [list(range(i, min(i + GROUP, n_tiles))) for i in range(0, n_tiles, GROUP)]
    m_scr[...] = jnp.full(m_scr.shape, -jnp.inf, jnp.float32)
    for group in groups:

        @pl.when(count > group[0])
        def _():
            for n in group:
                s = (
                    lax.dot_general(
                        q, kv_ref[0, order_ref[frame, n]], (((1,), (1,)), ((), ())),
                        preferred_element_type=jnp.float32,
                    )
                    * score_scale
                )
                s = jnp.where(n < count, s, -jnp.inf)
                s_scr[n] = s
                m_scr[...] = jnp.maximum(m_scr[...], s)

    m = jnp.max(m_scr[...], axis=1, keepdims=True)
    if has_in:
        acc_in, m_in, l_in = carry_in
        m_prev = m_in[:, 0:1]
        m = jnp.maximum(m_prev, m)
        rescale = jnp.exp(m_prev - m)
        acc_scr[...] = acc_in[...] * rescale
    else:
        acc_scr[...] = jnp.zeros(acc_scr.shape, jnp.float32)
    l_scr[...] = jnp.zeros(l_scr.shape, jnp.float32)
    for group in groups:

        @pl.when(count > group[0])
        def _():
            for n in group:
                e = jnp.exp(s_scr[n] - m)
                l_scr[...] += e
                acc_scr[...] += jnp.dot(
                    e.astype(jnp.bfloat16), kv_ref[1, order_ref[frame, n]],
                    preferred_element_type=jnp.float32,
                )

    total = jnp.sum(l_scr[...], axis=1, keepdims=True)
    if has_in:
        total = l_in[:, 0:1] * rescale + total
    if has_out:
        acc_out, m_out, l_out = outs
        acc_out[...] = acc_scr[...]
        m_out[...] = jnp.broadcast_to(m, m_out.shape)
        l_out[...] = jnp.broadcast_to(total, l_out.shape)
    else:
        outs[0][...] = (acc_scr[...] / total).astype(outs[0].dtype)


def attention(visible, queries, kv_list, frames, tile_size, carry=None, last=True):
    local_width = queries.shape[1]
    heads = local_width // HD
    slots = [t for _, ids in kv_list for t in ids]
    n_tiles = len(slots)
    kv_all = jnp.concatenate([kv for kv, _ in kv_list], axis=1)
    seen = visible[:, jnp.array(slots, jnp.int32)]
    order = jnp.argsort(1 - seen, axis=1, stable=True).astype(jnp.int32)
    count = jnp.sum(seen, axis=1).astype(jnp.int32)
    has_in = carry is not None
    kernel = functools.partial(attention_kernel, 1.0 / math.sqrt(HD), n_tiles, has_in, not last)
    kv_spec = pl.BlockSpec((2, n_tiles, tile_size, HD), lambda h, f, o, c: (0, 0, 0, h))
    row_spec = pl.BlockSpec((tile_size, HD), lambda h, f, o, c: (f, h))
    row_f32 = jax.ShapeDtypeStruct(queries.shape, jnp.float32)
    if last:
        out_specs = row_spec
        out_shape = jax.ShapeDtypeStruct(queries.shape, jnp.bfloat16)
    else:
        out_specs = [row_spec] * 3
        out_shape = [row_f32] * 3
    carried = list(carry) if has_in else []
    grid_spec = pltpu.PrefetchScalarGridSpec(
        num_scalar_prefetch=2,
        grid=(heads, frames),
        in_specs=[row_spec, kv_spec] + [row_spec] * len(carried),
        out_specs=out_specs,
        scratch_shapes=[
            pltpu.VMEM((n_tiles, tile_size, tile_size), jnp.float32),
            pltpu.VMEM((tile_size, tile_size), jnp.float32),
            pltpu.VMEM((tile_size, tile_size), jnp.float32),
            pltpu.VMEM((tile_size, HD), jnp.float32),
        ],
    )
    tokens = queries.shape[0]
    cost = pl.CostEstimate(
        flops=4 * tokens * n_tiles * tile_size * local_width // 2,
        transcendentals=tokens * n_tiles * tile_size * heads // 2,
        bytes_accessed=(2 * n_tiles * tile_size + 4 * tokens) * local_width * 2,
    )
    return pl.pallas_call(
        kernel,
        grid_spec=grid_spec,
        out_shape=out_shape,
        cost_estimate=cost,
    )(order, count, queries, kv_all, *carried)


def shards(
    latent,
    query_weight,
    key_weight,
    value_weight,
    output_weight,
    query_gain,
    key_gain,
    modulation,
    noise_level,
    tile_pattern,
):
    frames, strip_rows, columns, local_width = latent.shape
    width = local_width * lax.axis_size("heads")
    token_count = frames * strip_rows * columns
    tile_size = strip_rows * columns
    levels = modulation.shape[0]
    rows = latent.reshape(token_count, local_width)
    whole = gather_heads(rows)
    onehot = (noise_level[0] == jnp.arange(levels, dtype=jnp.int32)).astype(jnp.float32)
    mod_table = jnp.dot(
        onehot[None, :], modulation.reshape(levels, 3 * width), precision=lax.Precision.HIGHEST
    ).reshape(3, width)
    token_rows = whole.astype(jnp.float32)
    center = token_rows - jnp.mean(token_rows, axis=1, keepdims=True)
    normed = center * lax.rsqrt(jnp.mean(center * center, axis=1, keepdims=True) + EPSILON)
    hidden = (normed * (1.0 + mod_table[1]) + mod_table[0]).astype(jnp.bfloat16)
    query_raw = jnp.dot(hidden, query_weight, preferred_element_type=jnp.float32)
    key_raw = jnp.dot(hidden, key_weight, preferred_element_type=jnp.float32)
    value_rows = jnp.dot(hidden, value_weight, preferred_element_type=jnp.float32).astype(
        jnp.bfloat16
    )
    key_squares = lax.psum(jnp.sum(key_raw * key_raw, axis=1), "heads")
    query_squares = jnp.sum(query_raw * query_raw, axis=1)
    if lax.axis_size("heads") == 2:
        query_squares = query_squares + lax.ppermute(query_squares, "heads", [(0, 1), (1, 0)])
    else:
        query_squares = lax.psum(query_squares, "heads")
    queries = (query_raw * lax.rsqrt(query_squares / width + EPSILON)[:, None] * query_gain).astype(
        jnp.bfloat16
    )
    key_rows = (key_raw * lax.rsqrt(key_squares / width + EPSILON)[:, None] * key_gain).astype(
        jnp.bfloat16
    )
    kv = jnp.stack(
        [
            key_rows.reshape(frames, tile_size, local_width),
            value_rows.reshape(frames, tile_size, local_width),
        ]
    )
    pattern = jnp.transpose(tile_pattern[0].reshape(frames, 2, frames, 3), (0, 1, 3, 2))
    span_index = lax.axis_index("tm")
    strip_index = lax.axis_index("space")
    source_valid = jnp.stack([span_index > 0, jnp.array(True)])
    offset_valid = jnp.stack(
        [strip_index > 0, jnp.array(True), strip_index < lax.axis_size("space") - 1]
    )
    visible = (pattern > 0) & source_valid[None, :, None, None] & offset_valid[None, None, :, None]
    visible = visible.reshape(frames, 6 * frames).astype(jnp.int32)
    fr = list(range(frames))

    def ids(slot, part):
        return [slot * frames + f for f in part]

    own_low = from_behind(kv, "space", 1)
    own_high = from_behind(kv, "space", -1)
    prior_mid = from_behind(kv, "tm", 1)
    carry = attention(visible, queries, [(kv, ids(4, fr))], frames, tile_size, last=False)
    carry, own_low, own_high, prior_mid = lax.optimization_barrier(
        (carry, own_low, own_high, prior_mid)
    )
    split = frames - frames // 3
    low_far = from_behind(prior_mid[:, :split], "space", 1)
    high_far = from_behind(prior_mid[:, :split], "space", -1)
    low_near = from_behind(own_low[:, split:], "tm", 1)
    high_near = from_behind(own_high[:, split:], "tm", 1)
    near = [(prior_mid, ids(1, fr)), (own_low, ids(3, fr)), (own_high, ids(5, fr))]
    far = [
        (low_far, ids(0, fr[:split])),
        (low_near, ids(0, fr[split:])),
        (high_far, ids(2, fr[:split])),
        (high_near, ids(2, fr[split:])),
    ]
    carry = attention(visible, queries, near, frames, tile_size, carry, last=False)
    attended = attention(visible, queries, far, frames, tile_size, carry)
    column_start = lax.axis_index("heads") * local_width
    projected = output_columns(attended, output_weight, local_width)
    gate_half = lax.dynamic_slice_in_dim(mod_table[2], column_start, local_width)
    own_rows = rows.astype(jnp.float32)
    updated = (own_rows + gate_half * projected).astype(jnp.bfloat16)
    return updated.reshape(latent.shape)


def solution(mesh):
    placed = (
        P(("groups", "tm"), "space", None, "heads"),
        P(None, "heads"),
        P(None, "heads"),
        P(None, "heads"),
        P("heads", None),
        P("heads"),
        P("heads"),
        P(),
        P(("groups", "tm")),
        P("space", None, None, None),
    )
    return jax.shard_map(
        shards,
        mesh=mesh,
        in_specs=placed,
        out_specs=P(("groups", "tm"), "space", None, "heads"),
        check_vma=False,
    )
```

```python
import functools
import math

import jax
import jax.numpy as jnp
from jax import lax
from jax.experimental import pallas as pl
from jax.experimental.pallas import tpu as pltpu
from jax.sharding import PartitionSpec as P

HD = 128


EPSILON = 1e-06


def from_behind(value, axis, steps):
    count = lax.axis_size(axis)
    first, last = (max(0, -steps), min(count, count - steps))
    return lax.ppermute(value, axis, [(source, source + steps) for source in range(first, last)])


def gather_heads(half):
    if lax.axis_size("heads") != 2:
        return lax.all_gather(half, "heads", axis=half.ndim - 1, tiled=True)
    me = lax.axis_index("heads")
    other = lax.ppermute(half, "heads", [(0, 1), (1, 0)])
    first = jnp.where(me == 0, half, other)
    second = jnp.where(me == 0, other, half)
    return jnp.concatenate([first, second], axis=-1)


def sum_heads(partial, local_width):
    if lax.axis_size("heads") != 2:
        return lax.psum_scatter(partial, "heads", scatter_dimension=1, tiled=True)
    me = lax.axis_index("heads")
    mine = lax.dynamic_slice_in_dim(partial, me * local_width, local_width, 1)
    theirs = lax.dynamic_slice_in_dim(partial, (1 - me) * local_width, local_width, 1)
    return mine + lax.ppermute(theirs, "heads", [(0, 1), (1, 0)])


def output_columns(attended, output_weight, local_width):
    if lax.axis_size("heads") != 2:
        partial = jnp.dot(attended, output_weight, preferred_element_type=jnp.float32)
        return sum_heads(partial, local_width)
    me = lax.axis_index("heads")
    swap = [(0, 1), (1, 0)]
    mine = lax.dynamic_slice_in_dim(output_weight, me * local_width, local_width, 1)
    theirs = lax.dynamic_slice_in_dim(output_weight, (1 - me) * local_width, local_width, 1)
    received = lax.ppermute(theirs, "heads", swap)
    other = lax.ppermute(attended, "heads", swap)
    return jnp.dot(attended, mine, preferred_element_type=jnp.float32) + jnp.dot(
        other, received, preferred_element_type=jnp.float32
    )


GROUP = 3


def attention_kernel(score_scale, n_tiles, has_in, has_out, order_ref, count_ref, q_ref, *refs):
    kv_ref = refs[0]
    carry_in = refs[1:4] if has_in else ()
    outs = refs[1 + len(carry_in) : -4]
    s_scr, m_scr, l_scr, acc_scr = refs[-4:]
    frame = pl.program_id(1)
    count = count_ref[frame]
    q = q_ref[...]
    groups = [list(range(i, min(i + GROUP, n_tiles))) for i in range(0, n_tiles, GROUP)]
    m_scr[...] = jnp.full(m_scr.shape, -jnp.inf, jnp.float32)
    for group in groups:

        @pl.when(count > group[0])
        def _():
            for n in group:
                s = (
                    lax.dot_general(
                        q, kv_ref[order_ref[frame, n], 0], (((1,), (1,)), ((), ())),
                        preferred_element_type=jnp.float32,
                    )
                    * score_scale
                )
                s = jnp.where(n < count, s, -jnp.inf)
                s_scr[n] = s
                m_scr[...] = jnp.maximum(m_scr[...], s)

    m = jnp.max(m_scr[...], axis=1, keepdims=True)
    if has_in:
        acc_in, m_in, l_in = carry_in
        m_prev = m_in[:, 0:1]
        m = jnp.maximum(m_prev, m)
        rescale = jnp.exp(m_prev - m)
        acc_scr[...] = acc_in[...] * rescale
    else:
        acc_scr[...] = jnp.zeros(acc_scr.shape, jnp.float32)
    l_scr[...] = jnp.zeros(l_scr.shape, jnp.float32)
    for group in groups:

        @pl.when(count > group[0])
        def _():
            for n in group:
                e = jnp.exp(s_scr[n] - m)
                l_scr[...] += e
                acc_scr[...] += jnp.dot(
                    e.astype(jnp.bfloat16), kv_ref[order_ref[frame, n], 1],
                    preferred_element_type=jnp.float32,
                )

    total = jnp.sum(l_scr[...], axis=1, keepdims=True)
    if has_in:
        total = l_in[:, 0:1] * rescale + total
    if has_out:
        acc_out, m_out, l_out = outs
        acc_out[...] = acc_scr[...]
        m_out[...] = jnp.broadcast_to(m, m_out.shape)
        l_out[...] = jnp.broadcast_to(total, l_out.shape)
    else:
        outs[0][...] = (acc_scr[...] / total).astype(outs[0].dtype)


def attention(visible, queries, kv_list, frames, tile_size, carry=None, last=True):
    local_width = queries.shape[1]
    heads = local_width // HD
    slots = [t for _, ids in kv_list for t in ids]
    n_tiles = len(slots)
    kv_all = jnp.concatenate([kv for kv, _ in kv_list], axis=0)
    seen = visible[:, jnp.array(slots, jnp.int32)]
    order = jnp.argsort(1 - seen, axis=1, stable=True).astype(jnp.int32)
    count = jnp.sum(seen, axis=1).astype(jnp.int32)
    has_in = carry is not None
    kernel = functools.partial(attention_kernel, 1.0 / math.sqrt(HD), n_tiles, has_in, not last)
    kv_spec = pl.BlockSpec((n_tiles, 2, tile_size, HD), lambda h, f, o, c: (0, 0, 0, h))
    row_spec = pl.BlockSpec((tile_size, HD), lambda h, f, o, c: (f, h))
    row_f32 = jax.ShapeDtypeStruct(queries.shape, jnp.float32)
    if last:
        out_specs = row_spec
        out_shape = jax.ShapeDtypeStruct(queries.shape, jnp.bfloat16)
    else:
        out_specs = [row_spec] * 3
        out_shape = [row_f32] * 3
    carried = list(carry) if has_in else []
    grid_spec = pltpu.PrefetchScalarGridSpec(
        num_scalar_prefetch=2,
        grid=(heads, frames),
        in_specs=[row_spec, kv_spec] + [row_spec] * len(carried),
        out_specs=out_specs,
        scratch_shapes=[
            pltpu.VMEM((n_tiles, tile_size, tile_size), jnp.float32),
            pltpu.VMEM((tile_size, tile_size), jnp.float32),
            pltpu.VMEM((tile_size, tile_size), jnp.float32),
            pltpu.VMEM((tile_size, HD), jnp.float32),
        ],
    )
    tokens = queries.shape[0]
    cost = pl.CostEstimate(
        flops=4 * tokens * n_tiles * tile_size * local_width // 2,
        transcendentals=tokens * n_tiles * tile_size * heads // 2,
        bytes_accessed=(2 * n_tiles * tile_size + 4 * tokens) * local_width * 2,
    )
    return pl.pallas_call(
        kernel,
        grid_spec=grid_spec,
        out_shape=out_shape,
        cost_estimate=cost,
    )(order, count, queries, kv_all, *carried)


def shards(
    latent,
    query_weight,
    key_weight,
    value_weight,
    output_weight,
    query_gain,
    key_gain,
    modulation,
    noise_level,
    tile_pattern,
):
    frames, strip_rows, columns, local_width = latent.shape
    width = local_width * lax.axis_size("heads")
    token_count = frames * strip_rows * columns
    tile_size = strip_rows * columns
    levels = modulation.shape[0]
    rows = latent.reshape(token_count, local_width)
    whole = gather_heads(rows)
    onehot = (noise_level[0] == jnp.arange(levels, dtype=jnp.int32)).astype(jnp.float32)
    mod_table = jnp.dot(
        onehot[None, :], modulation.reshape(levels, 3 * width), precision=lax.Precision.HIGHEST
    ).reshape(3, width)
    token_rows = whole.astype(jnp.float32)
    center = token_rows - jnp.mean(token_rows, axis=1, keepdims=True)
    normed = center * lax.rsqrt(jnp.mean(center * center, axis=1, keepdims=True) + EPSILON)
    hidden = (normed * (1.0 + mod_table[1]) + mod_table[0]).astype(jnp.bfloat16)
    query_raw = jnp.dot(hidden, query_weight, preferred_element_type=jnp.float32)
    key_raw = jnp.dot(hidden, key_weight, preferred_element_type=jnp.float32)
    value_rows = jnp.dot(hidden, value_weight, preferred_element_type=jnp.float32).astype(
        jnp.bfloat16
    )
    key_squares = lax.psum(jnp.sum(key_raw * key_raw, axis=1), "heads")
    query_squares = jnp.sum(query_raw * query_raw, axis=1)
    if lax.axis_size("heads") == 2:
        query_squares = query_squares + lax.ppermute(query_squares, "heads", [(0, 1), (1, 0)])
    else:
        query_squares = lax.psum(query_squares, "heads")
    queries = (query_raw * lax.rsqrt(query_squares / width + EPSILON)[:, None] * query_gain).astype(
        jnp.bfloat16
    )
    key_rows = (key_raw * lax.rsqrt(key_squares / width + EPSILON)[:, None] * key_gain).astype(
        jnp.bfloat16
    )
    kv = jnp.stack(
        [
            key_rows.reshape(frames, tile_size, local_width),
            value_rows.reshape(frames, tile_size, local_width),
        ],
        axis=1,
    )
    own_low = from_behind(kv, "space", 1)
    own_high = from_behind(kv, "space", -1)
    prior_mid = from_behind(kv, "tm", 1)
    split = frames - frames // 3
    low_far = from_behind(prior_mid[:split], "space", 1)
    high_far = from_behind(prior_mid[:split], "space", -1)
    low_near = from_behind(own_low[split:], "tm", 1)
    high_near = from_behind(own_high[split:], "tm", 1)
    fr = list(range(frames))
    kv_list = [
        (low_far, [0 * frames + f for f in fr[:split]]),
        (low_near, [0 * frames + f for f in fr[split:]]),
        (prior_mid, [1 * frames + f for f in fr]),
        (high_far, [2 * frames + f for f in fr[:split]]),
        (high_near, [2 * frames + f for f in fr[split:]]),
        (own_low, [3 * frames + f for f in fr]),
        (kv, [4 * frames + f for f in fr]),
        (own_high, [5 * frames + f for f in fr]),
    ]
    pattern = jnp.transpose(tile_pattern[0].reshape(frames, 2, frames, 3), (0, 1, 3, 2))
    span_index = lax.axis_index("tm")
    strip_index = lax.axis_index("space")
    source_valid = jnp.stack([span_index > 0, jnp.array(True)])
    offset_valid = jnp.stack(
        [strip_index > 0, jnp.array(True), strip_index < lax.axis_size("space") - 1]
    )
    visible = (pattern > 0) & source_valid[None, :, None, None] & offset_valid[None, None, :, None]
    visible = visible.reshape(frames, 6 * frames).astype(jnp.int32)
    near = [kv_list[i] for i in (2, 5, 6, 7)]
    far = [kv_list[i] for i in (0, 1, 3, 4)]
    carry = attention(visible, queries, near, frames, tile_size, last=False)
    attended = attention(visible, queries, far, frames, tile_size, carry)
    column_start = lax.axis_index("heads") * local_width
    projected = output_columns(attended, output_weight, local_width)
    gate_half = lax.dynamic_slice_in_dim(mod_table[2], column_start, local_width)
    own_rows = rows.astype(jnp.float32)
    updated = (own_rows + gate_half * projected).astype(jnp.bfloat16)
    return updated.reshape(latent.shape)


def solution(mesh):
    placed = (
        P(("groups", "tm"), "space", None, "heads"),
        P(None, "heads"),
        P(None, "heads"),
        P(None, "heads"),
        P("heads", None),
        P("heads"),
        P("heads"),
        P(),
        P(("groups", "tm")),
        P("space", None, None, None),
    )
    return jax.shard_map(
        shards,
        mesh=mesh,
        in_specs=placed,
        out_specs=P(("groups", "tm"), "space", None, "heads"),
        check_vma=False,
    )
```

```python
import functools
import math

import jax
import jax.numpy as jnp
from jax import lax
from jax.experimental import pallas as pl
from jax.experimental.pallas import tpu as pltpu
from jax.sharding import PartitionSpec as P

HD = 128


EPSILON = 1e-06


def from_behind(value, axis, steps):
    count = lax.axis_size(axis)
    first, last = (max(0, -steps), min(count, count - steps))
    return lax.ppermute(value, axis, [(source, source + steps) for source in range(first, last)])


def gather_heads(half):
    if lax.axis_size("heads") != 2:
        return lax.all_gather(half, "heads", axis=half.ndim - 1, tiled=True)
    me = lax.axis_index("heads")
    other = lax.ppermute(half, "heads", [(0, 1), (1, 0)])
    first = jnp.where(me == 0, half, other)
    second = jnp.where(me == 0, other, half)
    return jnp.concatenate([first, second], axis=-1)


def sum_heads(partial, local_width):
    if lax.axis_size("heads") != 2:
        return lax.psum_scatter(partial, "heads", scatter_dimension=1, tiled=True)
    me = lax.axis_index("heads")
    mine = lax.dynamic_slice_in_dim(partial, me * local_width, local_width, 1)
    theirs = lax.dynamic_slice_in_dim(partial, (1 - me) * local_width, local_width, 1)
    return mine + lax.ppermute(theirs, "heads", [(0, 1), (1, 0)])


def sum_pair(value):
    if lax.axis_size("heads") != 2:
        return lax.psum(value, "heads")
    return value + lax.ppermute(value, "heads", [(0, 1), (1, 0)])


def output_columns(attended, output_weight, local_width):
    if lax.axis_size("heads") != 2:
        partial = jnp.dot(attended, output_weight, preferred_element_type=jnp.float32)
        return sum_heads(partial, local_width)
    me = lax.axis_index("heads")
    swap = [(0, 1), (1, 0)]
    mine = lax.dynamic_slice_in_dim(output_weight, me * local_width, local_width, 1)
    theirs = lax.dynamic_slice_in_dim(output_weight, (1 - me) * local_width, local_width, 1)
    received = lax.ppermute(theirs, "heads", swap)
    other = lax.ppermute(attended, "heads", swap)
    return jnp.dot(attended, mine, preferred_element_type=jnp.float32) + jnp.dot(
        other, received, preferred_element_type=jnp.float32
    )


GROUP = 3


def attention_kernel(score_scale, n_tiles, has_in, has_out, order_ref, count_ref, q_ref, *refs):
    kv_ref = refs[0]
    carry_in = refs[1:4] if has_in else ()
    outs = refs[1 + len(carry_in) : -4]
    s_scr, m_scr, l_scr, acc_scr = refs[-4:]
    frame = pl.program_id(1)
    count = count_ref[frame]
    q = q_ref[...]
    groups = [list(range(i, min(i + GROUP, n_tiles))) for i in range(0, n_tiles, GROUP)]
    m_scr[...] = jnp.full(m_scr.shape, -jnp.inf, jnp.float32)
    for group in groups:

        @pl.when(count > group[0])
        def _():
            for n in group:
                s = (
                    lax.dot_general(
                        q, kv_ref[0, order_ref[frame, n]], (((1,), (1,)), ((), ())),
                        preferred_element_type=jnp.float32,
                    )
                    * score_scale
                )
                s = jnp.where(n < count, s, -jnp.inf)
                s_scr[n] = s
                m_scr[...] = jnp.maximum(m_scr[...], s)

    m = jnp.max(m_scr[...], axis=1, keepdims=True)
    if has_in:
        acc_in, m_in, l_in = carry_in
        m_prev = m_in[:, 0:1]
        m = jnp.maximum(m_prev, m)
        rescale = jnp.exp(m_prev - m)
        acc_scr[...] = acc_in[...] * rescale
    else:
        acc_scr[...] = jnp.zeros(acc_scr.shape, jnp.float32)
    l_scr[...] = jnp.zeros(l_scr.shape, jnp.float32)
    for group in groups:

        @pl.when(count > group[0])
        def _():
            for n in group:
                e = jnp.exp(s_scr[n] - m)
                l_scr[...] += e
                acc_scr[...] += jnp.dot(
                    e.astype(jnp.bfloat16), kv_ref[1, order_ref[frame, n]],
                    preferred_element_type=jnp.float32,
                )

    total = jnp.sum(l_scr[...], axis=1, keepdims=True)
    if has_in:
        total = l_in[:, 0:1] * rescale + total
    if has_out:
        acc_out, m_out, l_out = outs
        acc_out[...] = acc_scr[...]
        m_out[...] = jnp.broadcast_to(m, m_out.shape)
        l_out[...] = jnp.broadcast_to(total, l_out.shape)
    else:
        outs[0][...] = (acc_scr[...] / total).astype(outs[0].dtype)


def attention(visible, queries, kv_list, frames, tile_size, carry=None, last=True):
    local_width = queries.shape[1]
    heads = local_width // HD
    slots = [t for _, ids in kv_list for t in ids]
    n_tiles = len(slots)
    kv_all = jnp.concatenate([kv for kv, _ in kv_list], axis=1)
    seen = visible[:, jnp.array(slots, jnp.int32)]
    order = jnp.argsort(1 - seen, axis=1, stable=True).astype(jnp.int32)
    count = jnp.sum(seen, axis=1).astype(jnp.int32)
    has_in = carry is not None
    kernel = functools.partial(attention_kernel, 1.0 / math.sqrt(HD), n_tiles, has_in, not last)
    kv_spec = pl.BlockSpec((2, n_tiles, tile_size, HD), lambda h, f, o, c: (0, 0, 0, h))
    row_spec = pl.BlockSpec((tile_size, HD), lambda h, f, o, c: (f, h))
    row_f32 = jax.ShapeDtypeStruct(queries.shape, jnp.float32)
    if last:
        out_specs = row_spec
        out_shape = jax.ShapeDtypeStruct(queries.shape, jnp.bfloat16)
    else:
        out_specs = [row_spec] * 3
        out_shape = [row_f32] * 3
    carried = list(carry) if has_in else []
    grid_spec = pltpu.PrefetchScalarGridSpec(
        num_scalar_prefetch=2,
        grid=(heads, frames),
        in_specs=[row_spec, kv_spec] + [row_spec] * len(carried),
        out_specs=out_specs,
        scratch_shapes=[
            pltpu.VMEM((n_tiles, tile_size, tile_size), jnp.float32),
            pltpu.VMEM((tile_size, tile_size), jnp.float32),
            pltpu.VMEM((tile_size, tile_size), jnp.float32),
            pltpu.VMEM((tile_size, HD), jnp.float32),
        ],
    )
    tokens = queries.shape[0]
    cost = pl.CostEstimate(
        flops=4 * tokens * n_tiles * tile_size * local_width // 2,
        transcendentals=tokens * n_tiles * tile_size * heads // 2,
        bytes_accessed=(2 * n_tiles * tile_size + 4 * tokens) * local_width * 2,
    )
    return pl.pallas_call(
        kernel,
        grid_spec=grid_spec,
        out_shape=out_shape,
        cost_estimate=cost,
    )(order, count, queries, kv_all, *carried)


def shards(
    latent,
    query_weight,
    key_weight,
    value_weight,
    output_weight,
    query_gain,
    key_gain,
    modulation,
    noise_level,
    tile_pattern,
):
    frames, strip_rows, columns, local_width = latent.shape
    width = local_width * lax.axis_size("heads")
    token_count = frames * strip_rows * columns
    tile_size = strip_rows * columns
    levels = modulation.shape[0]
    rows = latent.reshape(token_count, local_width)
    whole = gather_heads(rows)
    onehot = (noise_level[0] == jnp.arange(levels, dtype=jnp.int32)).astype(jnp.float32)
    mod_table = jnp.dot(
        onehot[None, :], modulation.reshape(levels, 3 * width), precision=lax.Precision.HIGHEST
    ).reshape(3, width)
    token_rows = whole.astype(jnp.float32)
    center = token_rows - jnp.mean(token_rows, axis=1, keepdims=True)
    normed = center * lax.rsqrt(jnp.mean(center * center, axis=1, keepdims=True) + EPSILON)
    hidden = (normed * (1.0 + mod_table[1]) + mod_table[0]).astype(jnp.bfloat16)
    query_raw = jnp.dot(hidden, query_weight, preferred_element_type=jnp.float32)
    key_raw = jnp.dot(hidden, key_weight, preferred_element_type=jnp.float32)
    value_rows = jnp.dot(hidden, value_weight, preferred_element_type=jnp.float32).astype(
        jnp.bfloat16
    )
    key_squares = sum_pair(jnp.sum(key_raw * key_raw, axis=1))
    query_squares = sum_pair(jnp.sum(query_raw * query_raw, axis=1))
    queries = (query_raw * lax.rsqrt(query_squares / width + EPSILON)[:, None] * query_gain).astype(
        jnp.bfloat16
    )
    key_rows = (key_raw * lax.rsqrt(key_squares / width + EPSILON)[:, None] * key_gain).astype(
        jnp.bfloat16
    )
    kv = jnp.stack(
        [
            key_rows.reshape(frames, tile_size, local_width),
            value_rows.reshape(frames, tile_size, local_width),
        ]
    )
    own_low = from_behind(kv, "space", 1)
    own_high = from_behind(kv, "space", -1)
    prior_mid = from_behind(kv, "tm", 1)
    split = frames - frames // 3
    low_far = from_behind(prior_mid[:, :split], "space", 1)
    high_far = from_behind(prior_mid[:, :split], "space", -1)
    low_near = from_behind(own_low[:, split:], "tm", 1)
    high_near = from_behind(own_high[:, split:], "tm", 1)
    fr = list(range(frames))
    kv_list = [
        (low_far, [0 * frames + f for f in fr[:split]]),
        (low_near, [0 * frames + f for f in fr[split:]]),
        (prior_mid, [1 * frames + f for f in fr]),
        (high_far, [2 * frames + f for f in fr[:split]]),
        (high_near, [2 * frames + f for f in fr[split:]]),
        (own_low, [3 * frames + f for f in fr]),
        (kv, [4 * frames + f for f in fr]),
        (own_high, [5 * frames + f for f in fr]),
    ]
    pattern = jnp.transpose(tile_pattern[0].reshape(frames, 2, frames, 3), (0, 1, 3, 2))
    span_index = lax.axis_index("tm")
    strip_index = lax.axis_index("space")
    source_valid = jnp.stack([span_index > 0, jnp.array(True)])
    offset_valid = jnp.stack(
        [strip_index > 0, jnp.array(True), strip_index < lax.axis_size("space") - 1]
    )
    visible = (pattern > 0) & source_valid[None, :, None, None] & offset_valid[None, None, :, None]
    visible = visible.reshape(frames, 6 * frames).astype(jnp.int32)
    near = [kv_list[i] for i in (2, 5, 6, 7)]
    far = [kv_list[i] for i in (0, 1, 3, 4)]
    carry = attention(visible, queries, near, frames, tile_size, last=False)
    attended = attention(visible, queries, far, frames, tile_size, carry)
    column_start = lax.axis_index("heads") * local_width
    projected = output_columns(attended, output_weight, local_width)
    gate_half = lax.dynamic_slice_in_dim(mod_table[2], column_start, local_width)
    own_rows = rows.astype(jnp.float32)
    updated = (own_rows + gate_half * projected).astype(jnp.bfloat16)
    return updated.reshape(latent.shape)


def solution(mesh):
    placed = (
        P(("groups", "tm"), "space", None, "heads"),
        P(None, "heads"),
        P(None, "heads"),
        P(None, "heads"),
        P("heads", None),
        P("heads"),
        P("heads"),
        P(),
        P(("groups", "tm")),
        P("space", None, None, None),
    )
    return jax.shard_map(
        shards,
        mesh=mesh,
        in_specs=placed,
        out_specs=P(("groups", "tm"), "space", None, "heads"),
        check_vma=False,
    )
```

```python
import functools
import math

import jax
import jax.numpy as jnp
from jax import lax
from jax.experimental import pallas as pl
from jax.experimental.pallas import tpu as pltpu
from jax.sharding import PartitionSpec as P

HD = 128


EPSILON = 1e-06


def from_behind(value, axis, steps):
    count = lax.axis_size(axis)
    first, last = (max(0, -steps), min(count, count - steps))
    return lax.ppermute(value, axis, [(source, source + steps) for source in range(first, last)])


def gather_heads(half):
    if lax.axis_size("heads") != 2:
        return lax.all_gather(half, "heads", axis=half.ndim - 1, tiled=True)
    me = lax.axis_index("heads")
    other = lax.ppermute(half, "heads", [(0, 1), (1, 0)])
    first = jnp.where(me == 0, half, other)
    second = jnp.where(me == 0, other, half)
    return jnp.concatenate([first, second], axis=-1)


def sum_heads(partial, local_width):
    if lax.axis_size("heads") != 2:
        return lax.psum_scatter(partial, "heads", scatter_dimension=1, tiled=True)
    me = lax.axis_index("heads")
    mine = lax.dynamic_slice_in_dim(partial, me * local_width, local_width, 1)
    theirs = lax.dynamic_slice_in_dim(partial, (1 - me) * local_width, local_width, 1)
    return mine + lax.ppermute(theirs, "heads", [(0, 1), (1, 0)])


def sum_pair(value):
    if lax.axis_size("heads") != 2:
        return lax.psum(value, "heads")
    return value + lax.ppermute(value, "heads", [(0, 1), (1, 0)])


def output_columns(attended, output_weight, local_width):
    if lax.axis_size("heads") != 2:
        partial = jnp.dot(attended, output_weight, preferred_element_type=jnp.float32)
        return sum_heads(partial, local_width)
    me = lax.axis_index("heads")
    swap = [(0, 1), (1, 0)]
    mine = lax.dynamic_slice_in_dim(output_weight, me * local_width, local_width, 1)
    theirs = lax.dynamic_slice_in_dim(output_weight, (1 - me) * local_width, local_width, 1)
    received = lax.ppermute(theirs, "heads", swap)
    other = lax.ppermute(attended, "heads", swap)
    return jnp.dot(attended, mine, preferred_element_type=jnp.float32) + jnp.dot(
        other, received, preferred_element_type=jnp.float32
    )


GROUP = 3


def attention_kernel(score_scale, n_tiles, group_size, has_in, has_out, order_ref, count_ref, q_ref, *refs):
    kv_ref = refs[0]
    carry_in = refs[1:4] if has_in else ()
    outs = refs[1 + len(carry_in) : -4]
    s_scr, m_scr, l_scr, acc_scr = refs[-4:]
    frame = pl.program_id(1)
    count = count_ref[frame]
    q = q_ref[...]
    groups = [list(range(i, min(i + group_size, n_tiles))) for i in range(0, n_tiles, group_size)]
    m_scr[...] = jnp.full(m_scr.shape, -jnp.inf, jnp.float32)
    for group in groups:

        @pl.when(count > group[0])
        def _():
            for n in group:
                s = (
                    lax.dot_general(
                        q, kv_ref[0, order_ref[frame, n]], (((1,), (1,)), ((), ())),
                        preferred_element_type=jnp.float32,
                    )
                    * score_scale
                )
                s = jnp.where(n < count, s, -jnp.inf)
                s_scr[n] = s
                m_scr[...] = jnp.maximum(m_scr[...], s)

    m = jnp.max(m_scr[...], axis=1, keepdims=True)
    if has_in:
        acc_in, m_in, l_in = carry_in
        m_prev = m_in[:, 0:1]
        m = jnp.maximum(m_prev, m)
        rescale = jnp.exp(m_prev - m)
        acc_scr[...] = acc_in[...] * rescale
    else:
        acc_scr[...] = jnp.zeros(acc_scr.shape, jnp.float32)
    l_scr[...] = jnp.zeros(l_scr.shape, jnp.float32)
    for group in groups:

        @pl.when(count > group[0])
        def _():
            for n in group:
                e = jnp.exp(s_scr[n] - m)
                l_scr[...] += e
                acc_scr[...] += jnp.dot(
                    e.astype(jnp.bfloat16), kv_ref[1, order_ref[frame, n]],
                    preferred_element_type=jnp.float32,
                )

    total = jnp.sum(l_scr[...], axis=1, keepdims=True)
    if has_in:
        total = l_in[:, 0:1] * rescale + total
    if has_out:
        acc_out, m_out, l_out = outs
        acc_out[...] = acc_scr[...]
        m_out[...] = jnp.broadcast_to(m, m_out.shape)
        l_out[...] = jnp.broadcast_to(total, l_out.shape)
    else:
        outs[0][...] = (acc_scr[...] / total).astype(outs[0].dtype)


def attention(visible, queries, kv_list, frames, tile_size, carry=None, last=True):
    local_width = queries.shape[1]
    heads = local_width // HD
    slots = [t for _, ids in kv_list for t in ids]
    n_tiles = len(slots)
    kv_all = jnp.concatenate([kv for kv, _ in kv_list], axis=1)
    seen = visible[:, jnp.array(slots, jnp.int32)]
    order = jnp.argsort(1 - seen, axis=1, stable=True).astype(jnp.int32)
    count = jnp.sum(seen, axis=1).astype(jnp.int32)
    has_in = carry is not None
    group_size = 2 * GROUP if n_tiles >= 4 * GROUP else GROUP
    kernel = functools.partial(
        attention_kernel, 1.0 / math.sqrt(HD), n_tiles, group_size, has_in, not last
    )
    kv_spec = pl.BlockSpec((2, n_tiles, tile_size, HD), lambda h, f, o, c: (0, 0, 0, h))
    row_spec = pl.BlockSpec((tile_size, HD), lambda h, f, o, c: (f, h))
    row_f32 = jax.ShapeDtypeStruct(queries.shape, jnp.float32)
    if last:
        out_specs = row_spec
        out_shape = jax.ShapeDtypeStruct(queries.shape, jnp.bfloat16)
    else:
        out_specs = [row_spec] * 3
        out_shape = [row_f32] * 3
    carried = list(carry) if has_in else []
    grid_spec = pltpu.PrefetchScalarGridSpec(
        num_scalar_prefetch=2,
        grid=(heads, frames),
        in_specs=[row_spec, kv_spec] + [row_spec] * len(carried),
        out_specs=out_specs,
        scratch_shapes=[
            pltpu.VMEM((n_tiles, tile_size, tile_size), jnp.float32),
            pltpu.VMEM((tile_size, tile_size), jnp.float32),
            pltpu.VMEM((tile_size, tile_size), jnp.float32),
            pltpu.VMEM((tile_size, HD), jnp.float32),
        ],
    )
    tokens = queries.shape[0]
    cost = pl.CostEstimate(
        flops=4 * tokens * n_tiles * tile_size * local_width // 2,
        transcendentals=tokens * n_tiles * tile_size * heads // 2,
        bytes_accessed=(2 * n_tiles * tile_size + 4 * tokens) * local_width * 2,
    )
    return pl.pallas_call(
        kernel,
        grid_spec=grid_spec,
        out_shape=out_shape,
        cost_estimate=cost,
    )(order, count, queries, kv_all, *carried)


def shards(
    latent,
    query_weight,
    key_weight,
    value_weight,
    output_weight,
    query_gain,
    key_gain,
    modulation,
    noise_level,
    tile_pattern,
):
    frames, strip_rows, columns, local_width = latent.shape
    width = local_width * lax.axis_size("heads")
    token_count = frames * strip_rows * columns
    tile_size = strip_rows * columns
    levels = modulation.shape[0]
    rows = latent.reshape(token_count, local_width)
    whole = gather_heads(rows)
    onehot = (noise_level[0] == jnp.arange(levels, dtype=jnp.int32)).astype(jnp.float32)
    mod_table = jnp.dot(
        onehot[None, :], modulation.reshape(levels, 3 * width), precision=lax.Precision.HIGHEST
    ).reshape(3, width)
    token_rows = whole.astype(jnp.float32)
    center = token_rows - jnp.mean(token_rows, axis=1, keepdims=True)
    normed = center * lax.rsqrt(jnp.mean(center * center, axis=1, keepdims=True) + EPSILON)
    hidden = (normed * (1.0 + mod_table[1]) + mod_table[0]).astype(jnp.bfloat16)
    query_raw = jnp.dot(hidden, query_weight, preferred_element_type=jnp.float32)
    key_raw = jnp.dot(hidden, key_weight, preferred_element_type=jnp.float32)
    value_rows = jnp.dot(hidden, value_weight, preferred_element_type=jnp.float32).astype(
        jnp.bfloat16
    )
    key_squares = sum_pair(jnp.sum(key_raw * key_raw, axis=1))
    query_squares = sum_pair(jnp.sum(query_raw * query_raw, axis=1))
    queries = (query_raw * lax.rsqrt(query_squares / width + EPSILON)[:, None] * query_gain).astype(
        jnp.bfloat16
    )
    key_rows = (key_raw * lax.rsqrt(key_squares / width + EPSILON)[:, None] * key_gain).astype(
        jnp.bfloat16
    )
    kv = jnp.stack(
        [
            key_rows.reshape(frames, tile_size, local_width),
            value_rows.reshape(frames, tile_size, local_width),
        ]
    )
    own_low = from_behind(kv, "space", 1)
    own_high = from_behind(kv, "space", -1)
    prior_mid = from_behind(kv, "tm", 1)
    split = frames - frames // 3
    low_far = from_behind(prior_mid[:, :split], "space", 1)
    high_far = from_behind(prior_mid[:, :split], "space", -1)
    low_near = from_behind(own_low[:, split:], "tm", 1)
    high_near = from_behind(own_high[:, split:], "tm", 1)
    fr = list(range(frames))
    kv_list = [
        (low_far, [0 * frames + f for f in fr[:split]]),
        (low_near, [0 * frames + f for f in fr[split:]]),
        (prior_mid, [1 * frames + f for f in fr]),
        (high_far, [2 * frames + f for f in fr[:split]]),
        (high_near, [2 * frames + f for f in fr[split:]]),
        (own_low, [3 * frames + f for f in fr]),
        (kv, [4 * frames + f for f in fr]),
        (own_high, [5 * frames + f for f in fr]),
    ]
    pattern = jnp.transpose(tile_pattern[0].reshape(frames, 2, frames, 3), (0, 1, 3, 2))
    span_index = lax.axis_index("tm")
    strip_index = lax.axis_index("space")
    source_valid = jnp.stack([span_index > 0, jnp.array(True)])
    offset_valid = jnp.stack(
        [strip_index > 0, jnp.array(True), strip_index < lax.axis_size("space") - 1]
    )
    visible = (pattern > 0) & source_valid[None, :, None, None] & offset_valid[None, None, :, None]
    visible = visible.reshape(frames, 6 * frames).astype(jnp.int32)
    near = [kv_list[i] for i in (2, 5, 6, 7)]
    far = [kv_list[i] for i in (0, 1, 3, 4)]
    carry = attention(visible, queries, near, frames, tile_size, last=False)
    attended = attention(visible, queries, far, frames, tile_size, carry)
    column_start = lax.axis_index("heads") * local_width
    projected = output_columns(attended, output_weight, local_width)
    gate_half = lax.dynamic_slice_in_dim(mod_table[2], column_start, local_width)
    own_rows = rows.astype(jnp.float32)
    updated = (own_rows + gate_half * projected).astype(jnp.bfloat16)
    return updated.reshape(latent.shape)


def solution(mesh):
    placed = (
        P(("groups", "tm"), "space", None, "heads"),
        P(None, "heads"),
        P(None, "heads"),
        P(None, "heads"),
        P("heads", None),
        P("heads"),
        P("heads"),
        P(),
        P(("groups", "tm")),
        P("space", None, None, None),
    )
    return jax.shard_map(
        shards,
        mesh=mesh,
        in_specs=placed,
        out_specs=P(("groups", "tm"), "space", None, "heads"),
        check_vma=False,
    )
```

```python
import functools
import math

import jax
import jax.numpy as jnp
from jax import lax
from jax.experimental import pallas as pl
from jax.experimental.pallas import tpu as pltpu
from jax.sharding import PartitionSpec as P

HD = 128


EPSILON = 1e-06


def from_behind(value, axis, steps):
    count = lax.axis_size(axis)
    first, last = (max(0, -steps), min(count, count - steps))
    return lax.ppermute(value, axis, [(source, source + steps) for source in range(first, last)])


def gather_heads(half):
    if lax.axis_size("heads") != 2:
        return lax.all_gather(half, "heads", axis=half.ndim - 1, tiled=True)
    me = lax.axis_index("heads")
    other = lax.ppermute(half, "heads", [(0, 1), (1, 0)])
    first = jnp.where(me == 0, half, other)
    second = jnp.where(me == 0, other, half)
    return jnp.concatenate([first, second], axis=-1)


def sum_heads(partial, local_width):
    if lax.axis_size("heads") != 2:
        return lax.psum_scatter(partial, "heads", scatter_dimension=1, tiled=True)
    me = lax.axis_index("heads")
    mine = lax.dynamic_slice_in_dim(partial, me * local_width, local_width, 1)
    theirs = lax.dynamic_slice_in_dim(partial, (1 - me) * local_width, local_width, 1)
    return mine + lax.ppermute(theirs, "heads", [(0, 1), (1, 0)])


def sum_pair(value):
    if lax.axis_size("heads") != 2:
        return lax.psum(value, "heads")
    return value + lax.ppermute(value, "heads", [(0, 1), (1, 0)])


def output_columns(attended, output_weight, local_width):
    if lax.axis_size("heads") != 2:
        partial = jnp.dot(attended, output_weight, preferred_element_type=jnp.float32)
        return sum_heads(partial, local_width)
    me = lax.axis_index("heads")
    swap = [(0, 1), (1, 0)]
    mine = lax.dynamic_slice_in_dim(output_weight, me * local_width, local_width, 1)
    theirs = lax.dynamic_slice_in_dim(output_weight, (1 - me) * local_width, local_width, 1)
    received = lax.ppermute(theirs, "heads", swap)
    other = lax.ppermute(attended, "heads", swap)
    return jnp.dot(attended, mine, preferred_element_type=jnp.float32) + jnp.dot(
        other, received, preferred_element_type=jnp.float32
    )


GROUP = 3


def attention_kernel(
    score_scale, n_tiles, group_size, sources, has_in, has_out, order_ref, count_ref, q_ref, *refs
):
    n_kv = len(sources) if sources else 1
    kv_refs = refs[:n_kv]
    carry_in = refs[n_kv : n_kv + 3] if has_in else ()
    outs = refs[n_kv + len(carry_in) : -4]
    s_scr, m_scr, l_scr, acc_scr = refs[-4:]
    frame = pl.program_id(1)
    q = q_ref[...]
    if sources:
        groups, n = [], 0
        for src, slots in enumerate(sources):
            groups.append((count_ref[frame, src] > 0, []))
            for g, slot in enumerate(slots):
                groups[-1][1].append((n, kv_refs[src].at[:, g], order_ref[frame, slot] > 0))
                n += 1
    else:
        count = count_ref[frame]
        groups = [
            (
                count > i,
                [
                    (n, kv_refs[0].at[:, order_ref[frame, n]], n < count)
                    for n in range(i, min(i + group_size, n_tiles))
                ],
            )
            for i in range(0, n_tiles, group_size)
        ]
    m_scr[...] = jnp.full(m_scr.shape, -jnp.inf, jnp.float32)
    for cond, group in groups:

        @pl.when(cond)
        def _():
            for n, tile, valid in group:
                s = (
                    lax.dot_general(
                        q, tile[0], (((1,), (1,)), ((), ())),
                        preferred_element_type=jnp.float32,
                    )
                    * score_scale
                )
                s = jnp.where(valid, s, -jnp.inf)
                s_scr[n] = s
                m_scr[...] = jnp.maximum(m_scr[...], s)

    m = jnp.max(m_scr[...], axis=1, keepdims=True)
    if has_in:
        acc_in, m_in, l_in = carry_in
        m_prev = m_in[:, 0:1]
        m = jnp.maximum(m_prev, m)
        rescale = jnp.exp(m_prev - m)
        acc_scr[...] = acc_in[...] * rescale
    else:
        acc_scr[...] = jnp.zeros(acc_scr.shape, jnp.float32)
    l_scr[...] = jnp.zeros(l_scr.shape, jnp.float32)
    for cond, group in groups:

        @pl.when(cond)
        def _():
            for n, tile, valid in group:
                e = jnp.exp(s_scr[n] - m)
                l_scr[...] += e
                acc_scr[...] += jnp.dot(
                    e.astype(jnp.bfloat16), tile[1], preferred_element_type=jnp.float32
                )

    total = jnp.sum(l_scr[...], axis=1, keepdims=True)
    if has_in:
        total = l_in[:, 0:1] * rescale + total
    if has_out:
        acc_out, m_out, l_out = outs
        acc_out[...] = acc_scr[...]
        m_out[...] = jnp.broadcast_to(m, m_out.shape)
        l_out[...] = jnp.broadcast_to(total, l_out.shape)
    else:
        outs[0][...] = (acc_scr[...] / total).astype(outs[0].dtype)


def attention(visible, queries, kv_list, frames, tile_size, carry=None, last=True):
    local_width = queries.shape[1]
    heads = local_width // HD
    slots = [t for _, ids in kv_list for t in ids]
    n_tiles = len(slots)
    has_in = carry is not None
    group_size = 2 * GROUP if n_tiles >= 4 * GROUP else GROUP
    by_source = n_tiles < 4 * GROUP
    if by_source:
        sources = tuple(tuple(ids) for _, ids in kv_list)
        kv_inputs = [kv for kv, _ in kv_list]
        order = visible
        count = jnp.stack(
            [jnp.max(visible[:, jnp.array(ids, jnp.int32)], axis=1) for ids in sources], axis=1
        ).astype(jnp.int32)
        kv_specs = [
            pl.BlockSpec((2, len(ids), tile_size, HD), lambda h, f, o, c: (0, 0, 0, h))
            for ids in sources
        ]
    else:
        sources = None
        kv_inputs = [jnp.concatenate([kv for kv, _ in kv_list], axis=1)]
        seen = visible[:, jnp.array(slots, jnp.int32)]
        order = jnp.argsort(1 - seen, axis=1, stable=True).astype(jnp.int32)
        count = jnp.sum(seen, axis=1).astype(jnp.int32)
        kv_specs = [pl.BlockSpec((2, n_tiles, tile_size, HD), lambda h, f, o, c: (0, 0, 0, h))]
    kernel = functools.partial(
        attention_kernel, 1.0 / math.sqrt(HD), n_tiles, group_size, sources, has_in, not last
    )
    row_spec = pl.BlockSpec((tile_size, HD), lambda h, f, o, c: (f, h))
    row_f32 = jax.ShapeDtypeStruct(queries.shape, jnp.float32)
    if last:
        out_specs = row_spec
        out_shape = jax.ShapeDtypeStruct(queries.shape, jnp.bfloat16)
    else:
        out_specs = [row_spec] * 3
        out_shape = [row_f32] * 3
    carried = list(carry) if has_in else []
    grid_spec = pltpu.PrefetchScalarGridSpec(
        num_scalar_prefetch=2,
        grid=(heads, frames),
        in_specs=[row_spec] + kv_specs + [row_spec] * len(carried),
        out_specs=out_specs,
        scratch_shapes=[
            pltpu.VMEM((n_tiles, tile_size, tile_size), jnp.float32),
            pltpu.VMEM((tile_size, tile_size), jnp.float32),
            pltpu.VMEM((tile_size, tile_size), jnp.float32),
            pltpu.VMEM((tile_size, HD), jnp.float32),
        ],
    )
    tokens = queries.shape[0]
    cost = pl.CostEstimate(
        flops=4 * tokens * n_tiles * tile_size * local_width // 2,
        transcendentals=tokens * n_tiles * tile_size * heads // 2,
        bytes_accessed=(2 * n_tiles * tile_size + 4 * tokens) * local_width * 2,
    )
    return pl.pallas_call(
        kernel,
        grid_spec=grid_spec,
        out_shape=out_shape,
        cost_estimate=cost,
    )(order, count, queries, *kv_inputs, *carried)


def shards(
    latent,
    query_weight,
    key_weight,
    value_weight,
    output_weight,
    query_gain,
    key_gain,
    modulation,
    noise_level,
    tile_pattern,
):
    frames, strip_rows, columns, local_width = latent.shape
    width = local_width * lax.axis_size("heads")
    token_count = frames * strip_rows * columns
    tile_size = strip_rows * columns
    levels = modulation.shape[0]
    rows = latent.reshape(token_count, local_width)
    whole = gather_heads(rows)
    onehot = (noise_level[0] == jnp.arange(levels, dtype=jnp.int32)).astype(jnp.float32)
    mod_table = jnp.dot(
        onehot[None, :], modulation.reshape(levels, 3 * width), precision=lax.Precision.HIGHEST
    ).reshape(3, width)
    token_rows = whole.astype(jnp.float32)
    center = token_rows - jnp.mean(token_rows, axis=1, keepdims=True)
    normed = center * lax.rsqrt(jnp.mean(center * center, axis=1, keepdims=True) + EPSILON)
    hidden = (normed * (1.0 + mod_table[1]) + mod_table[0]).astype(jnp.bfloat16)
    query_raw = jnp.dot(hidden, query_weight, preferred_element_type=jnp.float32)
    key_raw = jnp.dot(hidden, key_weight, preferred_element_type=jnp.float32)
    value_rows = jnp.dot(hidden, value_weight, preferred_element_type=jnp.float32).astype(
        jnp.bfloat16
    )
    key_squares = sum_pair(jnp.sum(key_raw * key_raw, axis=1))
    query_squares = sum_pair(jnp.sum(query_raw * query_raw, axis=1))
    queries = (query_raw * lax.rsqrt(query_squares / width + EPSILON)[:, None] * query_gain).astype(
        jnp.bfloat16
    )
    key_rows = (key_raw * lax.rsqrt(key_squares / width + EPSILON)[:, None] * key_gain).astype(
        jnp.bfloat16
    )
    kv = jnp.stack(
        [
            key_rows.reshape(frames, tile_size, local_width),
            value_rows.reshape(frames, tile_size, local_width),
        ]
    )
    own_low = from_behind(kv, "space", 1)
    own_high = from_behind(kv, "space", -1)
    prior_mid = from_behind(kv, "tm", 1)
    split = frames - frames // 3
    low_far = from_behind(prior_mid[:, :split], "space", 1)
    high_far = from_behind(prior_mid[:, :split], "space", -1)
    low_near = from_behind(own_low[:, split:], "tm", 1)
    high_near = from_behind(own_high[:, split:], "tm", 1)
    fr = list(range(frames))
    kv_list = [
        (low_far, [0 * frames + f for f in fr[:split]]),
        (low_near, [0 * frames + f for f in fr[split:]]),
        (prior_mid, [1 * frames + f for f in fr]),
        (high_far, [2 * frames + f for f in fr[:split]]),
        (high_near, [2 * frames + f for f in fr[split:]]),
        (own_low, [3 * frames + f for f in fr]),
        (kv, [4 * frames + f for f in fr]),
        (own_high, [5 * frames + f for f in fr]),
    ]
    pattern = jnp.transpose(tile_pattern[0].reshape(frames, 2, frames, 3), (0, 1, 3, 2))
    span_index = lax.axis_index("tm")
    strip_index = lax.axis_index("space")
    source_valid = jnp.stack([span_index > 0, jnp.array(True)])
    offset_valid = jnp.stack(
        [strip_index > 0, jnp.array(True), strip_index < lax.axis_size("space") - 1]
    )
    visible = (pattern > 0) & source_valid[None, :, None, None] & offset_valid[None, None, :, None]
    visible = visible.reshape(frames, 6 * frames).astype(jnp.int32)
    near = [kv_list[i] for i in (2, 5, 6, 7)]
    far = [kv_list[i] for i in (0, 1, 3, 4)]
    carry = attention(visible, queries, near, frames, tile_size, last=False)
    attended = attention(visible, queries, far, frames, tile_size, carry)
    column_start = lax.axis_index("heads") * local_width
    projected = output_columns(attended, output_weight, local_width)
    gate_half = lax.dynamic_slice_in_dim(mod_table[2], column_start, local_width)
    own_rows = rows.astype(jnp.float32)
    updated = (own_rows + gate_half * projected).astype(jnp.bfloat16)
    return updated.reshape(latent.shape)


def solution(mesh):
    placed = (
        P(("groups", "tm"), "space", None, "heads"),
        P(None, "heads"),
        P(None, "heads"),
        P(None, "heads"),
        P("heads", None),
        P("heads"),
        P("heads"),
        P(),
        P(("groups", "tm")),
        P("space", None, None, None),
    )
    return jax.shard_map(
        shards,
        mesh=mesh,
        in_specs=placed,
        out_specs=P(("groups", "tm"), "space", None, "heads"),
        check_vma=False,
    )
```

```python
import functools
import math

import jax
import jax.numpy as jnp
from jax import lax
from jax.experimental import pallas as pl
from jax.experimental.pallas import tpu as pltpu
from jax.sharding import PartitionSpec as P

HD = 128


EPSILON = 1e-06


def from_behind(value, axis, steps):
    count = lax.axis_size(axis)
    first, last = (max(0, -steps), min(count, count - steps))
    return lax.ppermute(value, axis, [(source, source + steps) for source in range(first, last)])


def gather_heads(half):
    if lax.axis_size("heads") != 2:
        return lax.all_gather(half, "heads", axis=half.ndim - 1, tiled=True)
    me = lax.axis_index("heads")
    other = lax.ppermute(half, "heads", [(0, 1), (1, 0)])
    first = jnp.where(me == 0, half, other)
    second = jnp.where(me == 0, other, half)
    return jnp.concatenate([first, second], axis=-1)


def sum_heads(partial, local_width):
    if lax.axis_size("heads") != 2:
        return lax.psum_scatter(partial, "heads", scatter_dimension=1, tiled=True)
    me = lax.axis_index("heads")
    mine = lax.dynamic_slice_in_dim(partial, me * local_width, local_width, 1)
    theirs = lax.dynamic_slice_in_dim(partial, (1 - me) * local_width, local_width, 1)
    return mine + lax.ppermute(theirs, "heads", [(0, 1), (1, 0)])


def sum_pair(value):
    if lax.axis_size("heads") != 2:
        return lax.psum(value, "heads")
    return value + lax.ppermute(value, "heads", [(0, 1), (1, 0)])


def output_columns(attended, output_weight, local_width):
    if lax.axis_size("heads") != 2:
        partial = jnp.dot(attended, output_weight, preferred_element_type=jnp.float32)
        return sum_heads(partial, local_width)
    me = lax.axis_index("heads")
    swap = [(0, 1), (1, 0)]
    mine = lax.dynamic_slice_in_dim(output_weight, me * local_width, local_width, 1)
    theirs = lax.dynamic_slice_in_dim(output_weight, (1 - me) * local_width, local_width, 1)
    received = lax.ppermute(theirs, "heads", swap)
    other = lax.ppermute(attended, "heads", swap)
    return jnp.dot(attended, mine, preferred_element_type=jnp.float32) + jnp.dot(
        other, received, preferred_element_type=jnp.float32
    )


GROUP = 3


def attention_kernel(score_scale, n_tiles, group_size, has_in, has_out, order_ref, count_ref, q_ref, *refs):
    kv_ref = refs[0]
    carry_in = refs[1:4] if has_in else ()
    outs = refs[1 + len(carry_in) : -4]
    s_scr, m_scr, l_scr, acc_scr = refs[-4:]
    frame = pl.program_id(1)
    count = count_ref[frame]
    q = q_ref[...]
    groups = [list(range(i, min(i + group_size, n_tiles))) for i in range(0, n_tiles, group_size)]
    m_scr[...] = jnp.full(m_scr.shape, -jnp.inf, jnp.float32)
    for group in groups:

        @pl.when(count > group[0])
        def _():
            for n in group:
                s = (
                    lax.dot_general(
                        q, kv_ref[0, order_ref[frame, n]], (((1,), (1,)), ((), ())),
                        preferred_element_type=jnp.float32,
                    )
                    * score_scale
                )
                s = jnp.where(n < count, s, -jnp.inf)
                s_scr[n] = s
                m_scr[...] = jnp.maximum(m_scr[...], s)

    m = jnp.max(m_scr[...], axis=1, keepdims=True)
    if has_in:
        acc_in, m_in, l_in = carry_in
        m_prev = m_in[:, 0:1]
        m = jnp.maximum(m_prev, m)
        rescale = jnp.exp(m_prev - m)
        acc_scr[...] = acc_in[...] * rescale
    else:
        acc_scr[...] = jnp.zeros(acc_scr.shape, jnp.float32)
    l_scr[...] = jnp.zeros(l_scr.shape, jnp.float32)
    for group in groups:

        @pl.when(count > group[0])
        def _():
            for n in group:
                e = jnp.exp(s_scr[n] - m)
                l_scr[...] += e
                acc_scr[...] += jnp.dot(
                    e.astype(jnp.bfloat16), kv_ref[1, order_ref[frame, n]],
                    preferred_element_type=jnp.float32,
                )

    total = jnp.sum(l_scr[...], axis=1, keepdims=True)
    if has_in:
        total = l_in[:, 0:1] * rescale + total
    if has_out:
        acc_out, m_out, l_out = outs
        acc_out[...] = acc_scr[...]
        m_out[...] = jnp.broadcast_to(m, m_out.shape)
        l_out[...] = jnp.broadcast_to(total, l_out.shape)
    else:
        outs[0][...] = (acc_scr[...] / total).astype(outs[0].dtype)


def attention(visible, queries, kv_list, frames, tile_size, carry=None, last=True):
    local_width = queries.shape[1]
    heads = local_width // HD
    slots = [t for _, ids in kv_list for t in ids]
    n_tiles = len(slots)
    kv_all = jnp.concatenate([kv for kv, _ in kv_list], axis=1)
    seen = visible[:, jnp.array(slots, jnp.int32)]
    order = jnp.argsort(1 - seen, axis=1, stable=True).astype(jnp.int32)
    count = jnp.sum(seen, axis=1).astype(jnp.int32)
    has_in = carry is not None
    group_size = n_tiles if n_tiles >= 4 * GROUP else GROUP
    kernel = functools.partial(
        attention_kernel, 1.0 / math.sqrt(HD), n_tiles, group_size, has_in, not last
    )
    kv_spec = pl.BlockSpec((2, n_tiles, tile_size, HD), lambda h, f, o, c: (0, 0, 0, h))
    row_spec = pl.BlockSpec((tile_size, HD), lambda h, f, o, c: (f, h))
    row_f32 = jax.ShapeDtypeStruct(queries.shape, jnp.float32)
    if last:
        out_specs = row_spec
        out_shape = jax.ShapeDtypeStruct(queries.shape, jnp.bfloat16)
    else:
        out_specs = [row_spec] * 3
        out_shape = [row_f32] * 3
    carried = list(carry) if has_in else []
    grid_spec = pltpu.PrefetchScalarGridSpec(
        num_scalar_prefetch=2,
        grid=(heads, frames),
        in_specs=[row_spec, kv_spec] + [row_spec] * len(carried),
        out_specs=out_specs,
        scratch_shapes=[
            pltpu.VMEM((n_tiles, tile_size, tile_size), jnp.float32),
            pltpu.VMEM((tile_size, tile_size), jnp.float32),
            pltpu.VMEM((tile_size, tile_size), jnp.float32),
            pltpu.VMEM((tile_size, HD), jnp.float32),
        ],
    )
    tokens = queries.shape[0]
    cost = pl.CostEstimate(
        flops=4 * tokens * n_tiles * tile_size * local_width // 2,
        transcendentals=tokens * n_tiles * tile_size * heads // 2,
        bytes_accessed=(2 * n_tiles * tile_size + 4 * tokens) * local_width * 2,
    )
    return pl.pallas_call(
        kernel,
        grid_spec=grid_spec,
        out_shape=out_shape,
        cost_estimate=cost,
    )(order, count, queries, kv_all, *carried)


def shards(
    latent,
    query_weight,
    key_weight,
    value_weight,
    output_weight,
    query_gain,
    key_gain,
    modulation,
    noise_level,
    tile_pattern,
):
    frames, strip_rows, columns, local_width = latent.shape
    width = local_width * lax.axis_size("heads")
    token_count = frames * strip_rows * columns
    tile_size = strip_rows * columns
    levels = modulation.shape[0]
    rows = latent.reshape(token_count, local_width)
    whole = gather_heads(rows)
    onehot = (noise_level[0] == jnp.arange(levels, dtype=jnp.int32)).astype(jnp.float32)
    mod_table = jnp.dot(
        onehot[None, :], modulation.reshape(levels, 3 * width), precision=lax.Precision.HIGHEST
    ).reshape(3, width)
    token_rows = whole.astype(jnp.float32)
    center = token_rows - jnp.mean(token_rows, axis=1, keepdims=True)
    normed = center * lax.rsqrt(jnp.mean(center * center, axis=1, keepdims=True) + EPSILON)
    hidden = (normed * (1.0 + mod_table[1]) + mod_table[0]).astype(jnp.bfloat16)
    query_raw = jnp.dot(hidden, query_weight, preferred_element_type=jnp.float32)
    key_raw = jnp.dot(hidden, key_weight, preferred_element_type=jnp.float32)
    value_rows = jnp.dot(hidden, value_weight, preferred_element_type=jnp.float32).astype(
        jnp.bfloat16
    )
    key_squares = sum_pair(jnp.sum(key_raw * key_raw, axis=1))
    query_squares = sum_pair(jnp.sum(query_raw * query_raw, axis=1))
    queries = (query_raw * lax.rsqrt(query_squares / width + EPSILON)[:, None] * query_gain).astype(
        jnp.bfloat16
    )
    key_rows = (key_raw * lax.rsqrt(key_squares / width + EPSILON)[:, None] * key_gain).astype(
        jnp.bfloat16
    )
    kv = jnp.stack(
        [
            key_rows.reshape(frames, tile_size, local_width),
            value_rows.reshape(frames, tile_size, local_width),
        ]
    )
    own_low = from_behind(kv, "space", 1)
    own_high = from_behind(kv, "space", -1)
    prior_mid = from_behind(kv, "tm", 1)
    split = frames - frames // 3
    low_far = from_behind(prior_mid[:, :split], "space", 1)
    high_far = from_behind(prior_mid[:, :split], "space", -1)
    low_near = from_behind(own_low[:, split:], "tm", 1)
    high_near = from_behind(own_high[:, split:], "tm", 1)
    fr = list(range(frames))
    kv_list = [
        (low_far, [0 * frames + f for f in fr[:split]]),
        (low_near, [0 * frames + f for f in fr[split:]]),
        (prior_mid, [1 * frames + f for f in fr]),
        (high_far, [2 * frames + f for f in fr[:split]]),
        (high_near, [2 * frames + f for f in fr[split:]]),
        (own_low, [3 * frames + f for f in fr]),
        (kv, [4 * frames + f for f in fr]),
        (own_high, [5 * frames + f for f in fr]),
    ]
    pattern = jnp.transpose(tile_pattern[0].reshape(frames, 2, frames, 3), (0, 1, 3, 2))
    span_index = lax.axis_index("tm")
    strip_index = lax.axis_index("space")
    source_valid = jnp.stack([span_index > 0, jnp.array(True)])
    offset_valid = jnp.stack(
        [strip_index > 0, jnp.array(True), strip_index < lax.axis_size("space") - 1]
    )
    visible = (pattern > 0) & source_valid[None, :, None, None] & offset_valid[None, None, :, None]
    visible = visible.reshape(frames, 6 * frames).astype(jnp.int32)
    near = [kv_list[i] for i in (2, 5, 6, 7)]
    far = [kv_list[i] for i in (0, 1, 3, 4)]
    carry = attention(visible, queries, near, frames, tile_size, last=False)
    attended = attention(visible, queries, far, frames, tile_size, carry)
    column_start = lax.axis_index("heads") * local_width
    projected = output_columns(attended, output_weight, local_width)
    gate_half = lax.dynamic_slice_in_dim(mod_table[2], column_start, local_width)
    own_rows = rows.astype(jnp.float32)
    updated = (own_rows + gate_half * projected).astype(jnp.bfloat16)
    return updated.reshape(latent.shape)


def solution(mesh):
    placed = (
        P(("groups", "tm"), "space", None, "heads"),
        P(None, "heads"),
        P(None, "heads"),
        P(None, "heads"),
        P("heads", None),
        P("heads"),
        P("heads"),
        P(),
        P(("groups", "tm")),
        P("space", None, None, None),
    )
    return jax.shard_map(
        shards,
        mesh=mesh,
        in_specs=placed,
        out_specs=P(("groups", "tm"), "space", None, "heads"),
        check_vma=False,
    )
```

```python
import functools
import math

import jax
import jax.numpy as jnp
from jax import lax
from jax.experimental import pallas as pl
from jax.experimental.pallas import tpu as pltpu
from jax.sharding import PartitionSpec as P

HD = 128


EPSILON = 1e-06


def from_behind(value, axis, steps):
    count = lax.axis_size(axis)
    first, last = (max(0, -steps), min(count, count - steps))
    return lax.ppermute(value, axis, [(source, source + steps) for source in range(first, last)])


def gather_heads(half):
    if lax.axis_size("heads") != 2:
        return lax.all_gather(half, "heads", axis=half.ndim - 1, tiled=True)
    me = lax.axis_index("heads")
    other = lax.ppermute(half, "heads", [(0, 1), (1, 0)])
    first = jnp.where(me == 0, half, other)
    second = jnp.where(me == 0, other, half)
    return jnp.concatenate([first, second], axis=-1)


def sum_heads(partial, local_width):
    if lax.axis_size("heads") != 2:
        return lax.psum_scatter(partial, "heads", scatter_dimension=1, tiled=True)
    me = lax.axis_index("heads")
    mine = lax.dynamic_slice_in_dim(partial, me * local_width, local_width, 1)
    theirs = lax.dynamic_slice_in_dim(partial, (1 - me) * local_width, local_width, 1)
    return mine + lax.ppermute(theirs, "heads", [(0, 1), (1, 0)])


def sum_pair(value):
    if lax.axis_size("heads") != 2:
        return lax.psum(value, "heads")
    return value + lax.ppermute(value, "heads", [(0, 1), (1, 0)])


def output_columns(attended, output_weight, local_width):
    if lax.axis_size("heads") != 2:
        partial = jnp.dot(attended, output_weight, preferred_element_type=jnp.float32)
        return sum_heads(partial, local_width)
    me = lax.axis_index("heads")
    swap = [(0, 1), (1, 0)]
    mine = lax.dynamic_slice_in_dim(output_weight, me * local_width, local_width, 1)
    theirs = lax.dynamic_slice_in_dim(output_weight, (1 - me) * local_width, local_width, 1)
    received = lax.ppermute(theirs, "heads", swap)
    other = lax.ppermute(attended, "heads", swap)
    return jnp.dot(attended, mine, preferred_element_type=jnp.float32) + jnp.dot(
        other, received, preferred_element_type=jnp.float32
    )


GROUP = 3


def attention_kernel(score_scale, n_tiles, group_size, has_in, has_out, order_ref, count_ref, q_ref, *refs):
    kv_ref = refs[0]
    carry_in = refs[1:4] if has_in else ()
    outs = refs[1 + len(carry_in) : -4]
    s_scr, m_scr, l_scr, acc_scr = refs[-4:]
    frame = pl.program_id(1)
    count = count_ref[frame]
    q = q_ref[...]
    groups = [list(range(i, min(i + group_size, n_tiles))) for i in range(0, n_tiles, group_size)]
    m_scr[...] = jnp.full(m_scr.shape, -jnp.inf, jnp.float32)
    for group in groups:

        @pl.when(count > group[0])
        def _():
            for n in group:
                s = (
                    lax.dot_general(
                        q, kv_ref[0, order_ref[frame, n]], (((1,), (1,)), ((), ())),
                        preferred_element_type=jnp.float32,
                    )
                    * score_scale
                )
                s = jnp.where(n < count, s, -jnp.inf)
                s_scr[n] = s
                m_scr[...] = jnp.maximum(m_scr[...], s)

    m = jnp.max(m_scr[...], axis=1, keepdims=True)
    if has_in:
        acc_in, m_in, l_in = carry_in
        m_prev = m_in[:, 0:1]
        m = jnp.maximum(m_prev, m)
        rescale = jnp.exp(m_prev - m)
        acc_scr[...] = acc_in[...] * rescale
    else:
        acc_scr[...] = jnp.zeros(acc_scr.shape, jnp.float32)
    l_scr[...] = jnp.zeros(l_scr.shape, jnp.float32)
    for group in groups:

        @pl.when(count > group[0])
        def _():
            for n in group:
                e = jnp.exp(s_scr[n] - m)
                l_scr[...] += e
                acc_scr[...] += jnp.dot(
                    e.astype(jnp.bfloat16), kv_ref[1, order_ref[frame, n]],
                    preferred_element_type=jnp.float32,
                )

    total = jnp.sum(l_scr[...], axis=1, keepdims=True)
    if has_in:
        total = l_in[:, 0:1] * rescale + total
    if has_out:
        acc_out, m_out, l_out = outs
        acc_out[...] = acc_scr[...]
        m_out[...] = jnp.broadcast_to(m, m_out.shape)
        l_out[...] = jnp.broadcast_to(total, l_out.shape)
    else:
        outs[0][...] = (acc_scr[...] / total).astype(outs[0].dtype)


def attention(visible, queries, kv_list, frames, tile_size, carry=None, last=True):
    local_width = queries.shape[1]
    heads = local_width // HD
    slots = [t for _, ids in kv_list for t in ids]
    n_tiles = len(slots)
    kv_all = jnp.concatenate([kv for kv, _ in kv_list], axis=1)
    seen = visible[:, jnp.array(slots, jnp.int32)]
    order = jnp.argsort(1 - seen, axis=1, stable=True).astype(jnp.int32)
    count = jnp.sum(seen, axis=1).astype(jnp.int32)
    has_in = carry is not None
    group_size = n_tiles
    kernel = functools.partial(
        attention_kernel, 1.0 / math.sqrt(HD), n_tiles, group_size, has_in, not last
    )
    kv_spec = pl.BlockSpec((2, n_tiles, tile_size, HD), lambda h, f, o, c: (0, 0, 0, h))
    row_spec = pl.BlockSpec((tile_size, HD), lambda h, f, o, c: (f, h))
    row_f32 = jax.ShapeDtypeStruct(queries.shape, jnp.float32)
    if last:
        out_specs = row_spec
        out_shape = jax.ShapeDtypeStruct(queries.shape, jnp.bfloat16)
    else:
        out_specs = [row_spec] * 3
        out_shape = [row_f32] * 3
    carried = list(carry) if has_in else []
    grid_spec = pltpu.PrefetchScalarGridSpec(
        num_scalar_prefetch=2,
        grid=(heads, frames),
        in_specs=[row_spec, kv_spec] + [row_spec] * len(carried),
        out_specs=out_specs,
        scratch_shapes=[
            pltpu.VMEM((n_tiles, tile_size, tile_size), jnp.float32),
            pltpu.VMEM((tile_size, tile_size), jnp.float32),
            pltpu.VMEM((tile_size, tile_size), jnp.float32),
            pltpu.VMEM((tile_size, HD), jnp.float32),
        ],
    )
    tokens = queries.shape[0]
    cost = pl.CostEstimate(
        flops=4 * tokens * n_tiles * tile_size * local_width // 2,
        transcendentals=tokens * n_tiles * tile_size * heads // 2,
        bytes_accessed=(2 * n_tiles * tile_size + 4 * tokens) * local_width * 2,
    )
    return pl.pallas_call(
        kernel,
        grid_spec=grid_spec,
        out_shape=out_shape,
        cost_estimate=cost,
    )(order, count, queries, kv_all, *carried)


def shards(
    latent,
    query_weight,
    key_weight,
    value_weight,
    output_weight,
    query_gain,
    key_gain,
    modulation,
    noise_level,
    tile_pattern,
):
    frames, strip_rows, columns, local_width = latent.shape
    width = local_width * lax.axis_size("heads")
    token_count = frames * strip_rows * columns
    tile_size = strip_rows * columns
    levels = modulation.shape[0]
    rows = latent.reshape(token_count, local_width)
    whole = gather_heads(rows)
    onehot = (noise_level[0] == jnp.arange(levels, dtype=jnp.int32)).astype(jnp.float32)
    mod_table = jnp.dot(
        onehot[None, :], modulation.reshape(levels, 3 * width), precision=lax.Precision.HIGHEST
    ).reshape(3, width)
    token_rows = whole.astype(jnp.float32)
    center = token_rows - jnp.mean(token_rows, axis=1, keepdims=True)
    normed = center * lax.rsqrt(jnp.mean(center * center, axis=1, keepdims=True) + EPSILON)
    hidden = (normed * (1.0 + mod_table[1]) + mod_table[0]).astype(jnp.bfloat16)
    query_raw = jnp.dot(hidden, query_weight, preferred_element_type=jnp.float32)
    key_raw = jnp.dot(hidden, key_weight, preferred_element_type=jnp.float32)
    value_rows = jnp.dot(hidden, value_weight, preferred_element_type=jnp.float32).astype(
        jnp.bfloat16
    )
    key_squares = sum_pair(jnp.sum(key_raw * key_raw, axis=1))
    query_squares = sum_pair(jnp.sum(query_raw * query_raw, axis=1))
    queries = (query_raw * lax.rsqrt(query_squares / width + EPSILON)[:, None] * query_gain).astype(
        jnp.bfloat16
    )
    key_rows = (key_raw * lax.rsqrt(key_squares / width + EPSILON)[:, None] * key_gain).astype(
        jnp.bfloat16
    )
    kv = jnp.stack(
        [
            key_rows.reshape(frames, tile_size, local_width),
            value_rows.reshape(frames, tile_size, local_width),
        ]
    )
    own_low = from_behind(kv, "space", 1)
    own_high = from_behind(kv, "space", -1)
    prior_mid = from_behind(kv, "tm", 1)
    split = frames - frames // 3
    low_far = from_behind(prior_mid[:, :split], "space", 1)
    high_far = from_behind(prior_mid[:, :split], "space", -1)
    low_near = from_behind(own_low[:, split:], "tm", 1)
    high_near = from_behind(own_high[:, split:], "tm", 1)
    fr = list(range(frames))
    kv_list = [
        (low_far, [0 * frames + f for f in fr[:split]]),
        (low_near, [0 * frames + f for f in fr[split:]]),
        (prior_mid, [1 * frames + f for f in fr]),
        (high_far, [2 * frames + f for f in fr[:split]]),
        (high_near, [2 * frames + f for f in fr[split:]]),
        (own_low, [3 * frames + f for f in fr]),
        (kv, [4 * frames + f for f in fr]),
        (own_high, [5 * frames + f for f in fr]),
    ]
    pattern = jnp.transpose(tile_pattern[0].reshape(frames, 2, frames, 3), (0, 1, 3, 2))
    span_index = lax.axis_index("tm")
    strip_index = lax.axis_index("space")
    source_valid = jnp.stack([span_index > 0, jnp.array(True)])
    offset_valid = jnp.stack(
        [strip_index > 0, jnp.array(True), strip_index < lax.axis_size("space") - 1]
    )
    visible = (pattern > 0) & source_valid[None, :, None, None] & offset_valid[None, None, :, None]
    visible = visible.reshape(frames, 6 * frames).astype(jnp.int32)
    near = [kv_list[i] for i in (2, 5, 6, 7)]
    far = [kv_list[i] for i in (0, 1, 3, 4)]
    carry = attention(visible, queries, near, frames, tile_size, last=False)
    attended = attention(visible, queries, far, frames, tile_size, carry)
    column_start = lax.axis_index("heads") * local_width
    projected = output_columns(attended, output_weight, local_width)
    gate_half = lax.dynamic_slice_in_dim(mod_table[2], column_start, local_width)
    own_rows = rows.astype(jnp.float32)
    updated = (own_rows + gate_half * projected).astype(jnp.bfloat16)
    return updated.reshape(latent.shape)


def solution(mesh):
    placed = (
        P(("groups", "tm"), "space", None, "heads"),
        P(None, "heads"),
        P(None, "heads"),
        P(None, "heads"),
        P("heads", None),
        P("heads"),
        P("heads"),
        P(),
        P(("groups", "tm")),
        P("space", None, None, None),
    )
    return jax.shard_map(
        shards,
        mesh=mesh,
        in_specs=placed,
        out_specs=P(("groups", "tm"), "space", None, "heads"),
        check_vma=False,
    )
```

```python
import functools
import math

import jax
import jax.numpy as jnp
from jax import lax
from jax.experimental import pallas as pl
from jax.experimental.pallas import tpu as pltpu
from jax.sharding import PartitionSpec as P

HD = 128


EPSILON = 1e-06


def from_behind(value, axis, steps):
    count = lax.axis_size(axis)
    first, last = (max(0, -steps), min(count, count - steps))
    return lax.ppermute(value, axis, [(source, source + steps) for source in range(first, last)])


def gather_heads(half):
    if lax.axis_size("heads") != 2:
        return lax.all_gather(half, "heads", axis=half.ndim - 1, tiled=True)
    me = lax.axis_index("heads")
    other = lax.ppermute(half, "heads", [(0, 1), (1, 0)])
    first = jnp.where(me == 0, half, other)
    second = jnp.where(me == 0, other, half)
    return jnp.concatenate([first, second], axis=-1)


def sum_heads(partial, local_width):
    if lax.axis_size("heads") != 2:
        return lax.psum_scatter(partial, "heads", scatter_dimension=1, tiled=True)
    me = lax.axis_index("heads")
    mine = lax.dynamic_slice_in_dim(partial, me * local_width, local_width, 1)
    theirs = lax.dynamic_slice_in_dim(partial, (1 - me) * local_width, local_width, 1)
    return mine + lax.ppermute(theirs, "heads", [(0, 1), (1, 0)])


def sum_pair(value):
    if lax.axis_size("heads") != 2:
        return lax.psum(value, "heads")
    return value + lax.ppermute(value, "heads", [(0, 1), (1, 0)])


def output_columns(attended, output_weight, local_width):
    if lax.axis_size("heads") != 2:
        partial = jnp.dot(attended, output_weight, preferred_element_type=jnp.float32)
        return sum_heads(partial, local_width)
    me = lax.axis_index("heads")
    swap = [(0, 1), (1, 0)]
    mine = lax.dynamic_slice_in_dim(output_weight, me * local_width, local_width, 1)
    theirs = lax.dynamic_slice_in_dim(output_weight, (1 - me) * local_width, local_width, 1)
    received = lax.ppermute(theirs, "heads", swap)
    other = lax.ppermute(attended, "heads", swap)
    return jnp.dot(attended, mine, preferred_element_type=jnp.float32) + jnp.dot(
        other, received, preferred_element_type=jnp.float32
    )


GROUP = 3


def attention_kernel(
    score_scale, n_tiles, group_size, sources, has_in, has_out, order_ref, count_ref, q_ref, *refs
):
    n_kv = len(sources) if sources else 1
    kv_refs = refs[:n_kv]
    carry_in = refs[n_kv : n_kv + 3] if has_in else ()
    outs = refs[n_kv + len(carry_in) : -4]
    s_scr, m_scr, l_scr, acc_scr = refs[-4:]
    frame = pl.program_id(1)
    q = q_ref[...]
    if sources:
        items, n = [], 0
        for src, slots in enumerate(sources):
            for g, slot in enumerate(slots):
                items.append((n, kv_refs[src].at[:, g], order_ref[frame, slot] > 0))
                n += 1
        groups = [(None, items)]
    else:
        count = count_ref[frame]
        groups = [
            (
                count > i,
                [
                    (n, kv_refs[0].at[:, order_ref[frame, n]], n < count)
                    for n in range(i, min(i + group_size, n_tiles))
                ],
            )
            for i in range(0, n_tiles, group_size)
        ]
    m_scr[...] = jnp.full(m_scr.shape, -jnp.inf, jnp.float32)
    for cond, group in groups:

        def scores(group=group):
            for n, tile, valid in group:
                s = (
                    lax.dot_general(
                        q, tile[0], (((1,), (1,)), ((), ())),
                        preferred_element_type=jnp.float32,
                    )
                    * score_scale
                )
                s = jnp.where(valid, s, -jnp.inf)
                s_scr[n] = s
                m_scr[...] = jnp.maximum(m_scr[...], s)

        if cond is None:
            scores()
        else:
            pl.when(cond)(scores)

    m = jnp.max(m_scr[...], axis=1, keepdims=True)
    if has_in:
        acc_in, m_in, l_in = carry_in
        m_prev = m_in[:, 0:1]
        m = jnp.maximum(m_prev, m)
        rescale = jnp.exp(m_prev - m)
        acc_scr[...] = acc_in[...] * rescale
    else:
        acc_scr[...] = jnp.zeros(acc_scr.shape, jnp.float32)
    l_scr[...] = jnp.zeros(l_scr.shape, jnp.float32)
    for cond, group in groups:

        def weights(group=group):
            for n, tile, valid in group:
                e = jnp.exp(s_scr[n] - m)
                l_scr[...] += e
                acc_scr[...] += jnp.dot(
                    e.astype(jnp.bfloat16), tile[1], preferred_element_type=jnp.float32
                )

        if cond is None:
            weights()
        else:
            pl.when(cond)(weights)

    total = jnp.sum(l_scr[...], axis=1, keepdims=True)
    if has_in:
        total = l_in[:, 0:1] * rescale + total
    if has_out:
        acc_out, m_out, l_out = outs
        acc_out[...] = acc_scr[...]
        m_out[...] = jnp.broadcast_to(m, m_out.shape)
        l_out[...] = jnp.broadcast_to(total, l_out.shape)
    else:
        outs[0][...] = (acc_scr[...] / total).astype(outs[0].dtype)


def attention(visible, queries, kv_list, frames, tile_size, carry=None, last=True):
    local_width = queries.shape[1]
    heads = local_width // HD
    slots = [t for _, ids in kv_list for t in ids]
    n_tiles = len(slots)
    has_in = carry is not None
    group_size = 2 * GROUP if n_tiles >= 4 * GROUP else GROUP
    by_source = True
    if by_source:
        sources = tuple(tuple(ids) for _, ids in kv_list)
        kv_inputs = [kv for kv, _ in kv_list]
        order = visible
        count = jnp.stack(
            [jnp.max(visible[:, jnp.array(ids, jnp.int32)], axis=1) for ids in sources], axis=1
        ).astype(jnp.int32)
        kv_specs = [
            pl.BlockSpec((2, len(ids), tile_size, HD), lambda h, f, o, c: (0, 0, 0, h))
            for ids in sources
        ]
    else:
        sources = None
        kv_inputs = [jnp.concatenate([kv for kv, _ in kv_list], axis=1)]
        seen = visible[:, jnp.array(slots, jnp.int32)]
        order = jnp.argsort(1 - seen, axis=1, stable=True).astype(jnp.int32)
        count = jnp.sum(seen, axis=1).astype(jnp.int32)
        kv_specs = [pl.BlockSpec((2, n_tiles, tile_size, HD), lambda h, f, o, c: (0, 0, 0, h))]
    kernel = functools.partial(
        attention_kernel, 1.0 / math.sqrt(HD), n_tiles, group_size, sources, has_in, not last
    )
    row_spec = pl.BlockSpec((tile_size, HD), lambda h, f, o, c: (f, h))
    row_f32 = jax.ShapeDtypeStruct(queries.shape, jnp.float32)
    if last:
        out_specs = row_spec
        out_shape = jax.ShapeDtypeStruct(queries.shape, jnp.bfloat16)
    else:
        out_specs = [row_spec] * 3
        out_shape = [row_f32] * 3
    carried = list(carry) if has_in else []
    grid_spec = pltpu.PrefetchScalarGridSpec(
        num_scalar_prefetch=2,
        grid=(heads, frames),
        in_specs=[row_spec] + kv_specs + [row_spec] * len(carried),
        out_specs=out_specs,
        scratch_shapes=[
            pltpu.VMEM((n_tiles, tile_size, tile_size), jnp.float32),
            pltpu.VMEM((tile_size, tile_size), jnp.float32),
            pltpu.VMEM((tile_size, tile_size), jnp.float32),
            pltpu.VMEM((tile_size, HD), jnp.float32),
        ],
    )
    tokens = queries.shape[0]
    cost = pl.CostEstimate(
        flops=4 * tokens * n_tiles * tile_size * local_width // 2,
        transcendentals=tokens * n_tiles * tile_size * heads // 2,
        bytes_accessed=(2 * n_tiles * tile_size + 4 * tokens) * local_width * 2,
    )
    return pl.pallas_call(
        kernel,
        grid_spec=grid_spec,
        out_shape=out_shape,
        cost_estimate=cost,
    )(order, count, queries, *kv_inputs, *carried)


def shards(
    latent,
    query_weight,
    key_weight,
    value_weight,
    output_weight,
    query_gain,
    key_gain,
    modulation,
    noise_level,
    tile_pattern,
):
    frames, strip_rows, columns, local_width = latent.shape
    width = local_width * lax.axis_size("heads")
    token_count = frames * strip_rows * columns
    tile_size = strip_rows * columns
    levels = modulation.shape[0]
    rows = latent.reshape(token_count, local_width)
    whole = gather_heads(rows)
    onehot = (noise_level[0] == jnp.arange(levels, dtype=jnp.int32)).astype(jnp.float32)
    mod_table = jnp.dot(
        onehot[None, :], modulation.reshape(levels, 3 * width), precision=lax.Precision.HIGHEST
    ).reshape(3, width)
    token_rows = whole.astype(jnp.float32)
    center = token_rows - jnp.mean(token_rows, axis=1, keepdims=True)
    normed = center * lax.rsqrt(jnp.mean(center * center, axis=1, keepdims=True) + EPSILON)
    hidden = (normed * (1.0 + mod_table[1]) + mod_table[0]).astype(jnp.bfloat16)
    query_raw = jnp.dot(hidden, query_weight, preferred_element_type=jnp.float32)
    key_raw = jnp.dot(hidden, key_weight, preferred_element_type=jnp.float32)
    value_rows = jnp.dot(hidden, value_weight, preferred_element_type=jnp.float32).astype(
        jnp.bfloat16
    )
    key_squares = sum_pair(jnp.sum(key_raw * key_raw, axis=1))
    query_squares = sum_pair(jnp.sum(query_raw * query_raw, axis=1))
    queries = (query_raw * lax.rsqrt(query_squares / width + EPSILON)[:, None] * query_gain).astype(
        jnp.bfloat16
    )
    key_rows = (key_raw * lax.rsqrt(key_squares / width + EPSILON)[:, None] * key_gain).astype(
        jnp.bfloat16
    )
    kv = jnp.stack(
        [
            key_rows.reshape(frames, tile_size, local_width),
            value_rows.reshape(frames, tile_size, local_width),
        ]
    )
    own_low = from_behind(kv, "space", 1)
    own_high = from_behind(kv, "space", -1)
    prior_mid = from_behind(kv, "tm", 1)
    split = frames - frames // 3
    low_far = from_behind(prior_mid[:, :split], "space", 1)
    high_far = from_behind(prior_mid[:, :split], "space", -1)
    low_near = from_behind(own_low[:, split:], "tm", 1)
    high_near = from_behind(own_high[:, split:], "tm", 1)
    fr = list(range(frames))
    kv_list = [
        (low_far, [0 * frames + f for f in fr[:split]]),
        (low_near, [0 * frames + f for f in fr[split:]]),
        (prior_mid, [1 * frames + f for f in fr]),
        (high_far, [2 * frames + f for f in fr[:split]]),
        (high_near, [2 * frames + f for f in fr[split:]]),
        (own_low, [3 * frames + f for f in fr]),
        (kv, [4 * frames + f for f in fr]),
        (own_high, [5 * frames + f for f in fr]),
    ]
    pattern = jnp.transpose(tile_pattern[0].reshape(frames, 2, frames, 3), (0, 1, 3, 2))
    span_index = lax.axis_index("tm")
    strip_index = lax.axis_index("space")
    source_valid = jnp.stack([span_index > 0, jnp.array(True)])
    offset_valid = jnp.stack(
        [strip_index > 0, jnp.array(True), strip_index < lax.axis_size("space") - 1]
    )
    visible = (pattern > 0) & source_valid[None, :, None, None] & offset_valid[None, None, :, None]
    visible = visible.reshape(frames, 6 * frames).astype(jnp.int32)
    near = [kv_list[i] for i in (2, 5, 6, 7)]
    far = [kv_list[i] for i in (0, 1, 3, 4)]
    carry = attention(visible, queries, near, frames, tile_size, last=False)
    attended = attention(visible, queries, far, frames, tile_size, carry)
    column_start = lax.axis_index("heads") * local_width
    projected = output_columns(attended, output_weight, local_width)
    gate_half = lax.dynamic_slice_in_dim(mod_table[2], column_start, local_width)
    own_rows = rows.astype(jnp.float32)
    updated = (own_rows + gate_half * projected).astype(jnp.bfloat16)
    return updated.reshape(latent.shape)


def solution(mesh):
    placed = (
        P(("groups", "tm"), "space", None, "heads"),
        P(None, "heads"),
        P(None, "heads"),
        P(None, "heads"),
        P("heads", None),
        P("heads"),
        P("heads"),
        P(),
        P(("groups", "tm")),
        P("space", None, None, None),
    )
    return jax.shard_map(
        shards,
        mesh=mesh,
        in_specs=placed,
        out_specs=P(("groups", "tm"), "space", None, "heads"),
        check_vma=False,
    )
```

```python
import functools
import math

import jax
import jax.numpy as jnp
from jax import lax
from jax.experimental import pallas as pl
from jax.experimental.pallas import tpu as pltpu
from jax.sharding import PartitionSpec as P

HD = 128


EPSILON = 1e-06


def from_behind(value, axis, steps):
    count = lax.axis_size(axis)
    first, last = (max(0, -steps), min(count, count - steps))
    return lax.ppermute(value, axis, [(source, source + steps) for source in range(first, last)])


def gather_heads(half):
    if lax.axis_size("heads") != 2:
        return lax.all_gather(half, "heads", axis=half.ndim - 1, tiled=True)
    me = lax.axis_index("heads")
    other = lax.ppermute(half, "heads", [(0, 1), (1, 0)])
    first = jnp.where(me == 0, half, other)
    second = jnp.where(me == 0, other, half)
    return jnp.concatenate([first, second], axis=-1)


def sum_heads(partial, local_width):
    if lax.axis_size("heads") != 2:
        return lax.psum_scatter(partial, "heads", scatter_dimension=1, tiled=True)
    me = lax.axis_index("heads")
    mine = lax.dynamic_slice_in_dim(partial, me * local_width, local_width, 1)
    theirs = lax.dynamic_slice_in_dim(partial, (1 - me) * local_width, local_width, 1)
    return mine + lax.ppermute(theirs, "heads", [(0, 1), (1, 0)])


def sum_pair(value):
    if lax.axis_size("heads") != 2:
        return lax.psum(value, "heads")
    return value + lax.ppermute(value, "heads", [(0, 1), (1, 0)])


def output_columns(attended, output_weight, local_width):
    if lax.axis_size("heads") != 2:
        partial = jnp.dot(attended, output_weight, preferred_element_type=jnp.float32)
        return sum_heads(partial, local_width)
    me = lax.axis_index("heads")
    swap = [(0, 1), (1, 0)]
    mine = lax.dynamic_slice_in_dim(output_weight, me * local_width, local_width, 1)
    theirs = lax.dynamic_slice_in_dim(output_weight, (1 - me) * local_width, local_width, 1)
    received = lax.ppermute(theirs, "heads", swap)
    other = lax.ppermute(attended, "heads", swap)
    return jnp.dot(attended, mine, preferred_element_type=jnp.float32) + jnp.dot(
        other, received, preferred_element_type=jnp.float32
    )


GROUP = 3


def attention_kernel(score_scale, n_tiles, group_size, has_in, has_out, order_ref, count_ref, q_ref, *refs):
    kv_ref = refs[0]
    carry_in = refs[1:4] if has_in else ()
    outs = refs[1 + len(carry_in) : -4]
    s_scr, m_scr, l_scr, acc_scr = refs[-4:]
    frame = pl.program_id(1)
    count = count_ref[frame]
    q = q_ref[...]
    groups = [list(range(i, min(i + group_size, n_tiles))) for i in range(0, n_tiles, group_size)]
    m_scr[...] = jnp.full(m_scr.shape, -jnp.inf, jnp.float32)
    for group in groups:

        @pl.when(count > group[0])
        def _():
            for n in group:
                s = (
                    lax.dot_general(
                        q, kv_ref[0, n], (((1,), (1,)), ((), ())),
                        preferred_element_type=jnp.float32,
                    )
                    * score_scale
                )
                s = jnp.where(order_ref[frame, n] > 0, s, -jnp.inf)
                s_scr[n] = s
                m_scr[...] = jnp.maximum(m_scr[...], s)

    m = jnp.max(m_scr[...], axis=1, keepdims=True)
    if has_in:
        acc_in, m_in, l_in = carry_in
        m_prev = m_in[:, 0:1]
        m = jnp.maximum(m_prev, m)
        rescale = jnp.exp(m_prev - m)
        acc_scr[...] = acc_in[...] * rescale
    else:
        acc_scr[...] = jnp.zeros(acc_scr.shape, jnp.float32)
    l_scr[...] = jnp.zeros(l_scr.shape, jnp.float32)
    for group in groups:

        @pl.when(count > group[0])
        def _():
            for n in group:
                e = jnp.exp(s_scr[n] - m)
                l_scr[...] += e
                acc_scr[...] += jnp.dot(
                    e.astype(jnp.bfloat16), kv_ref[1, n],
                    preferred_element_type=jnp.float32,
                )

    total = jnp.sum(l_scr[...], axis=1, keepdims=True)
    if has_in:
        total = l_in[:, 0:1] * rescale + total
    if has_out:
        acc_out, m_out, l_out = outs
        acc_out[...] = acc_scr[...]
        m_out[...] = jnp.broadcast_to(m, m_out.shape)
        l_out[...] = jnp.broadcast_to(total, l_out.shape)
    else:
        outs[0][...] = (acc_scr[...] / total).astype(outs[0].dtype)


def attention(visible, queries, kv_list, frames, tile_size, carry=None, last=True):
    local_width = queries.shape[1]
    heads = local_width // HD
    slots = [t for _, ids in kv_list for t in ids]
    n_tiles = len(slots)
    kv_all = jnp.concatenate([kv for kv, _ in kv_list], axis=1)
    seen = visible[:, jnp.array(slots, jnp.int32)]
    order = seen.astype(jnp.int32)
    count = jnp.sum(seen, axis=1).astype(jnp.int32)
    has_in = carry is not None
    group_size = n_tiles
    kernel = functools.partial(
        attention_kernel, 1.0 / math.sqrt(HD), n_tiles, group_size, has_in, not last
    )
    kv_spec = pl.BlockSpec((2, n_tiles, tile_size, HD), lambda h, f, o, c: (0, 0, 0, h))
    row_spec = pl.BlockSpec((tile_size, HD), lambda h, f, o, c: (f, h))
    row_f32 = jax.ShapeDtypeStruct(queries.shape, jnp.float32)
    if last:
        out_specs = row_spec
        out_shape = jax.ShapeDtypeStruct(queries.shape, jnp.bfloat16)
    else:
        out_specs = [row_spec] * 3
        out_shape = [row_f32] * 3
    carried = list(carry) if has_in else []
    grid_spec = pltpu.PrefetchScalarGridSpec(
        num_scalar_prefetch=2,
        grid=(heads, frames),
        in_specs=[row_spec, kv_spec] + [row_spec] * len(carried),
        out_specs=out_specs,
        scratch_shapes=[
            pltpu.VMEM((n_tiles, tile_size, tile_size), jnp.float32),
            pltpu.VMEM((tile_size, tile_size), jnp.float32),
            pltpu.VMEM((tile_size, tile_size), jnp.float32),
            pltpu.VMEM((tile_size, HD), jnp.float32),
        ],
    )
    tokens = queries.shape[0]
    cost = pl.CostEstimate(
        flops=4 * tokens * n_tiles * tile_size * local_width // 2,
        transcendentals=tokens * n_tiles * tile_size * heads // 2,
        bytes_accessed=(2 * n_tiles * tile_size + 4 * tokens) * local_width * 2,
    )
    return pl.pallas_call(
        kernel,
        grid_spec=grid_spec,
        out_shape=out_shape,
        cost_estimate=cost,
    )(order, count, queries, kv_all, *carried)


def shards(
    latent,
    query_weight,
    key_weight,
    value_weight,
    output_weight,
    query_gain,
    key_gain,
    modulation,
    noise_level,
    tile_pattern,
):
    frames, strip_rows, columns, local_width = latent.shape
    width = local_width * lax.axis_size("heads")
    token_count = frames * strip_rows * columns
    tile_size = strip_rows * columns
    levels = modulation.shape[0]
    rows = latent.reshape(token_count, local_width)
    whole = gather_heads(rows)
    onehot = (noise_level[0] == jnp.arange(levels, dtype=jnp.int32)).astype(jnp.float32)
    mod_table = jnp.dot(
        onehot[None, :], modulation.reshape(levels, 3 * width), precision=lax.Precision.HIGHEST
    ).reshape(3, width)
    token_rows = whole.astype(jnp.float32)
    center = token_rows - jnp.mean(token_rows, axis=1, keepdims=True)
    normed = center * lax.rsqrt(jnp.mean(center * center, axis=1, keepdims=True) + EPSILON)
    hidden = (normed * (1.0 + mod_table[1]) + mod_table[0]).astype(jnp.bfloat16)
    query_raw = jnp.dot(hidden, query_weight, preferred_element_type=jnp.float32)
    key_raw = jnp.dot(hidden, key_weight, preferred_element_type=jnp.float32)
    value_rows = jnp.dot(hidden, value_weight, preferred_element_type=jnp.float32).astype(
        jnp.bfloat16
    )
    key_squares = sum_pair(jnp.sum(key_raw * key_raw, axis=1))
    query_squares = sum_pair(jnp.sum(query_raw * query_raw, axis=1))
    queries = (query_raw * lax.rsqrt(query_squares / width + EPSILON)[:, None] * query_gain).astype(
        jnp.bfloat16
    )
    key_rows = (key_raw * lax.rsqrt(key_squares / width + EPSILON)[:, None] * key_gain).astype(
        jnp.bfloat16
    )
    kv = jnp.stack(
        [
            key_rows.reshape(frames, tile_size, local_width),
            value_rows.reshape(frames, tile_size, local_width),
        ]
    )
    own_low = from_behind(kv, "space", 1)
    own_high = from_behind(kv, "space", -1)
    prior_mid = from_behind(kv, "tm", 1)
    split = frames - frames // 3
    low_far = from_behind(prior_mid[:, :split], "space", 1)
    high_far = from_behind(prior_mid[:, :split], "space", -1)
    low_near = from_behind(own_low[:, split:], "tm", 1)
    high_near = from_behind(own_high[:, split:], "tm", 1)
    fr = list(range(frames))
    kv_list = [
        (low_far, [0 * frames + f for f in fr[:split]]),
        (low_near, [0 * frames + f for f in fr[split:]]),
        (prior_mid, [1 * frames + f for f in fr]),
        (high_far, [2 * frames + f for f in fr[:split]]),
        (high_near, [2 * frames + f for f in fr[split:]]),
        (own_low, [3 * frames + f for f in fr]),
        (kv, [4 * frames + f for f in fr]),
        (own_high, [5 * frames + f for f in fr]),
    ]
    pattern = jnp.transpose(tile_pattern[0].reshape(frames, 2, frames, 3), (0, 1, 3, 2))
    span_index = lax.axis_index("tm")
    strip_index = lax.axis_index("space")
    source_valid = jnp.stack([span_index > 0, jnp.array(True)])
    offset_valid = jnp.stack(
        [strip_index > 0, jnp.array(True), strip_index < lax.axis_size("space") - 1]
    )
    visible = (pattern > 0) & source_valid[None, :, None, None] & offset_valid[None, None, :, None]
    visible = visible.reshape(frames, 6 * frames).astype(jnp.int32)
    near = [kv_list[i] for i in (2, 5, 6, 7)]
    far = [kv_list[i] for i in (0, 1, 3, 4)]
    carry = attention(visible, queries, near, frames, tile_size, last=False)
    attended = attention(visible, queries, far, frames, tile_size, carry)
    column_start = lax.axis_index("heads") * local_width
    projected = output_columns(attended, output_weight, local_width)
    gate_half = lax.dynamic_slice_in_dim(mod_table[2], column_start, local_width)
    own_rows = rows.astype(jnp.float32)
    updated = (own_rows + gate_half * projected).astype(jnp.bfloat16)
    return updated.reshape(latent.shape)


def solution(mesh):
    placed = (
        P(("groups", "tm"), "space", None, "heads"),
        P(None, "heads"),
        P(None, "heads"),
        P(None, "heads"),
        P("heads", None),
        P("heads"),
        P("heads"),
        P(),
        P(("groups", "tm")),
        P("space", None, None, None),
    )
    return jax.shard_map(
        shards,
        mesh=mesh,
        in_specs=placed,
        out_specs=P(("groups", "tm"), "space", None, "heads"),
        check_vma=False,
    )
```

```python
import functools
import math

import jax
import jax.numpy as jnp
from jax import lax
from jax.experimental import pallas as pl
from jax.experimental.pallas import tpu as pltpu
from jax.sharding import PartitionSpec as P

HD = 128


EPSILON = 1e-06


def from_behind(value, axis, steps):
    count = lax.axis_size(axis)
    first, last = (max(0, -steps), min(count, count - steps))
    return lax.ppermute(value, axis, [(source, source + steps) for source in range(first, last)])


def gather_heads(half):
    if lax.axis_size("heads") != 2:
        return lax.all_gather(half, "heads", axis=half.ndim - 1, tiled=True)
    me = lax.axis_index("heads")
    other = lax.ppermute(half, "heads", [(0, 1), (1, 0)])
    first = jnp.where(me == 0, half, other)
    second = jnp.where(me == 0, other, half)
    return jnp.concatenate([first, second], axis=-1)


def sum_heads(partial, local_width):
    if lax.axis_size("heads") != 2:
        return lax.psum_scatter(partial, "heads", scatter_dimension=1, tiled=True)
    me = lax.axis_index("heads")
    mine = lax.dynamic_slice_in_dim(partial, me * local_width, local_width, 1)
    theirs = lax.dynamic_slice_in_dim(partial, (1 - me) * local_width, local_width, 1)
    return mine + lax.ppermute(theirs, "heads", [(0, 1), (1, 0)])


def sum_pair(value):
    if lax.axis_size("heads") != 2:
        return lax.psum(value, "heads")
    return value + lax.ppermute(value, "heads", [(0, 1), (1, 0)])


def output_columns(attended, output_weight, local_width):
    if lax.axis_size("heads") != 2:
        partial = jnp.dot(attended, output_weight, preferred_element_type=jnp.float32)
        return sum_heads(partial, local_width)
    me = lax.axis_index("heads")
    swap = [(0, 1), (1, 0)]
    mine = lax.dynamic_slice_in_dim(output_weight, me * local_width, local_width, 1)
    theirs = lax.dynamic_slice_in_dim(output_weight, (1 - me) * local_width, local_width, 1)
    received = lax.ppermute(theirs, "heads", swap)
    other = lax.ppermute(attended, "heads", swap)
    return jnp.dot(attended, mine, preferred_element_type=jnp.float32) + jnp.dot(
        other, received, preferred_element_type=jnp.float32
    )


GROUP = 3


def run_now(body):
    return body()


def attention_kernel(score_scale, n_tiles, group_size, has_in, has_out, order_ref, count_ref, q_ref, *refs):
    kv_ref = refs[0]
    carry_in = refs[1:4] if has_in else ()
    outs = refs[1 + len(carry_in) : -4]
    s_scr, m_scr, l_scr, acc_scr = refs[-4:]
    frame = pl.program_id(1)
    count = count_ref[frame]
    q = q_ref[...]
    groups = [list(range(i, min(i + group_size, n_tiles))) for i in range(0, n_tiles, group_size)]
    m_scr[...] = jnp.full(m_scr.shape, -jnp.inf, jnp.float32)
    for group in groups:

        @run_now
        def _():
            for n in group:
                s = (
                    lax.dot_general(
                        q, kv_ref[0, n], (((1,), (1,)), ((), ())),
                        preferred_element_type=jnp.float32,
                    )
                    * score_scale
                )
                s = jnp.where(order_ref[frame, n] > 0, s, -jnp.inf)
                s_scr[n] = s
                m_scr[...] = jnp.maximum(m_scr[...], s)

    m = jnp.max(m_scr[...], axis=1, keepdims=True)
    if has_in:
        acc_in, m_in, l_in = carry_in
        m_prev = m_in[:, 0:1]
        m = jnp.maximum(m_prev, m)
        rescale = jnp.exp(m_prev - m)
        acc_scr[...] = acc_in[...] * rescale
    else:
        acc_scr[...] = jnp.zeros(acc_scr.shape, jnp.float32)
    l_scr[...] = jnp.zeros(l_scr.shape, jnp.float32)
    for group in groups:

        @run_now
        def _():
            for n in group:
                e = jnp.exp(s_scr[n] - m)
                l_scr[...] += e
                acc_scr[...] += jnp.dot(
                    e.astype(jnp.bfloat16), kv_ref[1, n],
                    preferred_element_type=jnp.float32,
                )

    total = jnp.sum(l_scr[...], axis=1, keepdims=True)
    if has_in:
        total = l_in[:, 0:1] * rescale + total
    if has_out:
        acc_out, m_out, l_out = outs
        acc_out[...] = acc_scr[...]
        m_out[...] = jnp.broadcast_to(m, m_out.shape)
        l_out[...] = jnp.broadcast_to(total, l_out.shape)
    else:
        outs[0][...] = (acc_scr[...] / total).astype(outs[0].dtype)


def attention(visible, queries, kv_list, frames, tile_size, carry=None, last=True):
    local_width = queries.shape[1]
    heads = local_width // HD
    slots = [t for _, ids in kv_list for t in ids]
    n_tiles = len(slots)
    kv_all = jnp.concatenate([kv for kv, _ in kv_list], axis=1)
    seen = visible[:, jnp.array(slots, jnp.int32)]
    order = seen.astype(jnp.int32)
    count = jnp.sum(seen, axis=1).astype(jnp.int32)
    has_in = carry is not None
    group_size = n_tiles
    kernel = functools.partial(
        attention_kernel, 1.0 / math.sqrt(HD), n_tiles, group_size, has_in, not last
    )
    kv_spec = pl.BlockSpec((2, n_tiles, tile_size, HD), lambda h, f, o, c: (0, 0, 0, h))
    row_spec = pl.BlockSpec((tile_size, HD), lambda h, f, o, c: (f, h))
    row_f32 = jax.ShapeDtypeStruct(queries.shape, jnp.float32)
    if last:
        out_specs = row_spec
        out_shape = jax.ShapeDtypeStruct(queries.shape, jnp.bfloat16)
    else:
        out_specs = [row_spec] * 3
        out_shape = [row_f32] * 3
    carried = list(carry) if has_in else []
    grid_spec = pltpu.PrefetchScalarGridSpec(
        num_scalar_prefetch=2,
        grid=(heads, frames),
        in_specs=[row_spec, kv_spec] + [row_spec] * len(carried),
        out_specs=out_specs,
        scratch_shapes=[
            pltpu.VMEM((n_tiles, tile_size, tile_size), jnp.float32),
            pltpu.VMEM((tile_size, tile_size), jnp.float32),
            pltpu.VMEM((tile_size, tile_size), jnp.float32),
            pltpu.VMEM((tile_size, HD), jnp.float32),
        ],
    )
    tokens = queries.shape[0]
    cost = pl.CostEstimate(
        flops=4 * tokens * n_tiles * tile_size * local_width // 2,
        transcendentals=tokens * n_tiles * tile_size * heads // 2,
        bytes_accessed=(2 * n_tiles * tile_size + 4 * tokens) * local_width * 2,
    )
    return pl.pallas_call(
        kernel,
        grid_spec=grid_spec,
        out_shape=out_shape,
        cost_estimate=cost,
    )(order, count, queries, kv_all, *carried)


def shards(
    latent,
    query_weight,
    key_weight,
    value_weight,
    output_weight,
    query_gain,
    key_gain,
    modulation,
    noise_level,
    tile_pattern,
):
    frames, strip_rows, columns, local_width = latent.shape
    width = local_width * lax.axis_size("heads")
    token_count = frames * strip_rows * columns
    tile_size = strip_rows * columns
    levels = modulation.shape[0]
    rows = latent.reshape(token_count, local_width)
    whole = gather_heads(rows)
    onehot = (noise_level[0] == jnp.arange(levels, dtype=jnp.int32)).astype(jnp.float32)
    mod_table = jnp.dot(
        onehot[None, :], modulation.reshape(levels, 3 * width), precision=lax.Precision.HIGHEST
    ).reshape(3, width)
    token_rows = whole.astype(jnp.float32)
    center = token_rows - jnp.mean(token_rows, axis=1, keepdims=True)
    normed = center * lax.rsqrt(jnp.mean(center * center, axis=1, keepdims=True) + EPSILON)
    hidden = (normed * (1.0 + mod_table[1]) + mod_table[0]).astype(jnp.bfloat16)
    query_raw = jnp.dot(hidden, query_weight, preferred_element_type=jnp.float32)
    key_raw = jnp.dot(hidden, key_weight, preferred_element_type=jnp.float32)
    value_rows = jnp.dot(hidden, value_weight, preferred_element_type=jnp.float32).astype(
        jnp.bfloat16
    )
    key_squares = sum_pair(jnp.sum(key_raw * key_raw, axis=1))
    query_squares = sum_pair(jnp.sum(query_raw * query_raw, axis=1))
    queries = (query_raw * lax.rsqrt(query_squares / width + EPSILON)[:, None] * query_gain).astype(
        jnp.bfloat16
    )
    key_rows = (key_raw * lax.rsqrt(key_squares / width + EPSILON)[:, None] * key_gain).astype(
        jnp.bfloat16
    )
    kv = jnp.stack(
        [
            key_rows.reshape(frames, tile_size, local_width),
            value_rows.reshape(frames, tile_size, local_width),
        ]
    )
    own_low = from_behind(kv, "space", 1)
    own_high = from_behind(kv, "space", -1)
    prior_mid = from_behind(kv, "tm", 1)
    split = frames - frames // 3
    low_far = from_behind(prior_mid[:, :split], "space", 1)
    high_far = from_behind(prior_mid[:, :split], "space", -1)
    low_near = from_behind(own_low[:, split:], "tm", 1)
    high_near = from_behind(own_high[:, split:], "tm", 1)
    fr = list(range(frames))
    kv_list = [
        (low_far, [0 * frames + f for f in fr[:split]]),
        (low_near, [0 * frames + f for f in fr[split:]]),
        (prior_mid, [1 * frames + f for f in fr]),
        (high_far, [2 * frames + f for f in fr[:split]]),
        (high_near, [2 * frames + f for f in fr[split:]]),
        (own_low, [3 * frames + f for f in fr]),
        (kv, [4 * frames + f for f in fr]),
        (own_high, [5 * frames + f for f in fr]),
    ]
    pattern = jnp.transpose(tile_pattern[0].reshape(frames, 2, frames, 3), (0, 1, 3, 2))
    span_index = lax.axis_index("tm")
    strip_index = lax.axis_index("space")
    source_valid = jnp.stack([span_index > 0, jnp.array(True)])
    offset_valid = jnp.stack(
        [strip_index > 0, jnp.array(True), strip_index < lax.axis_size("space") - 1]
    )
    visible = (pattern > 0) & source_valid[None, :, None, None] & offset_valid[None, None, :, None]
    visible = visible.reshape(frames, 6 * frames).astype(jnp.int32)
    near = [kv_list[i] for i in (2, 5, 6, 7)]
    far = [kv_list[i] for i in (0, 1, 3, 4)]
    carry = attention(visible, queries, near, frames, tile_size, last=False)
    attended = attention(visible, queries, far, frames, tile_size, carry)
    column_start = lax.axis_index("heads") * local_width
    projected = output_columns(attended, output_weight, local_width)
    gate_half = lax.dynamic_slice_in_dim(mod_table[2], column_start, local_width)
    own_rows = rows.astype(jnp.float32)
    updated = (own_rows + gate_half * projected).astype(jnp.bfloat16)
    return updated.reshape(latent.shape)


def solution(mesh):
    placed = (
        P(("groups", "tm"), "space", None, "heads"),
        P(None, "heads"),
        P(None, "heads"),
        P(None, "heads"),
        P("heads", None),
        P("heads"),
        P("heads"),
        P(),
        P(("groups", "tm")),
        P("space", None, None, None),
    )
    return jax.shard_map(
        shards,
        mesh=mesh,
        in_specs=placed,
        out_specs=P(("groups", "tm"), "space", None, "heads"),
        check_vma=False,
    )
```
